32 devices in a mesh: ctx: 16 (over z, x, core), tp: 2 (over y).
Axes of the slice: x: 2, y: 2, z: 4, core: 2. Of those that a mesh axis runs over, the one named last changes fastest.
Arguments:
- streams: bfloat16 [4096, 3, 4096], P(('ctx', 'tp')), may hold values from -6 to 6
- short_filter: float32 [3, 3, 4096], replicated, may hold values from -2 to 2
- skip: float32 [4096], replicated, may hold values from 0.5 to 1.5
- rates: float32 [4096, 16], replicated, may hold values from 0 to 0.05, as said below
- residues: float32 [4096, 16], replicated, may hold values from -0.5 to 0.5
Outputs:
- mixed: bfloat16 [4096, 4096], P(('ctx', 'tp'))
The draws below stay inside these ranges and needn't reach their ends.
Inputs may be any that keep to these rules, and one draw needn't show every extreme that they name: Positive decay rates.
All inputs are finite; a program needn't handle non-finite values.
Results may differ from the reference program's by a relative error of at most 0.0095.
Values may be sent and summed in bfloat16 or wider, within the bound.
No kernel may reach another device: no remote copies, remote signals or barrier semaphores. Data moves between devices by JAX's collectives and lax.ppermute only.
A program may use at most 128 MiB of HBM per device.

```python
import jax
import jax.numpy as jnp
from jax import lax

D = 4096
KW = 3
MODES = 16
L = 4096


def mode_params(key):
    first, second = jax.random.split(jax.random.fold_in(key, 7), 2)
    lowest = jnp.log(0.5 / L)
    highest = jnp.log(1.0 / 20.0)
    logs = jax.random.uniform(first, (D, MODES), jnp.float32, lowest, highest)
    decay = jnp.exp(logs)
    amplitude = jnp.clip(jax.random.normal(second, (D, MODES), jnp.float32), -4.0, 4.0)
    return (decay, amplitude * jnp.sqrt(2.0 * decay / MODES))


def draw_rates(key, part):
    return mode_params(key)[0]


def draw_residues(key, part):
    return mode_params(key)[1]


def levels(rng, dims, cuts, low, high):
    factor_of = 1.0
    for dim, shards_of in cuts:
        heights = jax.random.uniform(jax.random.fold_in(jax.random.fold_in(rng, 6), dim), (shards_of,), jnp.float32, low / len(cuts), high / len(cuts))
        factor_of = factor_of * jnp.repeat(jnp.exp(heights), dims[dim] // shards_of).reshape((-1,) + (1,) * (len(dims) - 1 - dim))
    return factor_of


def bell_draw(own_key, extent, deviation, most, shards=(), held_as=jnp.bfloat16):
    values = deviation * jax.random.normal(own_key, extent, jnp.float32)
    if shards:
        values = values * levels(own_key, extent, shards, -0.22, 0.18)
    return jnp.clip(values, -most, most).astype(held_as)


def setup_inputs(seed: int = 0) -> dict:
    arg_keys = jax.random.split(jax.random.key(seed), 6)
    streams = bell_draw(arg_keys[0], (L, 3, D), 1.0, 6.0, ((0, 32),))
    short_filter = bell_draw(arg_keys[1], (KW, 3, D), 0.5, 2.0, (), jnp.float32)
    skip = jnp.clip(jax.random.uniform(arg_keys[2], (D,), jnp.float32, 0.5, 1.5), 0.5, 1.5)
    rates = draw_rates(jax.random.fold_in(arg_keys[5], 71), 0)
    residues = draw_residues(jax.random.fold_in(arg_keys[5], 71), 0)
    return {"streams": streams, "short_filter": short_filter, "skip": skip, "rates": rates, "residues": residues}


def reference(streams, short_filter, skip, rates, residues):
    length = streams.shape[0]
    width = streams.shape[2]
    block = 128

    def one_block(index):
        start = (index * block).astype(jnp.int32)
        values = lax.dynamic_slice_in_dim(streams, start, block, 2).astype(jnp.float32)
        taps = lax.dynamic_slice_in_dim(short_filter, start, block, 2)
        padded = jnp.pad(values, ((KW - 1, 0), (0, 0), (0, 0)))
        feat = jnp.zeros((length, 3, block), jnp.float32)
        for tap in range(KW):
            feat = feat + taps[tap][None] * padded[KW - 1 - tap:KW - 1 - tap + length]
        gated = (feat[:, 1] * feat[:, 2]).astype(jnp.bfloat16)
        rate_block = lax.dynamic_slice_in_dim(rates, start, block, 0)
        residue_block = lax.dynamic_slice_in_dim(residues, start, block, 0)
        times = jnp.arange(length).astype(jnp.float32)
        kernel = jnp.sum(residue_block[None] * jnp.exp(-rate_block[None] * times[:, None, None]), axis=2)
        signal = gated.astype(jnp.float32)
        spectrum = jnp.fft.rfft(signal, n=2 * length, axis=0) * jnp.fft.rfft(kernel, n=2 * length, axis=0)
        conv = jnp.fft.irfft(spectrum, n=2 * length, axis=0)[:length]
        skip_block = lax.dynamic_slice_in_dim(skip, start, block, 0)
        result = (conv + skip_block[None] * signal).astype(jnp.bfloat16)
        return (feat[:, 0] * result.astype(jnp.float32)).astype(jnp.bfloat16)

    pieces = lax.map(one_block, jnp.arange(width // block).astype(jnp.int32))
    return jnp.transpose(pieces, (1, 0, 2)).reshape(length, width)
```

```python
import functools

import jax
import jax.numpy as jnp
from jax import lax
from jax.experimental import pallas as pl
from jax.experimental.pallas import tpu as pltpu
from jax.sharding import PartitionSpec as P

LANES = 128
GROUPS = 8


def features(x_ref, f_ref, t):
    taps = f_ref.shape[0]
    feats = []
    for s in range(x_ref.shape[0]):
        acc = f_ref[0, s] * x_ref[s, t + taps - 1]
        for tap in range(1, taps):
            acc = acc + f_ref[tap, s] * x_ref[s, t + taps - 1 - tap]
        feats.append(acc)
    return feats


def gate(feats):
    return (feats[1] * feats[2]).astype(jnp.bfloat16).astype(jnp.float32)


def state_kernel(x_ref, f_ref, d_ref, h_ref):
    modes = d_ref.shape[0]
    steps = x_ref.shape[1] - f_ref.shape[0] + 1

    def step(t, states):
        u = gate(features(x_ref, f_ref, t))
        return tuple(d_ref[m] * states[m] + u for m in range(modes))

    zero = jnp.zeros(h_ref.shape[1:], jnp.float32)
    states = lax.fori_loop(0, steps, step, (zero,) * modes, unroll=2)
    for m in range(modes):
        h_ref[m] = states[m]


def out_kernel(x_ref, f_ref, d_ref, r_ref, skip_ref, h_ref, o_ref):
    modes = d_ref.shape[0]
    steps = x_ref.shape[1] - f_ref.shape[0] + 1

    def step(t, states):
        feats = features(x_ref, f_ref, t)
        u = gate(feats)
        new = []
        conv = None
        for m in range(modes):
            sm = d_ref[m] * states[m] + u
            term = r_ref[m] * sm
            conv = term if conv is None else conv + term
            new.append(sm)
        y = (conv + skip_ref[...] * u).astype(jnp.bfloat16).astype(jnp.float32)
        o_ref[t] = feats[0] * y
        return tuple(new)

    lax.fori_loop(0, steps, step, tuple(h_ref[m] for m in range(modes)), unroll=2)


def run_state(x, f, d):
    streams_count, rows, groups, lanes = x.shape
    taps = f.shape[0]
    modes = d.shape[0]
    grid = (groups // GROUPS,)
    return pl.pallas_call(
        state_kernel,
        grid=grid,
        in_specs=[
            pl.BlockSpec((streams_count, rows, GROUPS, lanes), lambda i: (0, 0, i, 0)),
            pl.BlockSpec((taps, streams_count, GROUPS, lanes), lambda i: (0, 0, i, 0)),
            pl.BlockSpec((modes, GROUPS, lanes), lambda i: (0, i, 0)),
        ],
        out_specs=pl.BlockSpec((modes, GROUPS, lanes), lambda i: (0, i, 0)),
        out_shape=jax.ShapeDtypeStruct((modes, groups, lanes), jnp.float32),
    )(x, f, d)


def run_out(x, f, d, r, skip, h):
    streams_count, rows, groups, lanes = x.shape
    taps = f.shape[0]
    modes = d.shape[0]
    steps = rows - taps + 1
    grid = (groups // GROUPS,)
    return pl.pallas_call(
        out_kernel,
        grid=grid,
        in_specs=[
            pl.BlockSpec((streams_count, rows, GROUPS, lanes), lambda i: (0, 0, i, 0)),
            pl.BlockSpec((taps, streams_count, GROUPS, lanes), lambda i: (0, 0, i, 0)),
            pl.BlockSpec((modes, GROUPS, lanes), lambda i: (0, i, 0)),
            pl.BlockSpec((modes, GROUPS, lanes), lambda i: (0, i, 0)),
            pl.BlockSpec((GROUPS, lanes), lambda i: (i, 0)),
            pl.BlockSpec((modes, GROUPS, lanes), lambda i: (0, i, 0)),
        ],
        out_specs=pl.BlockSpec((steps, GROUPS, lanes), lambda i: (0, i, 0)),
        out_shape=jax.ShapeDtypeStruct((steps, groups, lanes), jnp.float32),
    )(x, f, d, r, skip, h)


def body(streams, short_filter, skip, rates, residues):
    axes = ("ctx", "tp")
    devices = lax.axis_size("ctx") * lax.axis_size("tp")
    tok_rows, streams_count, width = streams.shape
    taps = short_filter.shape[0]
    modes = rates.shape[1]
    groups = width // LANES

    def shift(value, offset):
        pairs = [(j, j + offset) for j in range(devices - offset)]
        return lax.ppermute(value, axes, pairs)

    halo = shift(streams[tok_rows - (taps - 1) :], 1)
    padded = jnp.concatenate([halo, streams], axis=0)
    x = jnp.transpose(padded, (1, 0, 2)).astype(jnp.float32)
    x = x.reshape(streams_count, tok_rows + taps - 1, groups, LANES)
    f = short_filter.reshape(taps, streams_count, groups, LANES)
    rate_t = rates.T.reshape(modes, groups, LANES)
    residue_t = residues.T.reshape(modes, groups, LANES)
    decay = jnp.exp(-rate_t)
    local = run_state(x, f, decay)

    carried = shift(local, 1)
    offset = 1
    while offset < devices:
        factor = jnp.exp(-rate_t * float(tok_rows * offset))
        carried = carried + factor * shift(carried, offset)
        offset *= 2

    out = run_out(x, f, decay, residue_t, skip.reshape(groups, LANES), carried)
    return out.reshape(tok_rows, width).astype(jnp.bfloat16)


def solution(mesh):
    return jax.shard_map(
        body,
        mesh=mesh,
        in_specs=(P(("ctx", "tp"), None, None), P(), P(), P(), P()),
        out_specs=P(("ctx", "tp"), None),
        check_vma=False,
    )
```

```python
import functools

import jax
import jax.numpy as jnp
from jax import lax
from jax.experimental import pallas as pl
from jax.experimental.pallas import tpu as pltpu
from jax.sharding import PartitionSpec as P

LANES = 128
GROUPS = 8


def features(x_ref, f_ref, t):
    taps = f_ref.shape[0]
    feats = []
    for s in range(x_ref.shape[0]):
        acc = f_ref[0, s] * x_ref[s, t + taps - 1]
        for tap in range(1, taps):
            acc = acc + f_ref[tap, s] * x_ref[s, t + taps - 1 - tap]
        feats.append(acc)
    return feats


def gate(feats):
    return (feats[1] * feats[2]).astype(jnp.bfloat16).astype(jnp.float32)


def state_kernel(x_ref, f_ref, d_ref, h_ref):
    modes = d_ref.shape[0]
    steps = x_ref.shape[1] - f_ref.shape[0] + 1

    def step(t, states):
        u = gate(features(x_ref, f_ref, t))
        return tuple(d_ref[m] * states[m] + u for m in range(modes))

    zero = jnp.zeros(h_ref.shape[1:], jnp.float32)
    states = lax.fori_loop(0, steps, step, (zero,) * modes, unroll=2)
    for m in range(modes):
        h_ref[m] = states[m]


def out_kernel(x_ref, f_ref, d_ref, r_ref, skip_ref, h_ref, o_ref):
    modes = d_ref.shape[0]
    steps = x_ref.shape[1] - f_ref.shape[0] + 1

    def step(t, states):
        feats = features(x_ref, f_ref, t)
        u = gate(feats)
        new = []
        conv = None
        for m in range(modes):
            sm = d_ref[m] * states[m] + u
            term = r_ref[m] * sm
            conv = term if conv is None else conv + term
            new.append(sm)
        y = (conv + skip_ref[...] * u).astype(jnp.bfloat16).astype(jnp.float32)
        o_ref[t] = feats[0] * y
        return tuple(new)

    lax.fori_loop(0, steps, step, tuple(h_ref[m] for m in range(modes)), unroll=2)


def run_state(x, f, d):
    streams_count, rows, groups, lanes = x.shape
    taps = f.shape[0]
    modes = d.shape[0]
    grid = (groups // GROUPS,)
    return pl.pallas_call(
        state_kernel,
        grid=grid,
        in_specs=[
            pl.BlockSpec((streams_count, rows, GROUPS, lanes), lambda i: (0, 0, i, 0)),
            pl.BlockSpec((taps, streams_count, GROUPS, lanes), lambda i: (0, 0, i, 0)),
            pl.BlockSpec((modes, GROUPS, lanes), lambda i: (0, i, 0)),
        ],
        out_specs=pl.BlockSpec((modes, GROUPS, lanes), lambda i: (0, i, 0)),
        out_shape=jax.ShapeDtypeStruct((modes, groups, lanes), jnp.float32),
    )(x, f, d)


def run_out(x, f, d, r, skip, h):
    streams_count, rows, groups, lanes = x.shape
    taps = f.shape[0]
    modes = d.shape[0]
    steps = rows - taps + 1
    grid = (groups // GROUPS,)
    return pl.pallas_call(
        out_kernel,
        grid=grid,
        in_specs=[
            pl.BlockSpec((streams_count, rows, GROUPS, lanes), lambda i: (0, 0, i, 0)),
            pl.BlockSpec((taps, streams_count, GROUPS, lanes), lambda i: (0, 0, i, 0)),
            pl.BlockSpec((modes, GROUPS, lanes), lambda i: (0, i, 0)),
            pl.BlockSpec((modes, GROUPS, lanes), lambda i: (0, i, 0)),
            pl.BlockSpec((GROUPS, lanes), lambda i: (i, 0)),
            pl.BlockSpec((modes, GROUPS, lanes), lambda i: (0, i, 0)),
        ],
        out_specs=pl.BlockSpec((steps, GROUPS, lanes), lambda i: (0, i, 0)),
        out_shape=jax.ShapeDtypeStruct((steps, groups, lanes), jnp.float32),
    )(x, f, d, r, skip, h)


def body(streams, short_filter, skip, rates, residues):
    axes = ("ctx", "tp")
    devices = lax.axis_size("ctx") * lax.axis_size("tp")
    tok_rows, streams_count, width = streams.shape
    taps = short_filter.shape[0]
    modes = rates.shape[1]
    groups = width // LANES

    def shift(value, offset):
        pairs = [(j, j + offset) for j in range(devices - offset)]
        return lax.ppermute(value, axes, pairs)

    halo = shift(streams[tok_rows - (taps - 1) :], 1)
    padded = jnp.concatenate([halo, streams], axis=0)
    x = jnp.transpose(padded, (1, 0, 2)).astype(jnp.float32)
    x = x.reshape(streams_count, tok_rows + taps - 1, groups, LANES)
    f = short_filter.reshape(taps, streams_count, groups, LANES)
    rate_t = rates.T.reshape(modes, groups, LANES)
    residue_t = residues.T.reshape(modes, groups, LANES)
    decay = jnp.exp(-rate_t)
    local = run_state(x, f, decay)

    carried = shift(local.astype(jnp.bfloat16), 1).astype(jnp.float32)
    offset = 1
    while offset < devices:
        factor = jnp.exp(-rate_t * float(tok_rows * offset))
        carried = carried + factor * shift(carried.astype(jnp.bfloat16), offset).astype(jnp.float32)
        offset *= 2

    out = run_out(x, f, decay, residue_t, skip.reshape(groups, LANES), carried)
    return out.reshape(tok_rows, width).astype(jnp.bfloat16)


def solution(mesh):
    return jax.shard_map(
        body,
        mesh=mesh,
        in_specs=(P(("ctx", "tp"), None, None), P(), P(), P(), P()),
        out_specs=P(("ctx", "tp"), None),
        check_vma=False,
    )
```

```python
import functools

import jax
import jax.numpy as jnp
from jax import lax
from jax.experimental import pallas as pl
from jax.experimental.pallas import tpu as pltpu
from jax.sharding import PartitionSpec as P

LANES = 128
GROUPS = 8
FIRST_WINDOW = 8


def features(x_ref, f_ref, t):
    taps = f_ref.shape[0]
    feats = []
    for s in range(x_ref.shape[0]):
        acc = f_ref[0, s] * x_ref[s, t + taps - 1]
        for tap in range(1, taps):
            acc = acc + f_ref[tap, s] * x_ref[s, t + taps - 1 - tap]
        feats.append(acc)
    return feats


def gate(feats):
    return (feats[1] * feats[2]).astype(jnp.bfloat16).astype(jnp.float32)


def state_kernel(x_ref, f_ref, d_ref, h_ref):
    modes = d_ref.shape[0]
    steps = x_ref.shape[1] - f_ref.shape[0] + 1

    def step(t, states):
        u = gate(features(x_ref, f_ref, t))
        return tuple(d_ref[m] * states[m] + u for m in range(modes))

    zero = jnp.zeros(h_ref.shape[1:], jnp.float32)
    states = lax.fori_loop(0, steps, step, (zero,) * modes, unroll=2)
    for m in range(modes):
        h_ref[m] = states[m]


def out_kernel(x_ref, f_ref, d_ref, r_ref, skip_ref, h_ref, o_ref):
    modes = d_ref.shape[0]
    steps = x_ref.shape[1] - f_ref.shape[0] + 1

    def step(t, states):
        feats = features(x_ref, f_ref, t)
        u = gate(feats)
        new = []
        conv = None
        for m in range(modes):
            sm = d_ref[m] * states[m] + u
            term = r_ref[m] * sm
            conv = term if conv is None else conv + term
            new.append(sm)
        y = (conv + skip_ref[...] * u).astype(jnp.bfloat16).astype(jnp.float32)
        o_ref[t] = feats[0] * y
        return tuple(new)

    lax.fori_loop(0, steps, step, tuple(h_ref[m] for m in range(modes)), unroll=2)


def run_state(x, f, d):
    streams_count, rows, groups, lanes = x.shape
    taps = f.shape[0]
    modes = d.shape[0]
    grid = (groups // GROUPS,)
    return pl.pallas_call(
        state_kernel,
        grid=grid,
        in_specs=[
            pl.BlockSpec((streams_count, rows, GROUPS, lanes), lambda i: (0, 0, i, 0)),
            pl.BlockSpec((taps, streams_count, GROUPS, lanes), lambda i: (0, 0, i, 0)),
            pl.BlockSpec((modes, GROUPS, lanes), lambda i: (0, i, 0)),
        ],
        out_specs=pl.BlockSpec((modes, GROUPS, lanes), lambda i: (0, i, 0)),
        out_shape=jax.ShapeDtypeStruct((modes, groups, lanes), jnp.float32),
    )(x, f, d)


def run_out(x, f, d, r, skip, h):
    streams_count, rows, groups, lanes = x.shape
    taps = f.shape[0]
    modes = d.shape[0]
    steps = rows - taps + 1
    grid = (groups // GROUPS,)
    return pl.pallas_call(
        out_kernel,
        grid=grid,
        in_specs=[
            pl.BlockSpec((streams_count, rows, GROUPS, lanes), lambda i: (0, 0, i, 0)),
            pl.BlockSpec((taps, streams_count, GROUPS, lanes), lambda i: (0, 0, i, 0)),
            pl.BlockSpec((modes, GROUPS, lanes), lambda i: (0, i, 0)),
            pl.BlockSpec((modes, GROUPS, lanes), lambda i: (0, i, 0)),
            pl.BlockSpec((GROUPS, lanes), lambda i: (i, 0)),
            pl.BlockSpec((modes, GROUPS, lanes), lambda i: (0, i, 0)),
        ],
        out_specs=pl.BlockSpec((steps, GROUPS, lanes), lambda i: (0, i, 0)),
        out_shape=jax.ShapeDtypeStruct((steps, groups, lanes), jnp.float32),
    )(x, f, d, r, skip, h)


def body(streams, short_filter, skip, rates, residues):
    axes = ("ctx", "tp")
    devices = lax.axis_size("ctx") * lax.axis_size("tp")
    tok_rows, streams_count, width = streams.shape
    taps = short_filter.shape[0]
    modes = rates.shape[1]
    groups = width // LANES

    def shift(value, offset):
        pairs = [(j, j + offset) for j in range(devices - offset)]
        return lax.ppermute(value, axes, pairs)

    halo = shift(streams[tok_rows - (taps - 1) :], 1)
    padded = jnp.concatenate([halo, streams], axis=0)
    x = jnp.transpose(padded, (1, 0, 2)).astype(jnp.float32)
    x = x.reshape(streams_count, tok_rows + taps - 1, groups, LANES)
    f = short_filter.reshape(taps, streams_count, groups, LANES)
    rate_t = rates.T.reshape(modes, groups, LANES)
    residue_t = residues.T.reshape(modes, groups, LANES)
    decay = jnp.exp(-rate_t)
    local = run_state(x, f, decay)

    def decay_pow(steps):
        return jnp.exp(-rate_t * float(tok_rows * steps))

    def gather_window(value, spacing, count):
        sent = value.astype(jnp.bfloat16)
        total = None
        for k in range(1, count + 1):
            if k * spacing >= devices:
                break
            term = decay_pow((k - 1) * spacing) * shift(sent, k * spacing).astype(jnp.float32)
            total = term if total is None else total + term
        return total

    first = min(FIRST_WINDOW, devices - 1)
    carried = gather_window(local, 1, first)
    window = first
    while window < devices - 1:
        count = min(-(-(devices - 1) // window) - 1, FIRST_WINDOW)
        carried = carried + decay_pow(window) * gather_window(carried, window, count)
        window *= count + 1

    out = run_out(x, f, decay, residue_t, skip.reshape(groups, LANES), carried)
    return out.reshape(tok_rows, width).astype(jnp.bfloat16)


def solution(mesh):
    return jax.shard_map(
        body,
        mesh=mesh,
        in_specs=(P(("ctx", "tp"), None, None), P(), P(), P(), P()),
        out_specs=P(("ctx", "tp"), None),
        check_vma=False,
    )
```

```python
import jax
import jax.numpy as jnp
from jax import lax
from jax.experimental import pallas as pl
from jax.experimental.pallas import tpu as pltpu
from jax.sharding import PartitionSpec as P

LANES = 128
SUB = 8
BLOCK = 512
FIRST_WINDOW = 8


def lane_slice(c):
    return pl.ds(pl.multiple_of(c * LANES, LANES), LANES)


def row(ref, index, lanes):
    return jnp.broadcast_to(ref[pl.ds(index, 1), lanes], (SUB, LANES))


def first_prev(xs, halo_ref, c, lanes, seg, taps, sub):
    prev = []
    for back in range(1, taps):
        per_stream = []
        for s in range(xs.shape[0]):
            rows = xs[s, c, pl.ds(seg - back, SUB, stride=seg), :]
            edge = jnp.broadcast_to(halo_ref[s, pl.ds(taps - 1 - back, 1), lanes], (SUB, LANES))
            per_stream.append(jnp.where(sub == 0, edge, pltpu.roll(rows, 1, 0)))
        prev.append(per_stream)
    return prev


def step_features(xs, f_ref, c, lanes, seg, j, prev):
    taps = f_ref.shape[0]
    now = [xs[s, c, pl.ds(j, SUB, stride=seg), :] for s in range(xs.shape[0])]
    feats = []
    for s in range(xs.shape[0]):
        acc = jnp.broadcast_to(f_ref[0, pl.ds(s, 1), lanes], (SUB, LANES)) * now[s]
        for tap in range(1, taps):
            weight = jnp.broadcast_to(f_ref[tap, pl.ds(s, 1), lanes], (SUB, LANES))
            acc = acc + weight * prev[tap - 1][s]
        feats.append(acc)
    new_prev = [now] + prev[:-1]
    return feats, new_prev


def gate(feats):
    return (feats[1] * feats[2]).astype(jnp.bfloat16).astype(jnp.float32)


def state_kernel(x_ref, halo_ref, f_ref, a_ref, seg_ref, h_ref, xs, dsc):
    streams_count, rows, block = x_ref.shape
    taps = f_ref.shape[0]
    modes = a_ref.shape[0]
    seg = rows // SUB
    for c in range(block // LANES):
        xs[:, c] = x_ref[:, :, c * LANES : (c + 1) * LANES].astype(jnp.float32)
    sub = lax.broadcasted_iota(jnp.int32, (SUB, LANES), 0)

    def lane_group(c, carry):
        lanes = lane_slice(c)
        for m in range(modes):
            dsc[m] = jnp.exp(-row(a_ref, m, lanes))

        def step(j, state):
            prev, states = state
            feats, prev = step_features(xs, f_ref, c, lanes, seg, j, prev)
            u = gate(feats)
            return prev, tuple(dsc[m] * states[m] + u for m in range(modes))

        zero = jnp.zeros((SUB, LANES), jnp.float32)
        init = (first_prev(xs, halo_ref, c, lanes, seg, taps, sub), (zero,) * modes)
        _, states = lax.fori_loop(0, seg, step, init, unroll=2)
        later = (SUB - 1 - sub).astype(jnp.float32) * float(seg)
        for m in range(modes):
            seg_ref[m, :, lanes] = states[m]
            weight = jnp.exp(-row(a_ref, m, lanes) * later)
            h_ref[pl.ds(m, 1), lanes] = jnp.sum(weight * states[m], axis=0, keepdims=True)
        return carry

    lax.fori_loop(0, block // LANES, lane_group, 0)


def out_kernel(x_ref, halo_ref, f_ref, a_ref, r_ref, skip_ref, seg_ref, hin_ref, o_ref, xs, ys, dsc, rsc):
    streams_count, rows, block = x_ref.shape
    taps = f_ref.shape[0]
    modes = a_ref.shape[0]
    seg = rows // SUB
    for c in range(block // LANES):
        xs[:, c] = x_ref[:, :, c * LANES : (c + 1) * LANES].astype(jnp.float32)
    sub = lax.broadcasted_iota(jnp.int32, (SUB, LANES), 0)

    def lane_group(c, carry):
        lanes = lane_slice(c)
        starts = []
        for m in range(modes):
            rate = row(a_ref, m, lanes)
            dsc[m] = jnp.exp(-rate)
            rsc[m] = row(r_ref, m, lanes)
            ends = seg_ref[m, :, lanes]
            carried = jnp.where(sub >= 1, pltpu.roll(ends, 1, 0), 0.0)
            offset = 1
            while offset < SUB:
                factor = jnp.exp(-rate * float(seg * offset))
                carried = carried + jnp.where(sub >= offset, factor * pltpu.roll(carried, offset, 0), 0.0)
                offset *= 2
            lead = jnp.exp(-rate * (sub.astype(jnp.float32) * float(seg)))
            starts.append(carried + lead * row(hin_ref, m, lanes))
        skip_rows = row(skip_ref, 0, lanes)

        def step(j, state):
            prev, states = state
            feats, prev = step_features(xs, f_ref, c, lanes, seg, j, prev)
            u = gate(feats)
            new = []
            conv = None
            for m in range(modes):
                sm = dsc[m] * states[m] + u
                term = rsc[m] * sm
                conv = term if conv is None else conv + term
                new.append(sm)
            y = (conv + skip_rows * u).astype(jnp.bfloat16).astype(jnp.float32)
            ys[c, pl.ds(j, SUB, stride=seg), :] = feats[0] * y
            return prev, tuple(new)

        init = (first_prev(xs, halo_ref, c, lanes, seg, taps, sub), tuple(starts))
        lax.fori_loop(0, seg, step, init, unroll=2)
        return carry

    lax.fori_loop(0, block // LANES, lane_group, 0)
    for c in range(block // LANES):
        o_ref[:, c * LANES : (c + 1) * LANES] = ys[c].astype(o_ref.dtype)


def run_state(x, halo, f, rate_t):
    streams_count, rows, width = x.shape
    taps = f.shape[0]
    modes = rate_t.shape[0]
    return pl.pallas_call(
        state_kernel,
        grid=(width // BLOCK,),
        in_specs=[
            pl.BlockSpec((streams_count, rows, BLOCK), lambda i: (0, 0, i)),
            pl.BlockSpec((streams_count, taps - 1, BLOCK), lambda i: (0, 0, i)),
            pl.BlockSpec((taps, streams_count, BLOCK), lambda i: (0, 0, i)),
            pl.BlockSpec((modes, BLOCK), lambda i: (0, i)),
        ],
        out_specs=[
            pl.BlockSpec((modes, SUB, BLOCK), lambda i: (0, 0, i)),
            pl.BlockSpec((modes, BLOCK), lambda i: (0, i)),
        ],
        out_shape=[
            jax.ShapeDtypeStruct((modes, SUB, width), jnp.float32),
            jax.ShapeDtypeStruct((modes, width), jnp.float32),
        ],
        scratch_shapes=[
            pltpu.VMEM((streams_count, BLOCK // LANES, rows, LANES), jnp.float32),
            pltpu.VMEM((modes, SUB, LANES), jnp.float32),
        ],
    )(x, halo, f, rate_t)


def run_out(x, halo, f, rate_t, residue_t, skip, ends, hin):
    streams_count, rows, width = x.shape
    taps = f.shape[0]
    modes = rate_t.shape[0]
    return pl.pallas_call(
        out_kernel,
        grid=(width // BLOCK,),
        in_specs=[
            pl.BlockSpec((streams_count, rows, BLOCK), lambda i: (0, 0, i)),
            pl.BlockSpec((streams_count, taps - 1, BLOCK), lambda i: (0, 0, i)),
            pl.BlockSpec((taps, streams_count, BLOCK), lambda i: (0, 0, i)),
            pl.BlockSpec((modes, BLOCK), lambda i: (0, i)),
            pl.BlockSpec((modes, BLOCK), lambda i: (0, i)),
            pl.BlockSpec((1, BLOCK), lambda i: (0, i)),
            pl.BlockSpec((modes, SUB, BLOCK), lambda i: (0, 0, i)),
            pl.BlockSpec((modes, BLOCK), lambda i: (0, i)),
        ],
        out_specs=pl.BlockSpec((rows, BLOCK), lambda i: (0, i)),
        out_shape=jax.ShapeDtypeStruct((rows, width), jnp.bfloat16),
        scratch_shapes=[
            pltpu.VMEM((streams_count, BLOCK // LANES, rows, LANES), jnp.float32),
            pltpu.VMEM((BLOCK // LANES, rows, LANES), jnp.float32),
            pltpu.VMEM((modes, SUB, LANES), jnp.float32),
            pltpu.VMEM((modes, SUB, LANES), jnp.float32),
        ],
    )(x, halo, f, rate_t, residue_t, skip, ends, hin)


def body(streams, short_filter, skip, rates, residues):
    axes = ("ctx", "tp")
    devices = lax.axis_size("ctx") * lax.axis_size("tp")
    tok_rows, streams_count, width = streams.shape
    taps = short_filter.shape[0]
    modes = rates.shape[1]

    def shift(value, offset):
        pairs = [(j, j + offset) for j in range(devices - offset)]
        return lax.ppermute(value, axes, pairs)

    halo = shift(streams[tok_rows - (taps - 1) :], 1)
    halo = jnp.transpose(halo, (1, 0, 2)).astype(jnp.float32)
    x = jnp.transpose(streams, (1, 0, 2))
    rate_t = rates.T
    residue_t = residues.T
    ends, local = run_state(x, halo, short_filter, rate_t)

    def decay_pow(steps):
        return jnp.exp(-rate_t * float(tok_rows * steps))

    def gather_window(value, spacing, count):
        sent = value.astype(jnp.bfloat16)
        total = None
        for k in range(1, count + 1):
            if k * spacing >= devices:
                break
            term = decay_pow((k - 1) * spacing) * shift(sent, k * spacing).astype(jnp.float32)
            total = term if total is None else total + term
        return total

    first = min(FIRST_WINDOW, devices - 1)
    carried = gather_window(local, 1, first)
    window = first
    while window < devices - 1:
        count = min(-(-(devices - 1) // window) - 1, FIRST_WINDOW)
        carried = carried + decay_pow(window) * gather_window(carried, window, count)
        window *= count + 1

    return run_out(x, halo, short_filter, rate_t, residue_t, skip.reshape(1, width), ends, carried)


def solution(mesh):
    return jax.shard_map(
        body,
        mesh=mesh,
        in_specs=(P(("ctx", "tp"), None, None), P(), P(), P(), P()),
        out_specs=P(("ctx", "tp"), None),
        check_vma=False,
    )
```

```python
import jax
import jax.numpy as jnp
from jax import lax
from jax.experimental import pallas as pl
from jax.experimental.pallas import tpu as pltpu
from jax.sharding import PartitionSpec as P

LANES = 128
SUB = 8
BLOCK = 512
FIRST_WINDOW = 3
UNROLL = 4


def lane_slice(c):
    return pl.ds(pl.multiple_of(c * LANES, LANES), LANES)


def row(ref, index, lanes):
    return jnp.broadcast_to(ref[pl.ds(index, 1), lanes], (SUB, LANES))


def first_prev(xs, halo_ref, c, lanes, seg, taps, sub):
    prev = []
    for back in range(1, taps):
        per_stream = []
        for s in range(xs.shape[0]):
            rows = xs[s, c, pl.ds(seg - back, SUB, stride=seg), :]
            edge = jnp.broadcast_to(halo_ref[s, pl.ds(taps - 1 - back, 1), lanes], (SUB, LANES))
            per_stream.append(jnp.where(sub == 0, edge, pltpu.roll(rows, 1, 0)))
        prev.append(per_stream)
    return prev


def fill_filters(f_ref, fsc, lanes):
    streams_count = f_ref.shape[1]
    for tap in range(f_ref.shape[0]):
        for s in range(streams_count):
            fsc[tap * streams_count + s] = row(f_ref.at[tap], s, lanes)


def step_features(xs, fsc, c, seg, j, prev):
    streams_count = xs.shape[0]
    taps = len(prev) + 1
    now = [xs[s, c, pl.ds(j, SUB, stride=seg), :] for s in range(streams_count)]
    feats = []
    for s in range(streams_count):
        acc = fsc[s] * now[s]
        for tap in range(1, taps):
            acc = acc + fsc[tap * streams_count + s] * prev[tap - 1][s]
        feats.append(acc)
    new_prev = [now] + prev[:-1]
    return feats, new_prev


def gate(feats):
    return (feats[1] * feats[2]).astype(jnp.bfloat16).astype(jnp.float32)


def state_kernel(x_ref, halo_ref, f_ref, a_ref, seg_ref, h_ref, xs, dsc, fsc):
    streams_count, rows, block = x_ref.shape
    taps = f_ref.shape[0]
    modes = a_ref.shape[0]
    seg = rows // SUB
    for c in range(block // LANES):
        xs[:, c] = x_ref[:, :, c * LANES : (c + 1) * LANES].astype(jnp.float32)
    sub = lax.broadcasted_iota(jnp.int32, (SUB, LANES), 0)

    def lane_group(c, carry):
        lanes = lane_slice(c)
        fill_filters(f_ref, fsc, lanes)
        for m in range(modes):
            dsc[m] = jnp.exp(-row(a_ref, m, lanes))

        def step(j, state):
            prev, states = state
            feats, prev = step_features(xs, fsc, c, seg, j, prev)
            u = gate(feats)
            return prev, tuple(dsc[m] * states[m] + u for m in range(modes))

        zero = jnp.zeros((SUB, LANES), jnp.float32)
        init = (first_prev(xs, halo_ref, c, lanes, seg, taps, sub), (zero,) * modes)
        _, states = lax.fori_loop(0, seg, step, init, unroll=UNROLL)
        later = (SUB - 1 - sub).astype(jnp.float32) * float(seg)
        for m in range(modes):
            seg_ref[m, :, lanes] = states[m]
            weight = jnp.exp(-row(a_ref, m, lanes) * later)
            h_ref[pl.ds(m, 1), lanes] = jnp.sum(weight * states[m], axis=0, keepdims=True)
        return carry

    lax.fori_loop(0, block // LANES, lane_group, 0)


def out_kernel(x_ref, halo_ref, f_ref, a_ref, r_ref, skip_ref, seg_ref, hin_ref, o_ref, xs, ys, dsc, rsc, fsc):
    streams_count, rows, block = x_ref.shape
    taps = f_ref.shape[0]
    modes = a_ref.shape[0]
    seg = rows // SUB
    for c in range(block // LANES):
        xs[:, c] = x_ref[:, :, c * LANES : (c + 1) * LANES].astype(jnp.float32)
    sub = lax.broadcasted_iota(jnp.int32, (SUB, LANES), 0)

    def lane_group(c, carry):
        lanes = lane_slice(c)
        fill_filters(f_ref, fsc, lanes)
        starts = []
        for m in range(modes):
            rate = row(a_ref, m, lanes)
            dsc[m] = jnp.exp(-rate)
            rsc[m] = row(r_ref, m, lanes)
            ends = seg_ref[m, :, lanes]
            carried = jnp.where(sub >= 1, pltpu.roll(ends, 1, 0), 0.0)
            offset = 1
            while offset < SUB:
                factor = jnp.exp(-rate * float(seg * offset))
                carried = carried + jnp.where(sub >= offset, factor * pltpu.roll(carried, offset, 0), 0.0)
                offset *= 2
            lead = jnp.exp(-rate * (sub.astype(jnp.float32) * float(seg)))
            starts.append(carried + lead * row(hin_ref, m, lanes))
        skip_rows = row(skip_ref, 0, lanes)

        def step(j, state):
            prev, states = state
            feats, prev = step_features(xs, fsc, c, seg, j, prev)
            u = gate(feats)
            new = []
            conv = None
            for m in range(modes):
                sm = dsc[m] * states[m] + u
                term = rsc[m] * sm
                conv = term if conv is None else conv + term
                new.append(sm)
            y = (conv + skip_rows * u).astype(jnp.bfloat16).astype(jnp.float32)
            ys[c, pl.ds(j, SUB, stride=seg), :] = feats[0] * y
            return prev, tuple(new)

        init = (first_prev(xs, halo_ref, c, lanes, seg, taps, sub), tuple(starts))
        lax.fori_loop(0, seg, step, init, unroll=UNROLL)
        return carry

    lax.fori_loop(0, block // LANES, lane_group, 0)
    for c in range(block // LANES):
        o_ref[:, c * LANES : (c + 1) * LANES] = ys[c].astype(o_ref.dtype)


def run_state(x, halo, f, rate_t):
    streams_count, rows, width = x.shape
    taps = f.shape[0]
    modes = rate_t.shape[0]
    return pl.pallas_call(
        state_kernel,
        grid=(width // BLOCK,),
        in_specs=[
            pl.BlockSpec((streams_count, rows, BLOCK), lambda i: (0, 0, i)),
            pl.BlockSpec((streams_count, taps - 1, BLOCK), lambda i: (0, 0, i)),
            pl.BlockSpec((taps, streams_count, BLOCK), lambda i: (0, 0, i)),
            pl.BlockSpec((modes, BLOCK), lambda i: (0, i)),
        ],
        out_specs=[
            pl.BlockSpec((modes, SUB, BLOCK), lambda i: (0, 0, i)),
            pl.BlockSpec((modes, BLOCK), lambda i: (0, i)),
        ],
        out_shape=[
            jax.ShapeDtypeStruct((modes, SUB, width), jnp.float32),
            jax.ShapeDtypeStruct((modes, width), jnp.float32),
        ],
        scratch_shapes=[
            pltpu.VMEM((streams_count, BLOCK // LANES, rows, LANES), jnp.float32),
            pltpu.VMEM((modes, SUB, LANES), jnp.float32),
            pltpu.VMEM((taps * streams_count, SUB, LANES), jnp.float32),
        ],
    )(x, halo, f, rate_t)


def run_out(x, halo, f, rate_t, residue_t, skip, ends, hin):
    streams_count, rows, width = x.shape
    taps = f.shape[0]
    modes = rate_t.shape[0]
    return pl.pallas_call(
        out_kernel,
        grid=(width // BLOCK,),
        in_specs=[
            pl.BlockSpec((streams_count, rows, BLOCK), lambda i: (0, 0, i)),
            pl.BlockSpec((streams_count, taps - 1, BLOCK), lambda i: (0, 0, i)),
            pl.BlockSpec((taps, streams_count, BLOCK), lambda i: (0, 0, i)),
            pl.BlockSpec((modes, BLOCK), lambda i: (0, i)),
            pl.BlockSpec((modes, BLOCK), lambda i: (0, i)),
            pl.BlockSpec((1, BLOCK), lambda i: (0, i)),
            pl.BlockSpec((modes, SUB, BLOCK), lambda i: (0, 0, i)),
            pl.BlockSpec((modes, BLOCK), lambda i: (0, i)),
        ],
        out_specs=pl.BlockSpec((rows, BLOCK), lambda i: (0, i)),
        out_shape=jax.ShapeDtypeStruct((rows, width), jnp.bfloat16),
        scratch_shapes=[
            pltpu.VMEM((streams_count, BLOCK // LANES, rows, LANES), jnp.float32),
            pltpu.VMEM((BLOCK // LANES, rows, LANES), jnp.float32),
            pltpu.VMEM((modes, SUB, LANES), jnp.float32),
            pltpu.VMEM((modes, SUB, LANES), jnp.float32),
            pltpu.VMEM((taps * streams_count, SUB, LANES), jnp.float32),
        ],
    )(x, halo, f, rate_t, residue_t, skip, ends, hin)


def body(streams, short_filter, skip, rates, residues):
    axes = ("ctx", "tp")
    devices = lax.axis_size("ctx") * lax.axis_size("tp")
    tok_rows, streams_count, width = streams.shape
    taps = short_filter.shape[0]
    modes = rates.shape[1]

    def shift(value, offset):
        pairs = [(j, j + offset) for j in range(devices - offset)]
        return lax.ppermute(value, axes, pairs)

    halo = shift(streams[tok_rows - (taps - 1) :], 1)
    halo = jnp.transpose(halo, (1, 0, 2)).astype(jnp.float32)
    x = jnp.transpose(streams, (1, 0, 2))
    rate_t = rates.T
    residue_t = residues.T
    ends, local = run_state(x, halo, short_filter, rate_t)

    def decay_pow(steps):
        return jnp.exp(-rate_t * float(tok_rows * steps))

    def gather_window(value, spacing, count):
        sent = value.astype(jnp.bfloat16)
        total = None
        for k in range(1, count + 1):
            if k * spacing >= devices:
                break
            term = decay_pow((k - 1) * spacing) * shift(sent, k * spacing).astype(jnp.float32)
            total = term if total is None else total + term
        return total

    first = min(FIRST_WINDOW, devices - 1)
    carried = gather_window(local, 1, first)
    window = first
    while window < devices - 1:
        count = min(-(-(devices - 1) // window) - 1, FIRST_WINDOW)
        carried = carried + decay_pow(window) * gather_window(carried, window, count)
        window *= count + 1

    return run_out(x, halo, short_filter, rate_t, residue_t, skip.reshape(1, width), ends, carried)


def solution(mesh):
    return jax.shard_map(
        body,
        mesh=mesh,
        in_specs=(P(("ctx", "tp"), None, None), P(), P(), P(), P()),
        out_specs=P(("ctx", "tp"), None),
        check_vma=False,
    )
```

```python
import jax
import jax.numpy as jnp
from jax import lax
from jax.experimental import pallas as pl
from jax.experimental.pallas import tpu as pltpu
from jax.sharding import PartitionSpec as P

LANES = 128
SUB = 8
BLOCK = 512
FIRST_WINDOW = 3
UNROLL = 4


def lane_slice(c):
    return pl.ds(pl.multiple_of(c * LANES, LANES), LANES)


def row(ref, index, lanes):
    return jnp.broadcast_to(ref[pl.ds(index, 1), lanes], (SUB, LANES))


def first_prev(xs, halo_ref, c, lanes, seg, taps, sub):
    prev = []
    for back in range(1, taps):
        per_stream = []
        for s in range(xs.shape[0]):
            rows = xs[s, c, pl.ds(seg - back, SUB, stride=seg), :]
            edge = jnp.broadcast_to(halo_ref[s, pl.ds(taps - 1 - back, 1), lanes], (SUB, LANES))
            per_stream.append(jnp.where(sub == 0, edge, pltpu.roll(rows, 1, 0)))
        prev.append(per_stream)
    return prev


def fill_filters(f_ref, fsc, lanes):
    streams_count = f_ref.shape[1]
    for tap in range(f_ref.shape[0]):
        for s in range(streams_count):
            fsc[tap * streams_count + s] = row(f_ref.at[tap], s, lanes)


def step_features(xs, fsc, c, seg, j, prev):
    streams_count = xs.shape[0]
    taps = len(prev) + 1
    now = [xs[s, c, pl.ds(j, SUB, stride=seg), :] for s in range(streams_count)]
    feats = []
    for s in range(streams_count):
        acc = fsc[s] * now[s]
        for tap in range(1, taps):
            acc = acc + fsc[tap * streams_count + s] * prev[tap - 1][s]
        feats.append(acc)
    new_prev = [now] + prev[:-1]
    return feats, new_prev


def gate(feats):
    return (feats[1] * feats[2]).astype(jnp.bfloat16).astype(jnp.float32)


def state_kernel(x_ref, halo_ref, f_ref, a_ref, seg_ref, h_ref, xs, dsc, fsc):
    streams_count, rows, block = x_ref.shape
    taps = f_ref.shape[0]
    modes = a_ref.shape[0]
    seg = rows // SUB
    for c in range(block // LANES):
        xs[:, c] = x_ref[:, :, c * LANES : (c + 1) * LANES].astype(jnp.float32)
    sub = lax.broadcasted_iota(jnp.int32, (SUB, LANES), 0)

    def lane_group(c, carry):
        lanes = lane_slice(c)
        fill_filters(f_ref, fsc, lanes)
        for m in range(modes):
            dsc[m] = jnp.exp(-row(a_ref, m, lanes))

        def step(j, state):
            prev, states = state
            feats, prev = step_features(xs, fsc, c, seg, j, prev)
            u = gate(feats)
            return prev, tuple(dsc[m] * states[m] + u for m in range(modes))

        zero = jnp.zeros((SUB, LANES), jnp.float32)
        init = (first_prev(xs, halo_ref, c, lanes, seg, taps, sub), (zero,) * modes)
        _, states = lax.fori_loop(0, seg, step, init, unroll=UNROLL)
        later = (SUB - 1 - sub).astype(jnp.float32) * float(seg)
        for m in range(modes):
            seg_ref[m, :, lanes] = states[m]
            weight = jnp.exp(-row(a_ref, m, lanes) * later)
            h_ref[pl.ds(m, 1), lanes] = jnp.sum(weight * states[m], axis=0, keepdims=True)
        return carry

    lax.fori_loop(0, block // LANES, lane_group, 0)


def out_kernel(
    x_ref, halo_ref, f_ref, a_ref, r_ref, skip_ref, seg_ref, fix_ref, hin_ref, o_ref, xs, ys, dsc, rsc, fsc
):
    streams_count, rows, block = x_ref.shape
    taps = f_ref.shape[0]
    modes = a_ref.shape[0]
    seg = rows // SUB
    for c in range(block // LANES):
        xs[:, c] = x_ref[:, :, c * LANES : (c + 1) * LANES].astype(jnp.float32)
    sub = lax.broadcasted_iota(jnp.int32, (SUB, LANES), 0)

    def lane_group(c, carry):
        lanes = lane_slice(c)
        fill_filters(f_ref, fsc, lanes)
        starts = []
        for m in range(modes):
            rate = row(a_ref, m, lanes)
            dsc[m] = jnp.exp(-rate)
            rsc[m] = row(r_ref, m, lanes)
            ends = seg_ref[m, :, lanes] + jnp.where(sub == 0, row(fix_ref, m, lanes), 0.0)
            carried = jnp.where(sub >= 1, pltpu.roll(ends, 1, 0), 0.0)
            offset = 1
            while offset < SUB:
                factor = jnp.exp(-rate * float(seg * offset))
                carried = carried + jnp.where(sub >= offset, factor * pltpu.roll(carried, offset, 0), 0.0)
                offset *= 2
            lead = jnp.exp(-rate * (sub.astype(jnp.float32) * float(seg)))
            starts.append(carried + lead * row(hin_ref, m, lanes))
        skip_rows = row(skip_ref, 0, lanes)

        def step(j, state):
            prev, states = state
            feats, prev = step_features(xs, fsc, c, seg, j, prev)
            u = gate(feats)
            new = []
            conv = None
            for m in range(modes):
                sm = dsc[m] * states[m] + u
                term = rsc[m] * sm
                conv = term if conv is None else conv + term
                new.append(sm)
            y = (conv + skip_rows * u).astype(jnp.bfloat16).astype(jnp.float32)
            ys[c, pl.ds(j, SUB, stride=seg), :] = feats[0] * y
            return prev, tuple(new)

        init = (first_prev(xs, halo_ref, c, lanes, seg, taps, sub), tuple(starts))
        lax.fori_loop(0, seg, step, init, unroll=UNROLL)
        return carry

    lax.fori_loop(0, block // LANES, lane_group, 0)
    for c in range(block // LANES):
        o_ref[:, c * LANES : (c + 1) * LANES] = ys[c].astype(o_ref.dtype)


def run_state(x, halo, f, rate_t):
    streams_count, rows, width = x.shape
    taps = f.shape[0]
    modes = rate_t.shape[0]
    return pl.pallas_call(
        state_kernel,
        grid=(width // BLOCK,),
        in_specs=[
            pl.BlockSpec((streams_count, rows, BLOCK), lambda i: (0, 0, i)),
            pl.BlockSpec((streams_count, taps - 1, BLOCK), lambda i: (0, 0, i)),
            pl.BlockSpec((taps, streams_count, BLOCK), lambda i: (0, 0, i)),
            pl.BlockSpec((modes, BLOCK), lambda i: (0, i)),
        ],
        out_specs=[
            pl.BlockSpec((modes, SUB, BLOCK), lambda i: (0, 0, i)),
            pl.BlockSpec((modes, BLOCK), lambda i: (0, i)),
        ],
        out_shape=[
            jax.ShapeDtypeStruct((modes, SUB, width), jnp.float32),
            jax.ShapeDtypeStruct((modes, width), jnp.float32),
        ],
        scratch_shapes=[
            pltpu.VMEM((streams_count, BLOCK // LANES, rows, LANES), jnp.float32),
            pltpu.VMEM((modes, SUB, LANES), jnp.float32),
            pltpu.VMEM((taps * streams_count, SUB, LANES), jnp.float32),
        ],
    )(x, halo, f, rate_t)


def run_out(x, halo, f, rate_t, residue_t, skip, ends, fix, hin):
    streams_count, rows, width = x.shape
    taps = f.shape[0]
    modes = rate_t.shape[0]
    return pl.pallas_call(
        out_kernel,
        grid=(width // BLOCK,),
        in_specs=[
            pl.BlockSpec((streams_count, rows, BLOCK), lambda i: (0, 0, i)),
            pl.BlockSpec((streams_count, taps - 1, BLOCK), lambda i: (0, 0, i)),
            pl.BlockSpec((taps, streams_count, BLOCK), lambda i: (0, 0, i)),
            pl.BlockSpec((modes, BLOCK), lambda i: (0, i)),
            pl.BlockSpec((modes, BLOCK), lambda i: (0, i)),
            pl.BlockSpec((1, BLOCK), lambda i: (0, i)),
            pl.BlockSpec((modes, SUB, BLOCK), lambda i: (0, 0, i)),
            pl.BlockSpec((modes, BLOCK), lambda i: (0, i)),
            pl.BlockSpec((modes, BLOCK), lambda i: (0, i)),
        ],
        out_specs=pl.BlockSpec((rows, BLOCK), lambda i: (0, i)),
        out_shape=jax.ShapeDtypeStruct((rows, width), jnp.bfloat16),
        scratch_shapes=[
            pltpu.VMEM((streams_count, BLOCK // LANES, rows, LANES), jnp.float32),
            pltpu.VMEM((BLOCK // LANES, rows, LANES), jnp.float32),
            pltpu.VMEM((modes, SUB, LANES), jnp.float32),
            pltpu.VMEM((modes, SUB, LANES), jnp.float32),
            pltpu.VMEM((taps * streams_count, SUB, LANES), jnp.float32),
        ],
    )(x, halo, f, rate_t, residue_t, skip, ends, fix, hin)


def body(streams, short_filter, skip, rates, residues):
    axes = ("ctx", "tp")
    devices = lax.axis_size("ctx") * lax.axis_size("tp")
    tok_rows, streams_count, width = streams.shape
    taps = short_filter.shape[0]
    modes = rates.shape[1]

    def shift(value, offset):
        pairs = [(j, j + offset) for j in range(devices - offset)]
        return lax.ppermute(value, axes, pairs)

    halo_rows = shift(streams[tok_rows - (taps - 1) :], 1).astype(jnp.float32)
    halo = jnp.transpose(halo_rows, (1, 0, 2))
    x = jnp.transpose(streams, (1, 0, 2))
    rate_t = rates.T
    residue_t = residues.T
    ends, local = run_state(x, jnp.zeros_like(halo), short_filter, rate_t)

    head = streams[: taps - 1].astype(jnp.float32)

    def head_gate(before):
        rows = jnp.concatenate([before, head], axis=0)
        gated = []
        for t in range(taps - 1):
            feat = short_filter[0] * rows[t + taps - 1]
            for tap in range(1, taps):
                feat = feat + short_filter[tap] * rows[t + taps - 1 - tap]
            gated.append((feat[1] * feat[2]).astype(jnp.bfloat16).astype(jnp.float32))
        return gated

    seg = tok_rows // SUB
    true_head = head_gate(halo_rows)
    zero_head = head_gate(jnp.zeros_like(halo_rows))
    local_fix = None
    ends_fix = None
    for t in range(taps - 1):
        delta = (true_head[t] - zero_head[t])[None, :]
        to_end = jnp.exp(-rate_t * float(tok_rows - 1 - t)) * delta
        to_seg = jnp.exp(-rate_t * float(seg - 1 - t)) * delta
        local_fix = to_end if local_fix is None else local_fix + to_end
        ends_fix = to_seg if ends_fix is None else ends_fix + to_seg
    local = local + local_fix

    def decay_pow(steps):
        return jnp.exp(-rate_t * float(tok_rows * steps))

    def gather_window(value, spacing, count):
        sent = value.astype(jnp.bfloat16)
        total = None
        for k in range(1, count + 1):
            if k * spacing >= devices:
                break
            term = decay_pow((k - 1) * spacing) * shift(sent, k * spacing).astype(jnp.float32)
            total = term if total is None else total + term
        return total

    first = min(FIRST_WINDOW, devices - 1)
    carried = gather_window(local, 1, first)
    window = first
    while window < devices - 1:
        count = min(-(-(devices - 1) // window) - 1, FIRST_WINDOW)
        carried = carried + decay_pow(window) * gather_window(carried, window, count)
        window *= count + 1

    return run_out(x, halo, short_filter, rate_t, residue_t, skip.reshape(1, width), ends, ends_fix, carried)


def solution(mesh):
    return jax.shard_map(
        body,
        mesh=mesh,
        in_specs=(P(("ctx", "tp"), None, None), P(), P(), P(), P()),
        out_specs=P(("ctx", "tp"), None),
        check_vma=False,
    )
```

```python
import jax
import jax.numpy as jnp
from jax import lax
from jax.experimental import pallas as pl
from jax.experimental.pallas import tpu as pltpu
from jax.sharding import PartitionSpec as P

LANES = 128
SUB = 8
BLOCK = 512
FIRST_WINDOW = 3
UNROLL = 8


def lane_slice(c):
    return pl.ds(pl.multiple_of(c * LANES, LANES), LANES)


def row(ref, index, lanes):
    return jnp.broadcast_to(ref[pl.ds(index, 1), lanes], (SUB, LANES))


def first_prev(xs, halo_ref, c, lanes, seg, taps, sub):
    prev = []
    for back in range(1, taps):
        per_stream = []
        for s in range(xs.shape[0]):
            rows = xs[s, c, pl.ds(seg - back, SUB, stride=seg), :]
            edge = jnp.broadcast_to(halo_ref[s, pl.ds(taps - 1 - back, 1), lanes], (SUB, LANES))
            per_stream.append(jnp.where(sub == 0, edge, pltpu.roll(rows, 1, 0)))
        prev.append(per_stream)
    return prev


def fill_filters(f_ref, fsc, lanes):
    streams_count = f_ref.shape[1]
    for tap in range(f_ref.shape[0]):
        for s in range(streams_count):
            fsc[tap * streams_count + s] = row(f_ref.at[tap], s, lanes)


def step_features(xs, fsc, c, seg, j, prev):
    streams_count = xs.shape[0]
    taps = len(prev) + 1
    now = [xs[s, c, pl.ds(j, SUB, stride=seg), :] for s in range(streams_count)]
    feats = []
    for s in range(streams_count):
        acc = fsc[s] * now[s]
        for tap in range(1, taps):
            acc = acc + fsc[tap * streams_count + s] * prev[tap - 1][s]
        feats.append(acc)
    new_prev = [now] + prev[:-1]
    return feats, new_prev


def gate(feats):
    return (feats[1] * feats[2]).astype(jnp.bfloat16).astype(jnp.float32)


def state_kernel(x_ref, halo_ref, f_ref, a_ref, seg_ref, h_ref, xs, dsc, fsc):
    streams_count, rows, block = x_ref.shape
    taps = f_ref.shape[0]
    modes = a_ref.shape[0]
    seg = rows // SUB
    for c in range(block // LANES):
        xs[:, c] = x_ref[:, :, c * LANES : (c + 1) * LANES].astype(jnp.float32)
    sub = lax.broadcasted_iota(jnp.int32, (SUB, LANES), 0)

    def lane_group(c, carry):
        lanes = lane_slice(c)
        fill_filters(f_ref, fsc, lanes)
        for m in range(modes):
            dsc[m] = jnp.exp(-row(a_ref, m, lanes))

        def step(j, state):
            prev, states = state
            feats, prev = step_features(xs, fsc, c, seg, j, prev)
            u = gate(feats)
            return prev, tuple(dsc[m] * states[m] + u for m in range(modes))

        zero = jnp.zeros((SUB, LANES), jnp.float32)
        init = (first_prev(xs, halo_ref, c, lanes, seg, taps, sub), (zero,) * modes)
        _, states = lax.fori_loop(0, seg, step, init, unroll=UNROLL)
        later = (SUB - 1 - sub).astype(jnp.float32) * float(seg)
        for m in range(modes):
            seg_ref[m, :, lanes] = states[m]
            weight = jnp.exp(-row(a_ref, m, lanes) * later)
            h_ref[pl.ds(m, 1), lanes] = jnp.sum(weight * states[m], axis=0, keepdims=True)
        return carry

    lax.fori_loop(0, block // LANES, lane_group, 0)


def out_kernel(
    x_ref, halo_ref, f_ref, a_ref, r_ref, skip_ref, seg_ref, fix_ref, hin_ref, o_ref, xs, ys, dsc, rsc, fsc
):
    streams_count, rows, block = x_ref.shape
    taps = f_ref.shape[0]
    modes = a_ref.shape[0]
    seg = rows // SUB
    for c in range(block // LANES):
        xs[:, c] = x_ref[:, :, c * LANES : (c + 1) * LANES].astype(jnp.float32)
    sub = lax.broadcasted_iota(jnp.int32, (SUB, LANES), 0)

    def lane_group(c, carry):
        lanes = lane_slice(c)
        fill_filters(f_ref, fsc, lanes)
        starts = []
        for m in range(modes):
            rate = row(a_ref, m, lanes)
            dsc[m] = jnp.exp(-rate)
            rsc[m] = row(r_ref, m, lanes)
            ends = seg_ref[m, :, lanes] + jnp.where(sub == 0, row(fix_ref, m, lanes), 0.0)
            carried = jnp.where(sub >= 1, pltpu.roll(ends, 1, 0), 0.0)
            offset = 1
            while offset < SUB:
                factor = jnp.exp(-rate * float(seg * offset))
                carried = carried + jnp.where(sub >= offset, factor * pltpu.roll(carried, offset, 0), 0.0)
                offset *= 2
            lead = jnp.exp(-rate * (sub.astype(jnp.float32) * float(seg)))
            starts.append(carried + lead * row(hin_ref, m, lanes))
        skip_rows = row(skip_ref, 0, lanes)

        def step(j, state):
            prev, states = state
            feats, prev = step_features(xs, fsc, c, seg, j, prev)
            u = gate(feats)
            new = [dsc[m] * states[m] + u for m in range(modes)]
            terms = [rsc[m] * new[m] for m in range(modes)]
            while len(terms) > 1:
                paired = [terms[i] + terms[i + 1] for i in range(0, len(terms) - 1, 2)]
                terms = paired + terms[len(terms) - len(terms) % 2 :]
            conv = terms[0]
            y = (conv + skip_rows * u).astype(jnp.bfloat16).astype(jnp.float32)
            ys[c, pl.ds(j, SUB, stride=seg), :] = feats[0] * y
            return prev, tuple(new)

        init = (first_prev(xs, halo_ref, c, lanes, seg, taps, sub), tuple(starts))
        lax.fori_loop(0, seg, step, init, unroll=UNROLL)
        return carry

    lax.fori_loop(0, block // LANES, lane_group, 0)
    for c in range(block // LANES):
        o_ref[:, c * LANES : (c + 1) * LANES] = ys[c].astype(o_ref.dtype)


def run_state(x, halo, f, rate_t):
    streams_count, rows, width = x.shape
    taps = f.shape[0]
    modes = rate_t.shape[0]
    return pl.pallas_call(
        state_kernel,
        grid=(width // BLOCK,),
        in_specs=[
            pl.BlockSpec((streams_count, rows, BLOCK), lambda i: (0, 0, i)),
            pl.BlockSpec((streams_count, taps - 1, BLOCK), lambda i: (0, 0, i)),
            pl.BlockSpec((taps, streams_count, BLOCK), lambda i: (0, 0, i)),
            pl.BlockSpec((modes, BLOCK), lambda i: (0, i)),
        ],
        out_specs=[
            pl.BlockSpec((modes, SUB, BLOCK), lambda i: (0, 0, i)),
            pl.BlockSpec((modes, BLOCK), lambda i: (0, i)),
        ],
        out_shape=[
            jax.ShapeDtypeStruct((modes, SUB, width), jnp.float32),
            jax.ShapeDtypeStruct((modes, width), jnp.float32),
        ],
        scratch_shapes=[
            pltpu.VMEM((streams_count, BLOCK // LANES, rows, LANES), jnp.float32),
            pltpu.VMEM((modes, SUB, LANES), jnp.float32),
            pltpu.VMEM((taps * streams_count, SUB, LANES), jnp.float32),
        ],
    )(x, halo, f, rate_t)


def run_out(x, halo, f, rate_t, residue_t, skip, ends, fix, hin):
    streams_count, rows, width = x.shape
    taps = f.shape[0]
    modes = rate_t.shape[0]
    return pl.pallas_call(
        out_kernel,
        grid=(width // BLOCK,),
        in_specs=[
            pl.BlockSpec((streams_count, rows, BLOCK), lambda i: (0, 0, i)),
            pl.BlockSpec((streams_count, taps - 1, BLOCK), lambda i: (0, 0, i)),
            pl.BlockSpec((taps, streams_count, BLOCK), lambda i: (0, 0, i)),
            pl.BlockSpec((modes, BLOCK), lambda i: (0, i)),
            pl.BlockSpec((modes, BLOCK), lambda i: (0, i)),
            pl.BlockSpec((1, BLOCK), lambda i: (0, i)),
            pl.BlockSpec((modes, SUB, BLOCK), lambda i: (0, 0, i)),
            pl.BlockSpec((modes, BLOCK), lambda i: (0, i)),
            pl.BlockSpec((modes, BLOCK), lambda i: (0, i)),
        ],
        out_specs=pl.BlockSpec((rows, BLOCK), lambda i: (0, i)),
        out_shape=jax.ShapeDtypeStruct((rows, width), jnp.bfloat16),
        scratch_shapes=[
            pltpu.VMEM((streams_count, BLOCK // LANES, rows, LANES), jnp.float32),
            pltpu.VMEM((BLOCK // LANES, rows, LANES), jnp.float32),
            pltpu.VMEM((modes, SUB, LANES), jnp.float32),
            pltpu.VMEM((modes, SUB, LANES), jnp.float32),
            pltpu.VMEM((taps * streams_count, SUB, LANES), jnp.float32),
        ],
    )(x, halo, f, rate_t, residue_t, skip, ends, fix, hin)


def body(streams, short_filter, skip, rates, residues):
    axes = ("ctx", "tp")
    devices = lax.axis_size("ctx") * lax.axis_size("tp")
    tok_rows, streams_count, width = streams.shape
    taps = short_filter.shape[0]
    modes = rates.shape[1]

    def shift(value, offset):
        pairs = [(j, j + offset) for j in range(devices - offset)]
        return lax.ppermute(value, axes, pairs)

    halo_rows = shift(streams[tok_rows - (taps - 1) :], 1).astype(jnp.float32)
    halo = jnp.transpose(halo_rows, (1, 0, 2))
    x = jnp.transpose(streams, (1, 0, 2))
    rate_t = rates.T
    residue_t = residues.T
    ends, local = run_state(x, jnp.zeros_like(halo), short_filter, rate_t)

    head = streams[: taps - 1].astype(jnp.float32)

    def head_gate(before):
        rows = jnp.concatenate([before, head], axis=0)
        gated = []
        for t in range(taps - 1):
            feat = short_filter[0] * rows[t + taps - 1]
            for tap in range(1, taps):
                feat = feat + short_filter[tap] * rows[t + taps - 1 - tap]
            gated.append((feat[1] * feat[2]).astype(jnp.bfloat16).astype(jnp.float32))
        return gated

    seg = tok_rows // SUB
    true_head = head_gate(halo_rows)
    zero_head = head_gate(jnp.zeros_like(halo_rows))
    local_fix = None
    ends_fix = None
    for t in range(taps - 1):
        delta = (true_head[t] - zero_head[t])[None, :]
        to_end = jnp.exp(-rate_t * float(tok_rows - 1 - t)) * delta
        to_seg = jnp.exp(-rate_t * float(seg - 1 - t)) * delta
        local_fix = to_end if local_fix is None else local_fix + to_end
        ends_fix = to_seg if ends_fix is None else ends_fix + to_seg
    local = local + local_fix

    def decay_pow(steps):
        return jnp.exp(-rate_t * float(tok_rows * steps))

    def gather_window(value, spacing, count):
        sent = value.astype(jnp.bfloat16)
        total = None
        for k in range(1, count + 1):
            if k * spacing >= devices:
                break
            term = decay_pow((k - 1) * spacing) * shift(sent, k * spacing).astype(jnp.float32)
            total = term if total is None else total + term
        return total

    first = min(FIRST_WINDOW, devices - 1)
    carried = gather_window(local, 1, first)
    window = first
    while window < devices - 1:
        count = min(-(-(devices - 1) // window) - 1, FIRST_WINDOW)
        carried = carried + decay_pow(window) * gather_window(carried, window, count)
        window *= count + 1

    return run_out(x, halo, short_filter, rate_t, residue_t, skip.reshape(1, width), ends, ends_fix, carried)


def solution(mesh):
    return jax.shard_map(
        body,
        mesh=mesh,
        in_specs=(P(("ctx", "tp"), None, None), P(), P(), P(), P()),
        out_specs=P(("ctx", "tp"), None),
        check_vma=False,
    )
```

```python
import jax
import jax.numpy as jnp
from jax import lax
from jax.experimental import pallas as pl
from jax.experimental.pallas import tpu as pltpu
from jax.sharding import PartitionSpec as P

LANES = 128
SUB = 8
BLOCK = 512
FIRST_WINDOW = 3
UNROLL = 8


def lane_slice(c):
    return pl.ds(pl.multiple_of(c * LANES, LANES), LANES)


def row(ref, index, lanes):
    return jnp.broadcast_to(ref[pl.ds(index, 1), lanes], (SUB, LANES))


def first_prev(xs, halo_ref, c, lanes, seg, taps, sub):
    prev = []
    for back in range(1, taps):
        per_stream = []
        for s in range(xs.shape[0]):
            rows = xs[s, c, pl.ds(seg - back, SUB, stride=seg), :]
            edge = jnp.broadcast_to(halo_ref[s, pl.ds(taps - 1 - back, 1), lanes], (SUB, LANES))
            per_stream.append(jnp.where(sub == 0, edge, pltpu.roll(rows, 1, 0)))
        prev.append(per_stream)
    return prev


def fill_filters(f_ref, fsc, lanes):
    streams_count = f_ref.shape[1]
    for tap in range(f_ref.shape[0]):
        for s in range(streams_count):
            fsc[tap * streams_count + s] = row(f_ref.at[tap], s, lanes)


def step_features(xs, fsc, c, seg, j, prev, first=0):
    streams_count = xs.shape[0]
    taps = len(prev) + 1
    now = [xs[s, c, pl.ds(j, SUB, stride=seg), :] if s >= first else prev[0][s] for s in range(streams_count)]
    feats = []
    for s in range(streams_count):
        if s < first:
            feats.append(None)
            continue
        acc = fsc[s] * now[s]
        for tap in range(1, taps):
            acc = acc + fsc[tap * streams_count + s] * prev[tap - 1][s]
        feats.append(acc)
    new_prev = [now] + prev[:-1]
    return feats, new_prev


def gate(feats):
    return (feats[1] * feats[2]).astype(jnp.bfloat16).astype(jnp.float32)


def state_kernel(x_ref, halo_ref, f_ref, a_ref, decay_ref, seg_ref, h_ref, xs, dsc, fsc):
    streams_count, rows, block = x_ref.shape
    taps = f_ref.shape[0]
    modes = a_ref.shape[0]
    seg = rows // SUB
    for c in range(block // LANES):
        xs[:, c] = x_ref[:, :, c * LANES : (c + 1) * LANES].astype(jnp.float32)
    sub = lax.broadcasted_iota(jnp.int32, (SUB, LANES), 0)

    def lane_group(c, carry):
        lanes = lane_slice(c)
        fill_filters(f_ref, fsc, lanes)
        for m in range(modes):
            dsc[m] = row(decay_ref, m, lanes)

        def step(j, state):
            prev, states = state
            feats, prev = step_features(xs, fsc, c, seg, j, prev, first=1)
            u = gate(feats)
            return prev, tuple(dsc[m] * states[m] + u for m in range(modes))

        zero = jnp.zeros((SUB, LANES), jnp.float32)
        init = (first_prev(xs, halo_ref, c, lanes, seg, taps, sub), (zero,) * modes)
        _, states = lax.fori_loop(0, seg, step, init, unroll=UNROLL)
        later = (SUB - 1 - sub).astype(jnp.float32) * float(seg)
        for m in range(modes):
            seg_ref[m, :, lanes] = states[m]
            weight = jnp.exp(-row(a_ref, m, lanes) * later)
            h_ref[pl.ds(m, 1), lanes] = jnp.sum(weight * states[m], axis=0, keepdims=True)
        return carry

    lax.fori_loop(0, block // LANES, lane_group, 0)


def out_kernel(
    x_ref, halo_ref, f_ref, a_ref, decay_ref, r_ref, skip_ref, seg_ref, fix_ref, hin_ref, o_ref, xs, ys, dsc, rsc, fsc
):
    streams_count, rows, block = x_ref.shape
    taps = f_ref.shape[0]
    modes = a_ref.shape[0]
    seg = rows // SUB
    for c in range(block // LANES):
        xs[:, c] = x_ref[:, :, c * LANES : (c + 1) * LANES].astype(jnp.float32)
    sub = lax.broadcasted_iota(jnp.int32, (SUB, LANES), 0)

    def lane_group(c, carry):
        lanes = lane_slice(c)
        fill_filters(f_ref, fsc, lanes)
        starts = []
        for m in range(modes):
            rate = row(a_ref, m, lanes)
            dsc[m] = row(decay_ref, m, lanes)
            rsc[m] = row(r_ref, m, lanes)
            ends = seg_ref[m, :, lanes] + jnp.where(sub == 0, row(fix_ref, m, lanes), 0.0)
            carried = jnp.where(sub >= 1, pltpu.roll(ends, 1, 0), 0.0)
            offset = 1
            while offset < SUB:
                factor = jnp.exp(-rate * float(seg * offset))
                carried = carried + jnp.where(sub >= offset, factor * pltpu.roll(carried, offset, 0), 0.0)
                offset *= 2
            lead = jnp.exp(-rate * (sub.astype(jnp.float32) * float(seg)))
            starts.append(carried + lead * row(hin_ref, m, lanes))
        skip_rows = row(skip_ref, 0, lanes)

        def step(j, state):
            prev, states = state
            feats, prev = step_features(xs, fsc, c, seg, j, prev)
            u = gate(feats)
            new = [dsc[m] * states[m] + u for m in range(modes)]
            terms = [rsc[m] * new[m] for m in range(modes)]
            while len(terms) > 1:
                paired = [terms[i] + terms[i + 1] for i in range(0, len(terms) - 1, 2)]
                terms = paired + terms[len(terms) - len(terms) % 2 :]
            conv = terms[0]
            y = (conv + skip_rows * u).astype(jnp.bfloat16).astype(jnp.float32)
            ys[c, pl.ds(j, SUB, stride=seg), :] = feats[0] * y
            return prev, tuple(new)

        init = (first_prev(xs, halo_ref, c, lanes, seg, taps, sub), tuple(starts))
        lax.fori_loop(0, seg, step, init, unroll=UNROLL)
        return carry

    lax.fori_loop(0, block // LANES, lane_group, 0)
    for c in range(block // LANES):
        o_ref[:, c * LANES : (c + 1) * LANES] = ys[c].astype(o_ref.dtype)


def run_state(x, halo, f, rate_t, decay):
    streams_count, rows, width = x.shape
    taps = f.shape[0]
    modes = rate_t.shape[0]
    return pl.pallas_call(
        state_kernel,
        grid=(width // BLOCK,),
        in_specs=[
            pl.BlockSpec((streams_count, rows, BLOCK), lambda i: (0, 0, i)),
            pl.BlockSpec((streams_count, taps - 1, BLOCK), lambda i: (0, 0, i)),
            pl.BlockSpec((taps, streams_count, BLOCK), lambda i: (0, 0, i)),
            pl.BlockSpec((modes, BLOCK), lambda i: (0, i)),
            pl.BlockSpec((modes, BLOCK), lambda i: (0, i)),
        ],
        out_specs=[
            pl.BlockSpec((modes, SUB, BLOCK), lambda i: (0, 0, i)),
            pl.BlockSpec((modes, BLOCK), lambda i: (0, i)),
        ],
        out_shape=[
            jax.ShapeDtypeStruct((modes, SUB, width), jnp.float32),
            jax.ShapeDtypeStruct((modes, width), jnp.float32),
        ],
        scratch_shapes=[
            pltpu.VMEM((streams_count, BLOCK // LANES, rows, LANES), jnp.float32),
            pltpu.VMEM((modes, SUB, LANES), jnp.float32),
            pltpu.VMEM((taps * streams_count, SUB, LANES), jnp.float32),
        ],
    )(x, halo, f, rate_t, decay)


def run_out(x, halo, f, rate_t, decay, residue_t, skip, ends, fix, hin):
    streams_count, rows, width = x.shape
    taps = f.shape[0]
    modes = rate_t.shape[0]
    return pl.pallas_call(
        out_kernel,
        grid=(width // BLOCK,),
        in_specs=[
            pl.BlockSpec((streams_count, rows, BLOCK), lambda i: (0, 0, i)),
            pl.BlockSpec((streams_count, taps - 1, BLOCK), lambda i: (0, 0, i)),
            pl.BlockSpec((taps, streams_count, BLOCK), lambda i: (0, 0, i)),
            pl.BlockSpec((modes, BLOCK), lambda i: (0, i)),
            pl.BlockSpec((modes, BLOCK), lambda i: (0, i)),
            pl.BlockSpec((modes, BLOCK), lambda i: (0, i)),
            pl.BlockSpec((1, BLOCK), lambda i: (0, i)),
            pl.BlockSpec((modes, SUB, BLOCK), lambda i: (0, 0, i)),
            pl.BlockSpec((modes, BLOCK), lambda i: (0, i)),
            pl.BlockSpec((modes, BLOCK), lambda i: (0, i)),
        ],
        out_specs=pl.BlockSpec((rows, BLOCK), lambda i: (0, i)),
        out_shape=jax.ShapeDtypeStruct((rows, width), jnp.bfloat16),
        scratch_shapes=[
            pltpu.VMEM((streams_count, BLOCK // LANES, rows, LANES), jnp.float32),
            pltpu.VMEM((BLOCK // LANES, rows, LANES), jnp.float32),
            pltpu.VMEM((modes, SUB, LANES), jnp.float32),
            pltpu.VMEM((modes, SUB, LANES), jnp.float32),
            pltpu.VMEM((taps * streams_count, SUB, LANES), jnp.float32),
        ],
    )(x, halo, f, rate_t, decay, residue_t, skip, ends, fix, hin)


def body(streams, short_filter, skip, rates, residues):
    axes = ("ctx", "tp")
    devices = lax.axis_size("ctx") * lax.axis_size("tp")
    tok_rows, streams_count, width = streams.shape
    taps = short_filter.shape[0]
    modes = rates.shape[1]

    def shift(value, offset):
        pairs = [(j, j + offset) for j in range(devices - offset)]
        return lax.ppermute(value, axes, pairs)

    halo_rows = shift(streams[tok_rows - (taps - 1) :], 1).astype(jnp.float32)
    halo = jnp.transpose(halo_rows, (1, 0, 2))
    x = jnp.transpose(streams, (1, 0, 2))
    rate_t = rates.T
    residue_t = residues.T
    decay = jnp.exp(-rate_t)
    ends, local = run_state(x, jnp.zeros_like(halo), short_filter, rate_t, decay)

    head = streams[: taps - 1].astype(jnp.float32)

    def head_gate(before):
        rows = jnp.concatenate([before, head], axis=0)
        gated = []
        for t in range(taps - 1):
            feat = short_filter[0] * rows[t + taps - 1]
            for tap in range(1, taps):
                feat = feat + short_filter[tap] * rows[t + taps - 1 - tap]
            gated.append((feat[1] * feat[2]).astype(jnp.bfloat16).astype(jnp.float32))
        return gated

    seg = tok_rows // SUB
    true_head = head_gate(halo_rows)
    zero_head = head_gate(jnp.zeros_like(halo_rows))
    local_fix = None
    ends_fix = None
    for t in range(taps - 1):
        delta = (true_head[t] - zero_head[t])[None, :]
        to_end = jnp.exp(-rate_t * float(tok_rows - 1 - t)) * delta
        to_seg = jnp.exp(-rate_t * float(seg - 1 - t)) * delta
        local_fix = to_end if local_fix is None else local_fix + to_end
        ends_fix = to_seg if ends_fix is None else ends_fix + to_seg
    local = local + local_fix

    def decay_pow(steps):
        return jnp.exp(-rate_t * float(tok_rows * steps))

    def gather_window(value, spacing, count):
        sent = value.astype(jnp.bfloat16)
        total = None
        for k in range(1, count + 1):
            if k * spacing >= devices:
                break
            term = decay_pow((k - 1) * spacing) * shift(sent, k * spacing).astype(jnp.float32)
            total = term if total is None else total + term
        return total

    first = min(FIRST_WINDOW, devices - 1)
    carried = gather_window(local, 1, first)
    window = first
    while window < devices - 1:
        count = min(-(-(devices - 1) // window) - 1, FIRST_WINDOW)
        carried = carried + decay_pow(window) * gather_window(carried, window, count)
        window *= count + 1

    return run_out(x, halo, short_filter, rate_t, decay, residue_t, skip.reshape(1, width), ends, ends_fix, carried)


def solution(mesh):
    return jax.shard_map(
        body,
        mesh=mesh,
        in_specs=(P(("ctx", "tp"), None, None), P(), P(), P(), P()),
        out_specs=P(("ctx", "tp"), None),
        check_vma=False,
    )
```

```python
import jax
import jax.numpy as jnp
from jax import lax
from jax.experimental import pallas as pl
from jax.experimental.pallas import tpu as pltpu
from jax.sharding import PartitionSpec as P

LANES = 128
SUB = 8
BLOCK = 1024
FIRST_WINDOW = 3
UNROLL = 8


def lane_slice(c):
    return pl.ds(pl.multiple_of(c * LANES, LANES), LANES)


def row(ref, index, lanes):
    return jnp.broadcast_to(ref[pl.ds(index, 1), lanes], (SUB, LANES))


def first_prev(xs, halo_ref, c, lanes, seg, taps, sub):
    prev = []
    for back in range(1, taps):
        per_stream = []
        for s in range(xs.shape[0]):
            rows = xs[s, c, pl.ds(seg - back, SUB, stride=seg), :]
            edge = jnp.broadcast_to(halo_ref[s, pl.ds(taps - 1 - back, 1), lanes], (SUB, LANES))
            per_stream.append(jnp.where(sub == 0, edge, pltpu.roll(rows, 1, 0)))
        prev.append(per_stream)
    return prev


def fill_filters(f_ref, fsc, lanes):
    streams_count = f_ref.shape[1]
    for tap in range(f_ref.shape[0]):
        for s in range(streams_count):
            fsc[tap * streams_count + s] = row(f_ref.at[tap], s, lanes)


def step_features(xs, fsc, c, seg, j, prev):
    streams_count = xs.shape[0]
    taps = len(prev) + 1
    now = [xs[s, c, pl.ds(j, SUB, stride=seg), :] for s in range(streams_count)]
    feats = []
    for s in range(streams_count):
        acc = fsc[s] * now[s]
        for tap in range(1, taps):
            acc = acc + fsc[tap * streams_count + s] * prev[tap - 1][s]
        feats.append(acc)
    new_prev = [now] + prev[:-1]
    return feats, new_prev


def gate(feats):
    return (feats[1] * feats[2]).astype(jnp.bfloat16).astype(jnp.float32)


def state_kernel(x_ref, halo_ref, f_ref, a_ref, seg_ref, h_ref, xs, dsc, fsc):
    streams_count, rows, block = x_ref.shape
    taps = f_ref.shape[0]
    modes = a_ref.shape[0]
    seg = rows // SUB
    for c in range(block // LANES):
        xs[:, c] = x_ref[:, :, c * LANES : (c + 1) * LANES].astype(jnp.float32)
    sub = lax.broadcasted_iota(jnp.int32, (SUB, LANES), 0)

    def lane_group(c, carry):
        lanes = lane_slice(c)
        fill_filters(f_ref, fsc, lanes)
        for m in range(modes):
            dsc[m] = jnp.exp(-row(a_ref, m, lanes))

        def step(j, state):
            prev, states = state
            feats, prev = step_features(xs, fsc, c, seg, j, prev)
            u = gate(feats)
            return prev, tuple(dsc[m] * states[m] + u for m in range(modes))

        zero = jnp.zeros((SUB, LANES), jnp.float32)
        init = (first_prev(xs, halo_ref, c, lanes, seg, taps, sub), (zero,) * modes)
        _, states = lax.fori_loop(0, seg, step, init, unroll=UNROLL)
        later = (SUB - 1 - sub).astype(jnp.float32) * float(seg)
        for m in range(modes):
            seg_ref[m, :, lanes] = states[m]
            weight = jnp.exp(-row(a_ref, m, lanes) * later)
            h_ref[pl.ds(m, 1), lanes] = jnp.sum(weight * states[m], axis=0, keepdims=True)
        return carry

    lax.fori_loop(0, block // LANES, lane_group, 0)


def out_kernel(
    x_ref, halo_ref, f_ref, a_ref, r_ref, skip_ref, seg_ref, fix_ref, hin_ref, o_ref, xs, ys, dsc, rsc, fsc
):
    streams_count, rows, block = x_ref.shape
    taps = f_ref.shape[0]
    modes = a_ref.shape[0]
    seg = rows // SUB
    for c in range(block // LANES):
        xs[:, c] = x_ref[:, :, c * LANES : (c + 1) * LANES].astype(jnp.float32)
    sub = lax.broadcasted_iota(jnp.int32, (SUB, LANES), 0)

    def lane_group(c, carry):
        lanes = lane_slice(c)
        fill_filters(f_ref, fsc, lanes)
        starts = []
        for m in range(modes):
            rate = row(a_ref, m, lanes)
            dsc[m] = jnp.exp(-rate)
            rsc[m] = row(r_ref, m, lanes)
            ends = seg_ref[m, :, lanes] + jnp.where(sub == 0, row(fix_ref, m, lanes), 0.0)
            carried = jnp.where(sub >= 1, pltpu.roll(ends, 1, 0), 0.0)
            offset = 1
            while offset < SUB:
                factor = jnp.exp(-rate * float(seg * offset))
                carried = carried + jnp.where(sub >= offset, factor * pltpu.roll(carried, offset, 0), 0.0)
                offset *= 2
            lead = jnp.exp(-rate * (sub.astype(jnp.float32) * float(seg)))
            starts.append(carried + lead * row(hin_ref, m, lanes))
        skip_rows = row(skip_ref, 0, lanes)

        def step(j, state):
            prev, states = state
            feats, prev = step_features(xs, fsc, c, seg, j, prev)
            u = gate(feats)
            new = [dsc[m] * states[m] + u for m in range(modes)]
            terms = [rsc[m] * new[m] for m in range(modes)]
            while len(terms) > 1:
                paired = [terms[i] + terms[i + 1] for i in range(0, len(terms) - 1, 2)]
                terms = paired + terms[len(terms) - len(terms) % 2 :]
            conv = terms[0]
            y = (conv + skip_rows * u).astype(jnp.bfloat16).astype(jnp.float32)
            ys[c, pl.ds(j, SUB, stride=seg), :] = feats[0] * y
            return prev, tuple(new)

        init = (first_prev(xs, halo_ref, c, lanes, seg, taps, sub), tuple(starts))
        lax.fori_loop(0, seg, step, init, unroll=UNROLL)
        return carry

    lax.fori_loop(0, block // LANES, lane_group, 0)
    for c in range(block // LANES):
        o_ref[:, c * LANES : (c + 1) * LANES] = ys[c].astype(o_ref.dtype)


def run_state(x, halo, f, rate_t):
    streams_count, rows, width = x.shape
    taps = f.shape[0]
    modes = rate_t.shape[0]
    return pl.pallas_call(
        state_kernel,
        grid=(width // BLOCK,),
        in_specs=[
            pl.BlockSpec((streams_count, rows, BLOCK), lambda i: (0, 0, i)),
            pl.BlockSpec((streams_count, taps - 1, BLOCK), lambda i: (0, 0, i)),
            pl.BlockSpec((taps, streams_count, BLOCK), lambda i: (0, 0, i)),
            pl.BlockSpec((modes, BLOCK), lambda i: (0, i)),
        ],
        out_specs=[
            pl.BlockSpec((modes, SUB, BLOCK), lambda i: (0, 0, i)),
            pl.BlockSpec((modes, BLOCK), lambda i: (0, i)),
        ],
        out_shape=[
            jax.ShapeDtypeStruct((modes, SUB, width), jnp.float32),
            jax.ShapeDtypeStruct((modes, width), jnp.float32),
        ],
        scratch_shapes=[
            pltpu.VMEM((streams_count, BLOCK // LANES, rows, LANES), jnp.float32),
            pltpu.VMEM((modes, SUB, LANES), jnp.float32),
            pltpu.VMEM((taps * streams_count, SUB, LANES), jnp.float32),
        ],
    )(x, halo, f, rate_t)


def run_out(x, halo, f, rate_t, residue_t, skip, ends, fix, hin):
    streams_count, rows, width = x.shape
    taps = f.shape[0]
    modes = rate_t.shape[0]
    return pl.pallas_call(
        out_kernel,
        grid=(width // BLOCK,),
        in_specs=[
            pl.BlockSpec((streams_count, rows, BLOCK), lambda i: (0, 0, i)),
            pl.BlockSpec((streams_count, taps - 1, BLOCK), lambda i: (0, 0, i)),
            pl.BlockSpec((taps, streams_count, BLOCK), lambda i: (0, 0, i)),
            pl.BlockSpec((modes, BLOCK), lambda i: (0, i)),
            pl.BlockSpec((modes, BLOCK), lambda i: (0, i)),
            pl.BlockSpec((1, BLOCK), lambda i: (0, i)),
            pl.BlockSpec((modes, SUB, BLOCK), lambda i: (0, 0, i)),
            pl.BlockSpec((modes, BLOCK), lambda i: (0, i)),
            pl.BlockSpec((modes, BLOCK), lambda i: (0, i)),
        ],
        out_specs=pl.BlockSpec((rows, BLOCK), lambda i: (0, i)),
        out_shape=jax.ShapeDtypeStruct((rows, width), jnp.bfloat16),
        scratch_shapes=[
            pltpu.VMEM((streams_count, BLOCK // LANES, rows, LANES), jnp.float32),
            pltpu.VMEM((BLOCK // LANES, rows, LANES), jnp.float32),
            pltpu.VMEM((modes, SUB, LANES), jnp.float32),
            pltpu.VMEM((modes, SUB, LANES), jnp.float32),
            pltpu.VMEM((taps * streams_count, SUB, LANES), jnp.float32),
        ],
    )(x, halo, f, rate_t, residue_t, skip, ends, fix, hin)


def body(streams, short_filter, skip, rates, residues):
    axes = ("ctx", "tp")
    devices = lax.axis_size("ctx") * lax.axis_size("tp")
    tok_rows, streams_count, width = streams.shape
    taps = short_filter.shape[0]
    modes = rates.shape[1]

    def shift(value, offset):
        pairs = [(j, j + offset) for j in range(devices - offset)]
        return lax.ppermute(value, axes, pairs)

    halo_rows = shift(streams[tok_rows - (taps - 1) :], 1).astype(jnp.float32)
    halo = jnp.transpose(halo_rows, (1, 0, 2))
    x = jnp.transpose(streams, (1, 0, 2))
    rate_t = rates.T
    residue_t = residues.T
    ends, local = run_state(x, jnp.zeros_like(halo), short_filter, rate_t)

    head = streams[: taps - 1].astype(jnp.float32)

    def head_gate(before):
        rows = jnp.concatenate([before, head], axis=0)
        gated = []
        for t in range(taps - 1):
            feat = short_filter[0] * rows[t + taps - 1]
            for tap in range(1, taps):
                feat = feat + short_filter[tap] * rows[t + taps - 1 - tap]
            gated.append((feat[1] * feat[2]).astype(jnp.bfloat16).astype(jnp.float32))
        return gated

    seg = tok_rows // SUB
    true_head = head_gate(halo_rows)
    zero_head = head_gate(jnp.zeros_like(halo_rows))
    local_fix = None
    ends_fix = None
    for t in range(taps - 1):
        delta = (true_head[t] - zero_head[t])[None, :]
        to_end = jnp.exp(-rate_t * float(tok_rows - 1 - t)) * delta
        to_seg = jnp.exp(-rate_t * float(seg - 1 - t)) * delta
        local_fix = to_end if local_fix is None else local_fix + to_end
        ends_fix = to_seg if ends_fix is None else ends_fix + to_seg
    local = local + local_fix

    def decay_pow(steps):
        return jnp.exp(-rate_t * float(tok_rows * steps))

    def gather_window(value, spacing, count):
        sent = value.astype(jnp.bfloat16)
        total = None
        for k in range(1, count + 1):
            if k * spacing >= devices:
                break
            term = decay_pow((k - 1) * spacing) * shift(sent, k * spacing).astype(jnp.float32)
            total = term if total is None else total + term
        return total

    first = min(FIRST_WINDOW, devices - 1)
    carried = gather_window(local, 1, first)
    window = first
    while window < devices - 1:
        count = min(-(-(devices - 1) // window) - 1, FIRST_WINDOW)
        carried = carried + decay_pow(window) * gather_window(carried, window, count)
        window *= count + 1

    return run_out(x, halo, short_filter, rate_t, residue_t, skip.reshape(1, width), ends, ends_fix, carried)


def solution(mesh):
    return jax.shard_map(
        body,
        mesh=mesh,
        in_specs=(P(("ctx", "tp"), None, None), P(), P(), P(), P()),
        out_specs=P(("ctx", "tp"), None),
        check_vma=False,
    )
```

```python
import jax
import jax.numpy as jnp
from jax import lax
from jax.experimental import pallas as pl
from jax.experimental.pallas import tpu as pltpu
from jax.sharding import PartitionSpec as P

LANES = 128
SUB = 8
BLOCK = 2048
FIRST_WINDOW = 3
UNROLL = 8


def lane_slice(c):
    return pl.ds(pl.multiple_of(c * LANES, LANES), LANES)


def row(ref, index, lanes):
    return jnp.broadcast_to(ref[pl.ds(index, 1), lanes], (SUB, LANES))


def first_prev(xs, halo_ref, c, lanes, seg, taps, sub):
    prev = []
    for back in range(1, taps):
        per_stream = []
        for s in range(xs.shape[0]):
            rows = xs[s, c, pl.ds(seg - back, SUB, stride=seg), :]
            edge = jnp.broadcast_to(halo_ref[s, pl.ds(taps - 1 - back, 1), lanes], (SUB, LANES))
            per_stream.append(jnp.where(sub == 0, edge, pltpu.roll(rows, 1, 0)))
        prev.append(per_stream)
    return prev


def fill_filters(f_ref, fsc, lanes):
    streams_count = f_ref.shape[1]
    for tap in range(f_ref.shape[0]):
        for s in range(streams_count):
            fsc[tap * streams_count + s] = row(f_ref.at[tap], s, lanes)


def step_features(xs, fsc, c, seg, j, prev):
    streams_count = xs.shape[0]
    taps = len(prev) + 1
    now = [xs[s, c, pl.ds(j, SUB, stride=seg), :] for s in range(streams_count)]
    feats = []
    for s in range(streams_count):
        acc = fsc[s] * now[s]
        for tap in range(1, taps):
            acc = acc + fsc[tap * streams_count + s] * prev[tap - 1][s]
        feats.append(acc)
    new_prev = [now] + prev[:-1]
    return feats, new_prev


def gate(feats):
    return (feats[1] * feats[2]).astype(jnp.bfloat16).astype(jnp.float32)


def state_kernel(x_ref, halo_ref, f_ref, a_ref, seg_ref, h_ref, xs, dsc, fsc):
    streams_count, rows, block = x_ref.shape
    taps = f_ref.shape[0]
    modes = a_ref.shape[0]
    seg = rows // SUB
    for c in range(block // LANES):
        xs[:, c] = x_ref[:, :, c * LANES : (c + 1) * LANES].astype(jnp.float32)
    sub = lax.broadcasted_iota(jnp.int32, (SUB, LANES), 0)

    def lane_group(c, carry):
        lanes = lane_slice(c)
        fill_filters(f_ref, fsc, lanes)
        for m in range(modes):
            dsc[m] = jnp.exp(-row(a_ref, m, lanes))

        def step(j, state):
            prev, states = state
            feats, prev = step_features(xs, fsc, c, seg, j, prev)
            u = gate(feats)
            return prev, tuple(dsc[m] * states[m] + u for m in range(modes))

        zero = jnp.zeros((SUB, LANES), jnp.float32)
        init = (first_prev(xs, halo_ref, c, lanes, seg, taps, sub), (zero,) * modes)
        _, states = lax.fori_loop(0, seg, step, init, unroll=UNROLL)
        later = (SUB - 1 - sub).astype(jnp.float32) * float(seg)
        for m in range(modes):
            seg_ref[m, :, lanes] = states[m]
            weight = jnp.exp(-row(a_ref, m, lanes) * later)
            h_ref[pl.ds(m, 1), lanes] = jnp.sum(weight * states[m], axis=0, keepdims=True)
        return carry

    lax.fori_loop(0, block // LANES, lane_group, 0)


def out_kernel(
    x_ref, halo_ref, f_ref, a_ref, r_ref, skip_ref, seg_ref, fix_ref, hin_ref, o_ref, xs, ys, dsc, rsc, fsc
):
    streams_count, rows, block = x_ref.shape
    taps = f_ref.shape[0]
    modes = a_ref.shape[0]
    seg = rows // SUB
    for c in range(block // LANES):
        xs[:, c] = x_ref[:, :, c * LANES : (c + 1) * LANES].astype(jnp.float32)
    sub = lax.broadcasted_iota(jnp.int32, (SUB, LANES), 0)

    def lane_group(c, carry):
        lanes = lane_slice(c)
        fill_filters(f_ref, fsc, lanes)
        starts = []
        for m in range(modes):
            rate = row(a_ref, m, lanes)
            dsc[m] = jnp.exp(-rate)
            rsc[m] = row(r_ref, m, lanes)
            ends = seg_ref[m, :, lanes] + jnp.where(sub == 0, row(fix_ref, m, lanes), 0.0)
            carried = jnp.where(sub >= 1, pltpu.roll(ends, 1, 0), 0.0)
            offset = 1
            while offset < SUB:
                factor = jnp.exp(-rate * float(seg * offset))
                carried = carried + jnp.where(sub >= offset, factor * pltpu.roll(carried, offset, 0), 0.0)
                offset *= 2
            lead = jnp.exp(-rate * (sub.astype(jnp.float32) * float(seg)))
            starts.append(carried + lead * row(hin_ref, m, lanes))
        skip_rows = row(skip_ref, 0, lanes)

        def step(j, state):
            prev, states = state
            feats, prev = step_features(xs, fsc, c, seg, j, prev)
            u = gate(feats)
            new = [dsc[m] * states[m] + u for m in range(modes)]
            terms = [rsc[m] * new[m] for m in range(modes)]
            while len(terms) > 1:
                paired = [terms[i] + terms[i + 1] for i in range(0, len(terms) - 1, 2)]
                terms = paired + terms[len(terms) - len(terms) % 2 :]
            conv = terms[0]
            y = (conv + skip_rows * u).astype(jnp.bfloat16).astype(jnp.float32)
            ys[c, pl.ds(j, SUB, stride=seg), :] = feats[0] * y
            return prev, tuple(new)

        init = (first_prev(xs, halo_ref, c, lanes, seg, taps, sub), tuple(starts))
        lax.fori_loop(0, seg, step, init, unroll=UNROLL)
        return carry

    lax.fori_loop(0, block // LANES, lane_group, 0)
    for c in range(block // LANES):
        o_ref[:, c * LANES : (c + 1) * LANES] = ys[c].astype(o_ref.dtype)


def run_state(x, halo, f, rate_t):
    streams_count, rows, width = x.shape
    taps = f.shape[0]
    modes = rate_t.shape[0]
    return pl.pallas_call(
        state_kernel,
        grid=(width // BLOCK,),
        in_specs=[
            pl.BlockSpec((streams_count, rows, BLOCK), lambda i: (0, 0, i)),
            pl.BlockSpec((streams_count, taps - 1, BLOCK), lambda i: (0, 0, i)),
            pl.BlockSpec((taps, streams_count, BLOCK), lambda i: (0, 0, i)),
            pl.BlockSpec((modes, BLOCK), lambda i: (0, i)),
        ],
        out_specs=[
            pl.BlockSpec((modes, SUB, BLOCK), lambda i: (0, 0, i)),
            pl.BlockSpec((modes, BLOCK), lambda i: (0, i)),
        ],
        out_shape=[
            jax.ShapeDtypeStruct((modes, SUB, width), jnp.float32),
            jax.ShapeDtypeStruct((modes, width), jnp.float32),
        ],
        scratch_shapes=[
            pltpu.VMEM((streams_count, BLOCK // LANES, rows, LANES), jnp.float32),
            pltpu.VMEM((modes, SUB, LANES), jnp.float32),
            pltpu.VMEM((taps * streams_count, SUB, LANES), jnp.float32),
        ],
    )(x, halo, f, rate_t)


def run_out(x, halo, f, rate_t, residue_t, skip, ends, fix, hin):
    streams_count, rows, width = x.shape
    taps = f.shape[0]
    modes = rate_t.shape[0]
    return pl.pallas_call(
        out_kernel,
        grid=(width // BLOCK,),
        in_specs=[
            pl.BlockSpec((streams_count, rows, BLOCK), lambda i: (0, 0, i)),
            pl.BlockSpec((streams_count, taps - 1, BLOCK), lambda i: (0, 0, i)),
            pl.BlockSpec((taps, streams_count, BLOCK), lambda i: (0, 0, i)),
            pl.BlockSpec((modes, BLOCK), lambda i: (0, i)),
            pl.BlockSpec((modes, BLOCK), lambda i: (0, i)),
            pl.BlockSpec((1, BLOCK), lambda i: (0, i)),
            pl.BlockSpec((modes, SUB, BLOCK), lambda i: (0, 0, i)),
            pl.BlockSpec((modes, BLOCK), lambda i: (0, i)),
            pl.BlockSpec((modes, BLOCK), lambda i: (0, i)),
        ],
        out_specs=pl.BlockSpec((rows, BLOCK), lambda i: (0, i)),
        out_shape=jax.ShapeDtypeStruct((rows, width), jnp.bfloat16),
        scratch_shapes=[
            pltpu.VMEM((streams_count, BLOCK // LANES, rows, LANES), jnp.float32),
            pltpu.VMEM((BLOCK // LANES, rows, LANES), jnp.float32),
            pltpu.VMEM((modes, SUB, LANES), jnp.float32),
            pltpu.VMEM((modes, SUB, LANES), jnp.float32),
            pltpu.VMEM((taps * streams_count, SUB, LANES), jnp.float32),
        ],
    )(x, halo, f, rate_t, residue_t, skip, ends, fix, hin)


def body(streams, short_filter, skip, rates, residues):
    axes = ("ctx", "tp")
    devices = lax.axis_size("ctx") * lax.axis_size("tp")
    tok_rows, streams_count, width = streams.shape
    taps = short_filter.shape[0]
    modes = rates.shape[1]

    def shift(value, offset):
        pairs = [(j, j + offset) for j in range(devices - offset)]
        return lax.ppermute(value, axes, pairs)

    halo_rows = shift(streams[tok_rows - (taps - 1) :], 1).astype(jnp.float32)
    halo = jnp.transpose(halo_rows, (1, 0, 2))
    x = jnp.transpose(streams, (1, 0, 2))
    rate_t = rates.T
    residue_t = residues.T
    ends, local = run_state(x, jnp.zeros_like(halo), short_filter, rate_t)

    head = streams[: taps - 1].astype(jnp.float32)

    def head_gate(before):
        rows = jnp.concatenate([before, head], axis=0)
        gated = []
        for t in range(taps - 1):
            feat = short_filter[0] * rows[t + taps - 1]
            for tap in range(1, taps):
                feat = feat + short_filter[tap] * rows[t + taps - 1 - tap]
            gated.append((feat[1] * feat[2]).astype(jnp.bfloat16).astype(jnp.float32))
        return gated

    seg = tok_rows // SUB
    true_head = head_gate(halo_rows)
    zero_head = head_gate(jnp.zeros_like(halo_rows))
    local_fix = None
    ends_fix = None
    for t in range(taps - 1):
        delta = (true_head[t] - zero_head[t])[None, :]
        to_end = jnp.exp(-rate_t * float(tok_rows - 1 - t)) * delta
        to_seg = jnp.exp(-rate_t * float(seg - 1 - t)) * delta
        local_fix = to_end if local_fix is None else local_fix + to_end
        ends_fix = to_seg if ends_fix is None else ends_fix + to_seg
    local = local + local_fix

    def decay_pow(steps):
        return jnp.exp(-rate_t * float(tok_rows * steps))

    def gather_window(value, spacing, count):
        sent = value.astype(jnp.bfloat16)
        total = None
        for k in range(1, count + 1):
            if k * spacing >= devices:
                break
            term = decay_pow((k - 1) * spacing) * shift(sent, k * spacing).astype(jnp.float32)
            total = term if total is None else total + term
        return total

    first = min(FIRST_WINDOW, devices - 1)
    carried = gather_window(local, 1, first)
    window = first
    while window < devices - 1:
        count = min(-(-(devices - 1) // window) - 1, FIRST_WINDOW)
        carried = carried + decay_pow(window) * gather_window(carried, window, count)
        window *= count + 1

    return run_out(x, halo, short_filter, rate_t, residue_t, skip.reshape(1, width), ends, ends_fix, carried)


def solution(mesh):
    return jax.shard_map(
        body,
        mesh=mesh,
        in_specs=(P(("ctx", "tp"), None, None), P(), P(), P(), P()),
        out_specs=P(("ctx", "tp"), None),
        check_vma=False,
    )
```

```python
import jax
import jax.numpy as jnp
from jax import lax
from jax.experimental import pallas as pl
from jax.experimental.pallas import tpu as pltpu
from jax.sharding import PartitionSpec as P

LANES = 128
SUB = 8
BLOCK = 1024
FIRST_WINDOW = 3
UNROLL = 8


def lane_slice(c):
    return pl.ds(pl.multiple_of(c * LANES, LANES), LANES)


def row(ref, index, lanes):
    return jnp.broadcast_to(ref[pl.ds(index, 1), lanes], (SUB, LANES))


def first_prev(xs, halo_ref, c, lanes, seg, taps, sub):
    prev = []
    for back in range(1, taps):
        per_stream = []
        for s in range(xs.shape[0]):
            rows = xs[s, c, pl.ds(seg - back, SUB, stride=seg), :]
            edge = jnp.broadcast_to(halo_ref[s, pl.ds(taps - 1 - back, 1), lanes], (SUB, LANES))
            per_stream.append(jnp.where(sub == 0, edge, pltpu.roll(rows, 1, 0)))
        prev.append(per_stream)
    return prev


def fill_filters(f_ref, fsc, lanes):
    streams_count = f_ref.shape[1]
    for tap in range(f_ref.shape[0]):
        for s in range(streams_count):
            fsc[tap * streams_count + s] = row(f_ref.at[tap], s, lanes)


def step_features(xs, fsc, c, seg, j, prev):
    streams_count = xs.shape[0]
    taps = len(prev) + 1
    now = [xs[s, c, pl.ds(j, SUB, stride=seg), :] for s in range(streams_count)]
    feats = []
    for s in range(streams_count):
        acc = fsc[s] * now[s]
        for tap in range(1, taps):
            acc = acc + fsc[tap * streams_count + s] * prev[tap - 1][s]
        feats.append(acc)
    new_prev = [now] + prev[:-1]
    return feats, new_prev


def gate(feats):
    return (feats[1] * feats[2]).astype(jnp.bfloat16).astype(jnp.float32)


def state_kernel(x_ref, halo_ref, f_ref, a_ref, seg_ref, h_ref, xs, dsc, fsc):
    streams_count, rows, block = x_ref.shape
    taps = f_ref.shape[0]
    modes = a_ref.shape[0]
    seg = rows // SUB
    for c in range(block // LANES):
        xs[:, c] = x_ref[:, :, c * LANES : (c + 1) * LANES].astype(jnp.float32)
    sub = lax.broadcasted_iota(jnp.int32, (SUB, LANES), 0)

    def lane_group(c, carry):
        lanes = lane_slice(c)
        fill_filters(f_ref, fsc, lanes)
        for m in range(modes):
            dsc[m] = jnp.exp(-row(a_ref, m, lanes))

        def step(j, state):
            prev, states = state
            feats, prev = step_features(xs, fsc, c, seg, j, prev)
            u = gate(feats)
            return prev, tuple(dsc[m] * states[m] + u for m in range(modes))

        zero = jnp.zeros((SUB, LANES), jnp.float32)
        init = (first_prev(xs, halo_ref, c, lanes, seg, taps, sub), (zero,) * modes)
        _, states = lax.fori_loop(0, seg, step, init, unroll=UNROLL)
        later = (SUB - 1 - sub).astype(jnp.float32) * float(seg)
        for m in range(modes):
            seg_ref[m, :, lanes] = states[m]
            weight = jnp.exp(-row(a_ref, m, lanes) * later)
            h_ref[pl.ds(m, 1), lanes] = jnp.sum(weight * states[m], axis=0, keepdims=True)
        return carry

    lax.fori_loop(0, block // LANES, lane_group, 0)


def out_kernel(
    x_ref, halo_ref, f_ref, a_ref, r_ref, skip_ref, seg_ref, fix_ref, hin_ref, o_ref, xs, ys, dsc, rsc, fsc
):
    streams_count, rows, block = x_ref.shape
    taps = f_ref.shape[0]
    modes = a_ref.shape[0]
    seg = rows // SUB
    for c in range(block // LANES):
        xs[:, c] = x_ref[:, :, c * LANES : (c + 1) * LANES].astype(jnp.float32)
    sub = lax.broadcasted_iota(jnp.int32, (SUB, LANES), 0)

    def lane_group(c, carry):
        lanes = lane_slice(c)
        fill_filters(f_ref, fsc, lanes)
        starts = []
        for m in range(modes):
            rate = row(a_ref, m, lanes)
            dsc[m] = jnp.exp(-rate)
            rsc[m] = row(r_ref, m, lanes)
            ends = seg_ref[m, :, lanes] + jnp.where(sub == 0, row(fix_ref, m, lanes), 0.0)
            carried = jnp.where(sub >= 1, pltpu.roll(ends, 1, 0), 0.0)
            offset = 1
            while offset < SUB:
                factor = jnp.exp(-rate * float(seg * offset))
                carried = carried + jnp.where(sub >= offset, factor * pltpu.roll(carried, offset, 0), 0.0)
                offset *= 2
            lead = jnp.exp(-rate * (sub.astype(jnp.float32) * float(seg)))
            starts.append(carried + lead * row(hin_ref, m, lanes))
        skip_rows = row(skip_ref, 0, lanes)

        def step(j, state):
            prev, states = state
            feats, prev = step_features(xs, fsc, c, seg, j, prev)
            u = gate(feats)
            new = [dsc[m] * states[m] + u for m in range(modes)]
            terms = [rsc[m] * new[m] for m in range(modes)]
            while len(terms) > 1:
                paired = [terms[i] + terms[i + 1] for i in range(0, len(terms) - 1, 2)]
                terms = paired + terms[len(terms) - len(terms) % 2 :]
            conv = terms[0]
            y = (conv + skip_rows * u).astype(jnp.bfloat16).astype(jnp.float32)
            ys[c, pl.ds(j, SUB, stride=seg), :] = feats[0] * y
            return prev, tuple(new)

        init = (first_prev(xs, halo_ref, c, lanes, seg, taps, sub), tuple(starts))
        lax.fori_loop(0, seg, step, init, unroll=UNROLL)
        return carry

    lax.fori_loop(0, block // LANES, lane_group, 0)
    for c in range(block // LANES):
        o_ref[:, c * LANES : (c + 1) * LANES] = ys[c].astype(o_ref.dtype)


def run_state(x, halo, f, rate_t):
    streams_count, rows, width = x.shape
    taps = f.shape[0]
    modes = rate_t.shape[0]
    return pl.pallas_call(
        state_kernel,
        grid=(width // BLOCK,),
        in_specs=[
            pl.BlockSpec((streams_count, rows, BLOCK), lambda i: (0, 0, i)),
            pl.BlockSpec((streams_count, taps - 1, BLOCK), lambda i: (0, 0, i)),
            pl.BlockSpec((taps, streams_count, BLOCK), lambda i: (0, 0, i)),
            pl.BlockSpec((modes, BLOCK), lambda i: (0, i)),
        ],
        out_specs=[
            pl.BlockSpec((modes, SUB, BLOCK), lambda i: (0, 0, i)),
            pl.BlockSpec((modes, BLOCK), lambda i: (0, i)),
        ],
        out_shape=[
            jax.ShapeDtypeStruct((modes, SUB, width), jnp.float32),
            jax.ShapeDtypeStruct((modes, width), jnp.float32),
        ],
        scratch_shapes=[
            pltpu.VMEM((streams_count, BLOCK // LANES, rows, LANES), jnp.float32),
            pltpu.VMEM((modes, SUB, LANES), jnp.float32),
            pltpu.VMEM((taps * streams_count, SUB, LANES), jnp.float32),
        ],
    )(x, halo, f, rate_t)


def run_out(x, halo, f, rate_t, residue_t, skip, ends, fix, hin):
    streams_count, rows, width = x.shape
    taps = f.shape[0]
    modes = rate_t.shape[0]
    return pl.pallas_call(
        out_kernel,
        grid=(width // BLOCK,),
        in_specs=[
            pl.BlockSpec((streams_count, rows, BLOCK), lambda i: (0, 0, i)),
            pl.BlockSpec((streams_count, taps - 1, BLOCK), lambda i: (0, 0, i)),
            pl.BlockSpec((taps, streams_count, BLOCK), lambda i: (0, 0, i)),
            pl.BlockSpec((modes, BLOCK), lambda i: (0, i)),
            pl.BlockSpec((modes, BLOCK), lambda i: (0, i)),
            pl.BlockSpec((1, BLOCK), lambda i: (0, i)),
            pl.BlockSpec((modes, SUB, BLOCK), lambda i: (0, 0, i)),
            pl.BlockSpec((modes, BLOCK), lambda i: (0, i)),
            pl.BlockSpec((modes, BLOCK), lambda i: (0, i)),
        ],
        out_specs=pl.BlockSpec((rows, BLOCK), lambda i: (0, i)),
        out_shape=jax.ShapeDtypeStruct((rows, width), jnp.bfloat16),
        scratch_shapes=[
            pltpu.VMEM((streams_count, BLOCK // LANES, rows, LANES), jnp.float32),
            pltpu.VMEM((BLOCK // LANES, rows, LANES), jnp.float32),
            pltpu.VMEM((modes, SUB, LANES), jnp.float32),
            pltpu.VMEM((modes, SUB, LANES), jnp.float32),
            pltpu.VMEM((taps * streams_count, SUB, LANES), jnp.float32),
        ],
    )(x, halo, f, rate_t, residue_t, skip, ends, fix, hin)


def body(streams, short_filter, skip, rates, residues):
    axes = ("ctx", "tp")
    devices = lax.axis_size("ctx") * lax.axis_size("tp")
    tok_rows, streams_count, width = streams.shape
    taps = short_filter.shape[0]
    modes = rates.shape[1]

    def shift(value, offset):
        pairs = [(j, j + offset) for j in range(devices - offset)]
        return lax.ppermute(value, axes, pairs)

    halo_rows = shift(streams[tok_rows - (taps - 1) :], 1).astype(jnp.float32)
    halo = jnp.transpose(halo_rows, (1, 0, 2))
    x = jnp.transpose(streams, (1, 0, 2))
    rate_t = rates.T
    residue_t = residues.T
    ends, local = run_state(x, jnp.zeros_like(halo), short_filter, rate_t)

    head = streams[: taps - 1].astype(jnp.float32)

    def head_gate(before):
        rows = jnp.concatenate([before, head], axis=0)
        gated = []
        for t in range(taps - 1):
            feat = short_filter[0] * rows[t + taps - 1]
            for tap in range(1, taps):
                feat = feat + short_filter[tap] * rows[t + taps - 1 - tap]
            gated.append((feat[1] * feat[2]).astype(jnp.bfloat16).astype(jnp.float32))
        return gated

    seg = tok_rows // SUB
    true_head = head_gate(halo_rows)
    zero_head = head_gate(jnp.zeros_like(halo_rows))
    local_fix = None
    ends_fix = None
    for t in range(taps - 1):
        delta = (true_head[t] - zero_head[t])[None, :]
        to_end = jnp.exp(-rate_t * float(tok_rows - 1 - t)) * delta
        to_seg = jnp.exp(-rate_t * float(seg - 1 - t)) * delta
        local_fix = to_end if local_fix is None else local_fix + to_end
        ends_fix = to_seg if ends_fix is None else ends_fix + to_seg
    local = local + local_fix

    def decay_pow(steps):
        return jnp.exp(-rate_t * float(tok_rows * steps))

    def gather_window(value, spacing, count):
        sent = value
        total = None
        for k in range(1, count + 1):
            if k * spacing >= devices:
                break
            term = decay_pow((k - 1) * spacing) * shift(sent, k * spacing)
            total = term if total is None else total + term
        return total

    first = min(FIRST_WINDOW, devices - 1)
    carried = gather_window(local, 1, first)
    window = first
    while window < devices - 1:
        count = min(-(-(devices - 1) // window) - 1, FIRST_WINDOW)
        carried = carried + decay_pow(window) * gather_window(carried, window, count)
        window *= count + 1

    return run_out(x, halo, short_filter, rate_t, residue_t, skip.reshape(1, width), ends, ends_fix, carried)


def solution(mesh):
    return jax.shard_map(
        body,
        mesh=mesh,
        in_specs=(P(("ctx", "tp"), None, None), P(), P(), P(), P()),
        out_specs=P(("ctx", "tp"), None),
        check_vma=False,
    )
```

```python
import jax
import jax.numpy as jnp
from jax import lax
from jax.experimental import pallas as pl
from jax.experimental.pallas import tpu as pltpu
from jax.sharding import PartitionSpec as P

LANES = 128
SUB = 8
BLOCK = 1024
FIRST_WINDOW = 3
LATER_WINDOW = 4
UNROLL = 8


def lane_slice(c):
    return pl.ds(pl.multiple_of(c * LANES, LANES), LANES)


def row(ref, index, lanes):
    return jnp.broadcast_to(ref[pl.ds(index, 1), lanes], (SUB, LANES))


def first_prev(xs, halo_ref, c, lanes, seg, taps, sub):
    prev = []
    for back in range(1, taps):
        per_stream = []
        for s in range(xs.shape[0]):
            rows = xs[s, c, pl.ds(seg - back, SUB, stride=seg), :]
            edge = jnp.broadcast_to(halo_ref[s, pl.ds(taps - 1 - back, 1), lanes], (SUB, LANES))
            per_stream.append(jnp.where(sub == 0, edge, pltpu.roll(rows, 1, 0)))
        prev.append(per_stream)
    return prev


def fill_filters(f_ref, fsc, lanes):
    streams_count = f_ref.shape[1]
    for tap in range(f_ref.shape[0]):
        for s in range(streams_count):
            fsc[tap * streams_count + s] = row(f_ref.at[tap], s, lanes)


def step_features(xs, fsc, c, seg, j, prev):
    streams_count = xs.shape[0]
    taps = len(prev) + 1
    now = [xs[s, c, pl.ds(j, SUB, stride=seg), :] for s in range(streams_count)]
    feats = []
    for s in range(streams_count):
        acc = fsc[s] * now[s]
        for tap in range(1, taps):
            acc = acc + fsc[tap * streams_count + s] * prev[tap - 1][s]
        feats.append(acc)
    new_prev = [now] + prev[:-1]
    return feats, new_prev


def gate(feats):
    return (feats[1] * feats[2]).astype(jnp.bfloat16).astype(jnp.float32)


def state_kernel(x_ref, halo_ref, f_ref, a_ref, seg_ref, h_ref, xs, dsc, fsc):
    streams_count, rows, block = x_ref.shape
    taps = f_ref.shape[0]
    modes = a_ref.shape[0]
    seg = rows // SUB
    for c in range(block // LANES):
        xs[:, c] = x_ref[:, :, c * LANES : (c + 1) * LANES].astype(jnp.float32)
    sub = lax.broadcasted_iota(jnp.int32, (SUB, LANES), 0)

    def lane_group(c, carry):
        lanes = lane_slice(c)
        fill_filters(f_ref, fsc, lanes)
        for m in range(modes):
            dsc[m] = jnp.exp(-row(a_ref, m, lanes))

        def step(j, state):
            prev, states = state
            feats, prev = step_features(xs, fsc, c, seg, j, prev)
            u = gate(feats)
            return prev, tuple(dsc[m] * states[m] + u for m in range(modes))

        zero = jnp.zeros((SUB, LANES), jnp.float32)
        init = (first_prev(xs, halo_ref, c, lanes, seg, taps, sub), (zero,) * modes)
        _, states = lax.fori_loop(0, seg, step, init, unroll=UNROLL)
        later = (SUB - 1 - sub).astype(jnp.float32) * float(seg)
        for m in range(modes):
            seg_ref[m, :, lanes] = states[m]
            weight = jnp.exp(-row(a_ref, m, lanes) * later)
            h_ref[pl.ds(m, 1), lanes] = jnp.sum(weight * states[m], axis=0, keepdims=True)
        return carry

    lax.fori_loop(0, block // LANES, lane_group, 0)


def out_kernel(
    x_ref, halo_ref, f_ref, a_ref, r_ref, skip_ref, seg_ref, fix_ref, hin_ref, o_ref, xs, ys, dsc, rsc, fsc
):
    streams_count, rows, block = x_ref.shape
    taps = f_ref.shape[0]
    modes = a_ref.shape[0]
    seg = rows // SUB
    for c in range(block // LANES):
        xs[:, c] = x_ref[:, :, c * LANES : (c + 1) * LANES].astype(jnp.float32)
    sub = lax.broadcasted_iota(jnp.int32, (SUB, LANES), 0)

    def lane_group(c, carry):
        lanes = lane_slice(c)
        fill_filters(f_ref, fsc, lanes)
        starts = []
        for m in range(modes):
            rate = row(a_ref, m, lanes)
            dsc[m] = jnp.exp(-rate)
            rsc[m] = row(r_ref, m, lanes)
            ends = seg_ref[m, :, lanes] + jnp.where(sub == 0, row(fix_ref, m, lanes), 0.0)
            carried = jnp.where(sub >= 1, pltpu.roll(ends, 1, 0), 0.0)
            offset = 1
            while offset < SUB:
                factor = jnp.exp(-rate * float(seg * offset))
                carried = carried + jnp.where(sub >= offset, factor * pltpu.roll(carried, offset, 0), 0.0)
                offset *= 2
            lead = jnp.exp(-rate * (sub.astype(jnp.float32) * float(seg)))
            starts.append(carried + lead * row(hin_ref, m, lanes))
        skip_rows = row(skip_ref, 0, lanes)

        def step(j, state):
            prev, states = state
            feats, prev = step_features(xs, fsc, c, seg, j, prev)
            u = gate(feats)
            new = [dsc[m] * states[m] + u for m in range(modes)]
            terms = [rsc[m] * new[m] for m in range(modes)]
            while len(terms) > 1:
                paired = [terms[i] + terms[i + 1] for i in range(0, len(terms) - 1, 2)]
                terms = paired + terms[len(terms) - len(terms) % 2 :]
            conv = terms[0]
            y = (conv + skip_rows * u).astype(jnp.bfloat16).astype(jnp.float32)
            ys[c, pl.ds(j, SUB, stride=seg), :] = feats[0] * y
            return prev, tuple(new)

        init = (first_prev(xs, halo_ref, c, lanes, seg, taps, sub), tuple(starts))
        lax.fori_loop(0, seg, step, init, unroll=UNROLL)
        return carry

    lax.fori_loop(0, block // LANES, lane_group, 0)
    for c in range(block // LANES):
        o_ref[:, c * LANES : (c + 1) * LANES] = ys[c].astype(o_ref.dtype)


def run_state(x, halo, f, rate_t):
    streams_count, rows, width = x.shape
    taps = f.shape[0]
    modes = rate_t.shape[0]
    return pl.pallas_call(
        state_kernel,
        grid=(width // BLOCK,),
        in_specs=[
            pl.BlockSpec((streams_count, rows, BLOCK), lambda i: (0, 0, i)),
            pl.BlockSpec((streams_count, taps - 1, BLOCK), lambda i: (0, 0, i)),
            pl.BlockSpec((taps, streams_count, BLOCK), lambda i: (0, 0, i)),
            pl.BlockSpec((modes, BLOCK), lambda i: (0, i)),
        ],
        out_specs=[
            pl.BlockSpec((modes, SUB, BLOCK), lambda i: (0, 0, i)),
            pl.BlockSpec((modes, BLOCK), lambda i: (0, i)),
        ],
        out_shape=[
            jax.ShapeDtypeStruct((modes, SUB, width), jnp.float32),
            jax.ShapeDtypeStruct((modes, width), jnp.float32),
        ],
        scratch_shapes=[
            pltpu.VMEM((streams_count, BLOCK // LANES, rows, LANES), jnp.float32),
            pltpu.VMEM((modes, SUB, LANES), jnp.float32),
            pltpu.VMEM((taps * streams_count, SUB, LANES), jnp.float32),
        ],
    )(x, halo, f, rate_t)


def run_out(x, halo, f, rate_t, residue_t, skip, ends, fix, hin):
    streams_count, rows, width = x.shape
    taps = f.shape[0]
    modes = rate_t.shape[0]
    return pl.pallas_call(
        out_kernel,
        grid=(width // BLOCK,),
        in_specs=[
            pl.BlockSpec((streams_count, rows, BLOCK), lambda i: (0, 0, i)),
            pl.BlockSpec((streams_count, taps - 1, BLOCK), lambda i: (0, 0, i)),
            pl.BlockSpec((taps, streams_count, BLOCK), lambda i: (0, 0, i)),
            pl.BlockSpec((modes, BLOCK), lambda i: (0, i)),
            pl.BlockSpec((modes, BLOCK), lambda i: (0, i)),
            pl.BlockSpec((1, BLOCK), lambda i: (0, i)),
            pl.BlockSpec((modes, SUB, BLOCK), lambda i: (0, 0, i)),
            pl.BlockSpec((modes, BLOCK), lambda i: (0, i)),
            pl.BlockSpec((modes, BLOCK), lambda i: (0, i)),
        ],
        out_specs=pl.BlockSpec((rows, BLOCK), lambda i: (0, i)),
        out_shape=jax.ShapeDtypeStruct((rows, width), jnp.bfloat16),
        scratch_shapes=[
            pltpu.VMEM((streams_count, BLOCK // LANES, rows, LANES), jnp.float32),
            pltpu.VMEM((BLOCK // LANES, rows, LANES), jnp.float32),
            pltpu.VMEM((modes, SUB, LANES), jnp.float32),
            pltpu.VMEM((modes, SUB, LANES), jnp.float32),
            pltpu.VMEM((taps * streams_count, SUB, LANES), jnp.float32),
        ],
    )(x, halo, f, rate_t, residue_t, skip, ends, fix, hin)


def body(streams, short_filter, skip, rates, residues):
    axes = ("ctx", "tp")
    devices = lax.axis_size("ctx") * lax.axis_size("tp")
    tok_rows, streams_count, width = streams.shape
    taps = short_filter.shape[0]
    modes = rates.shape[1]

    def shift(value, offset):
        pairs = [(j, j + offset) for j in range(devices - offset)]
        return lax.ppermute(value, axes, pairs)

    halo_rows = shift(streams[tok_rows - (taps - 1) :], 1).astype(jnp.float32)
    halo = jnp.transpose(halo_rows, (1, 0, 2))
    x = jnp.transpose(streams, (1, 0, 2))
    rate_t = rates.T
    residue_t = residues.T
    ends, local = run_state(x, jnp.zeros_like(halo), short_filter, rate_t)

    head = streams[: taps - 1].astype(jnp.float32)

    def head_gate(before):
        rows = jnp.concatenate([before, head], axis=0)
        gated = []
        for t in range(taps - 1):
            feat = short_filter[0] * rows[t + taps - 1]
            for tap in range(1, taps):
                feat = feat + short_filter[tap] * rows[t + taps - 1 - tap]
            gated.append((feat[1] * feat[2]).astype(jnp.bfloat16).astype(jnp.float32))
        return gated

    seg = tok_rows // SUB
    true_head = head_gate(halo_rows)
    zero_head = head_gate(jnp.zeros_like(halo_rows))
    local_fix = None
    ends_fix = None
    for t in range(taps - 1):
        delta = (true_head[t] - zero_head[t])[None, :]
        to_end = jnp.exp(-rate_t * float(tok_rows - 1 - t)) * delta
        to_seg = jnp.exp(-rate_t * float(seg - 1 - t)) * delta
        local_fix = to_end if local_fix is None else local_fix + to_end
        ends_fix = to_seg if ends_fix is None else ends_fix + to_seg
    local = local + local_fix

    group = lax.axis_size("tp")
    spans = lax.axis_size("ctx")
    member = lax.axis_index("tp")
    piece = width // group

    def exchange(value, k):
        return lax.ppermute(value, "tp", [(q, (q + k) % group) for q in range(group)])

    def powers(rates_part, count):
        return jnp.exp(-rates_part * (float(tok_rows) * count))

    inside = None
    total = powers(rate_t, (group - 1 - member).astype(jnp.float32)) * local
    for k in range(1, group):
        other = exchange(local, k)
        source = (member - k) % group
        total = total + powers(rate_t, (group - 1 - source).astype(jnp.float32)) * other
        term = jnp.where(k <= member, powers(rate_t, float(k - 1)) * other, 0.0)
        inside = term if inside is None else inside + term
    if inside is None:
        inside = jnp.zeros_like(local)

    first_channel = member * piece
    rate_part = lax.dynamic_slice_in_dim(rate_t, first_channel, piece, 1)
    total_part = lax.dynamic_slice_in_dim(total, first_channel, piece, 1)

    def span_shift(value, offset):
        return lax.ppermute(value, "ctx", [(j, j + offset) for j in range(spans - offset)])

    def gather_window(value, spacing, count):
        gathered = None
        for k in range(1, count + 1):
            if k * spacing >= spans:
                break
            term = powers(rate_part, float(group * (k - 1) * spacing)) * span_shift(value, k * spacing)
            gathered = term if gathered is None else gathered + term
        return gathered

    if spans > 1:
        first = min(FIRST_WINDOW, spans - 1)
        before = gather_window(total_part, 1, first)
        window = first
        while window < spans - 1:
            count = min(-(-(spans - 1) // window) - 1, LATER_WINDOW)
            before = before + powers(rate_part, float(group * window)) * gather_window(before, window, count)
            window *= count + 1
    else:
        before = jnp.zeros_like(total_part)

    whole = jnp.zeros_like(local)
    for k in range(group):
        part = before if k == 0 else exchange(before, k)
        whole = lax.dynamic_update_slice_in_dim(whole, part, ((member - k) % group) * piece, 1)
    carried = powers(rate_t, member.astype(jnp.float32)) * whole + inside

    return run_out(x, halo, short_filter, rate_t, residue_t, skip.reshape(1, width), ends, ends_fix, carried)


def solution(mesh):
    return jax.shard_map(
        body,
        mesh=mesh,
        in_specs=(P(("ctx", "tp"), None, None), P(), P(), P(), P()),
        out_specs=P(("ctx", "tp"), None),
        check_vma=False,
    )
```

```python
import jax
import jax.numpy as jnp
from jax import lax
from jax.experimental import pallas as pl
from jax.experimental.pallas import tpu as pltpu
from jax.sharding import PartitionSpec as P

LANES = 128
SUB = 8
BLOCK = 1024
FIRST_WINDOW = 2
LATER_WINDOW = 2
UNROLL = 8


def lane_slice(c):
    return pl.ds(pl.multiple_of(c * LANES, LANES), LANES)


def row(ref, index, lanes):
    return jnp.broadcast_to(ref[pl.ds(index, 1), lanes], (SUB, LANES))


def first_prev(xs, halo_ref, c, lanes, seg, taps, sub):
    prev = []
    for back in range(1, taps):
        per_stream = []
        for s in range(xs.shape[0]):
            rows = xs[s, c, pl.ds(seg - back, SUB, stride=seg), :]
            edge = jnp.broadcast_to(halo_ref[s, pl.ds(taps - 1 - back, 1), lanes], (SUB, LANES))
            per_stream.append(jnp.where(sub == 0, edge, pltpu.roll(rows, 1, 0)))
        prev.append(per_stream)
    return prev


def fill_filters(f_ref, fsc, lanes):
    streams_count = f_ref.shape[1]
    for tap in range(f_ref.shape[0]):
        for s in range(streams_count):
            fsc[tap * streams_count + s] = row(f_ref.at[tap], s, lanes)


def step_features(xs, fsc, c, seg, j, prev):
    streams_count = xs.shape[0]
    taps = len(prev) + 1
    now = [xs[s, c, pl.ds(j, SUB, stride=seg), :] for s in range(streams_count)]
    feats = []
    for s in range(streams_count):
        acc = fsc[s] * now[s]
        for tap in range(1, taps):
            acc = acc + fsc[tap * streams_count + s] * prev[tap - 1][s]
        feats.append(acc)
    new_prev = [now] + prev[:-1]
    return feats, new_prev


def gate(feats):
    return (feats[1] * feats[2]).astype(jnp.bfloat16).astype(jnp.float32)


def state_kernel(x_ref, halo_ref, f_ref, a_ref, seg_ref, h_ref, xs, dsc, fsc):
    streams_count, rows, block = x_ref.shape
    taps = f_ref.shape[0]
    modes = a_ref.shape[0]
    seg = rows // SUB
    for c in range(block // LANES):
        xs[:, c] = x_ref[:, :, c * LANES : (c + 1) * LANES].astype(jnp.float32)
    sub = lax.broadcasted_iota(jnp.int32, (SUB, LANES), 0)

    def lane_group(c, carry):
        lanes = lane_slice(c)
        fill_filters(f_ref, fsc, lanes)
        for m in range(modes):
            dsc[m] = jnp.exp(-row(a_ref, m, lanes))

        def step(j, state):
            prev, states = state
            feats, prev = step_features(xs, fsc, c, seg, j, prev)
            u = gate(feats)
            return prev, tuple(dsc[m] * states[m] + u for m in range(modes))

        zero = jnp.zeros((SUB, LANES), jnp.float32)
        init = (first_prev(xs, halo_ref, c, lanes, seg, taps, sub), (zero,) * modes)
        _, states = lax.fori_loop(0, seg, step, init, unroll=UNROLL)
        later = (SUB - 1 - sub).astype(jnp.float32) * float(seg)
        for m in range(modes):
            seg_ref[m, :, lanes] = states[m]
            weight = jnp.exp(-row(a_ref, m, lanes) * later)
            h_ref[pl.ds(m, 1), lanes] = jnp.sum(weight * states[m], axis=0, keepdims=True)
        return carry

    lax.fori_loop(0, block // LANES, lane_group, 0)


def out_kernel(
    x_ref, halo_ref, f_ref, a_ref, r_ref, skip_ref, seg_ref, fix_ref, hin_ref, o_ref, xs, ys, dsc, rsc, fsc
):
    streams_count, rows, block = x_ref.shape
    taps = f_ref.shape[0]
    modes = a_ref.shape[0]
    seg = rows // SUB
    for c in range(block // LANES):
        xs[:, c] = x_ref[:, :, c * LANES : (c + 1) * LANES].astype(jnp.float32)
    sub = lax.broadcasted_iota(jnp.int32, (SUB, LANES), 0)

    def lane_group(c, carry):
        lanes = lane_slice(c)
        fill_filters(f_ref, fsc, lanes)
        starts = []
        for m in range(modes):
            rate = row(a_ref, m, lanes)
            dsc[m] = jnp.exp(-rate)
            rsc[m] = row(r_ref, m, lanes)
            ends = seg_ref[m, :, lanes] + jnp.where(sub == 0, row(fix_ref, m, lanes), 0.0)
            carried = jnp.where(sub >= 1, pltpu.roll(ends, 1, 0), 0.0)
            offset = 1
            while offset < SUB:
                factor = jnp.exp(-rate * float(seg * offset))
                carried = carried + jnp.where(sub >= offset, factor * pltpu.roll(carried, offset, 0), 0.0)
                offset *= 2
            lead = jnp.exp(-rate * (sub.astype(jnp.float32) * float(seg)))
            starts.append(carried + lead * row(hin_ref, m, lanes))
        skip_rows = row(skip_ref, 0, lanes)

        def step(j, state):
            prev, states = state
            feats, prev = step_features(xs, fsc, c, seg, j, prev)
            u = gate(feats)
            new = [dsc[m] * states[m] + u for m in range(modes)]
            terms = [rsc[m] * new[m] for m in range(modes)]
            while len(terms) > 1:
                paired = [terms[i] + terms[i + 1] for i in range(0, len(terms) - 1, 2)]
                terms = paired + terms[len(terms) - len(terms) % 2 :]
            conv = terms[0]
            y = (conv + skip_rows * u).astype(jnp.bfloat16).astype(jnp.float32)
            ys[c, pl.ds(j, SUB, stride=seg), :] = feats[0] * y
            return prev, tuple(new)

        init = (first_prev(xs, halo_ref, c, lanes, seg, taps, sub), tuple(starts))
        lax.fori_loop(0, seg, step, init, unroll=UNROLL)
        return carry

    lax.fori_loop(0, block // LANES, lane_group, 0)
    for c in range(block // LANES):
        o_ref[:, c * LANES : (c + 1) * LANES] = ys[c].astype(o_ref.dtype)


def run_state(x, halo, f, rate_t):
    streams_count, rows, width = x.shape
    taps = f.shape[0]
    modes = rate_t.shape[0]
    return pl.pallas_call(
        state_kernel,
        grid=(width // BLOCK,),
        in_specs=[
            pl.BlockSpec((streams_count, rows, BLOCK), lambda i: (0, 0, i)),
            pl.BlockSpec((streams_count, taps - 1, BLOCK), lambda i: (0, 0, i)),
            pl.BlockSpec((taps, streams_count, BLOCK), lambda i: (0, 0, i)),
            pl.BlockSpec((modes, BLOCK), lambda i: (0, i)),
        ],
        out_specs=[
            pl.BlockSpec((modes, SUB, BLOCK), lambda i: (0, 0, i)),
            pl.BlockSpec((modes, BLOCK), lambda i: (0, i)),
        ],
        out_shape=[
            jax.ShapeDtypeStruct((modes, SUB, width), jnp.float32),
            jax.ShapeDtypeStruct((modes, width), jnp.float32),
        ],
        scratch_shapes=[
            pltpu.VMEM((streams_count, BLOCK // LANES, rows, LANES), jnp.float32),
            pltpu.VMEM((modes, SUB, LANES), jnp.float32),
            pltpu.VMEM((taps * streams_count, SUB, LANES), jnp.float32),
        ],
    )(x, halo, f, rate_t)


def run_out(x, halo, f, rate_t, residue_t, skip, ends, fix, hin):
    streams_count, rows, width = x.shape
    taps = f.shape[0]
    modes = rate_t.shape[0]
    return pl.pallas_call(
        out_kernel,
        grid=(width // BLOCK,),
        in_specs=[
            pl.BlockSpec((streams_count, rows, BLOCK), lambda i: (0, 0, i)),
            pl.BlockSpec((streams_count, taps - 1, BLOCK), lambda i: (0, 0, i)),
            pl.BlockSpec((taps, streams_count, BLOCK), lambda i: (0, 0, i)),
            pl.BlockSpec((modes, BLOCK), lambda i: (0, i)),
            pl.BlockSpec((modes, BLOCK), lambda i: (0, i)),
            pl.BlockSpec((1, BLOCK), lambda i: (0, i)),
            pl.BlockSpec((modes, SUB, BLOCK), lambda i: (0, 0, i)),
            pl.BlockSpec((modes, BLOCK), lambda i: (0, i)),
            pl.BlockSpec((modes, BLOCK), lambda i: (0, i)),
        ],
        out_specs=pl.BlockSpec((rows, BLOCK), lambda i: (0, i)),
        out_shape=jax.ShapeDtypeStruct((rows, width), jnp.bfloat16),
        scratch_shapes=[
            pltpu.VMEM((streams_count, BLOCK // LANES, rows, LANES), jnp.float32),
            pltpu.VMEM((BLOCK // LANES, rows, LANES), jnp.float32),
            pltpu.VMEM((modes, SUB, LANES), jnp.float32),
            pltpu.VMEM((modes, SUB, LANES), jnp.float32),
            pltpu.VMEM((taps * streams_count, SUB, LANES), jnp.float32),
        ],
    )(x, halo, f, rate_t, residue_t, skip, ends, fix, hin)


def body(streams, short_filter, skip, rates, residues):
    axes = ("ctx", "tp")
    devices = lax.axis_size("ctx") * lax.axis_size("tp")
    tok_rows, streams_count, width = streams.shape
    taps = short_filter.shape[0]
    modes = rates.shape[1]

    def shift(value, offset):
        pairs = [(j, j + offset) for j in range(devices - offset)]
        return lax.ppermute(value, axes, pairs)

    halo_rows = shift(streams[tok_rows - (taps - 1) :], 1).astype(jnp.float32)
    halo = jnp.transpose(halo_rows, (1, 0, 2))
    x = jnp.transpose(streams, (1, 0, 2))
    rate_t = rates.T
    residue_t = residues.T
    ends, local = run_state(x, jnp.zeros_like(halo), short_filter, rate_t)

    head = streams[: taps - 1].astype(jnp.float32)

    def head_gate(before):
        rows = jnp.concatenate([before, head], axis=0)
        gated = []
        for t in range(taps - 1):
            feat = short_filter[0] * rows[t + taps - 1]
            for tap in range(1, taps):
                feat = feat + short_filter[tap] * rows[t + taps - 1 - tap]
            gated.append((feat[1] * feat[2]).astype(jnp.bfloat16).astype(jnp.float32))
        return gated

    seg = tok_rows // SUB
    true_head = head_gate(halo_rows)
    zero_head = head_gate(jnp.zeros_like(halo_rows))
    local_fix = None
    ends_fix = None
    for t in range(taps - 1):
        delta = (true_head[t] - zero_head[t])[None, :]
        to_end = jnp.exp(-rate_t * float(tok_rows - 1 - t)) * delta
        to_seg = jnp.exp(-rate_t * float(seg - 1 - t)) * delta
        local_fix = to_end if local_fix is None else local_fix + to_end
        ends_fix = to_seg if ends_fix is None else ends_fix + to_seg
    local = local + local_fix

    group = lax.axis_size("tp")
    spans = lax.axis_size("ctx")
    member = lax.axis_index("tp")
    piece = width // group

    def exchange(value, k):
        return lax.ppermute(value, "tp", [(q, (q + k) % group) for q in range(group)])

    def powers(rates_part, count):
        return jnp.exp(-rates_part * (float(tok_rows) * count))

    inside = None
    total = powers(rate_t, (group - 1 - member).astype(jnp.float32)) * local
    for k in range(1, group):
        other = exchange(local, k)
        source = (member - k) % group
        total = total + powers(rate_t, (group - 1 - source).astype(jnp.float32)) * other
        term = jnp.where(k <= member, powers(rate_t, float(k - 1)) * other, 0.0)
        inside = term if inside is None else inside + term
    if inside is None:
        inside = jnp.zeros_like(local)

    first_channel = member * piece
    rate_part = lax.dynamic_slice_in_dim(rate_t, first_channel, piece, 1)
    total_part = lax.dynamic_slice_in_dim(total, first_channel, piece, 1)

    def span_shift(value, offset):
        return lax.ppermute(value, "ctx", [(j, j + offset) for j in range(spans - offset)])

    def gather_window(value, spacing, count):
        gathered = None
        for k in range(1, count + 1):
            if k * spacing >= spans:
                break
            term = powers(rate_part, float(group * (k - 1) * spacing)) * span_shift(value, k * spacing)
            gathered = term if gathered is None else gathered + term
        return gathered

    if spans > 1:
        first = min(FIRST_WINDOW, spans - 1)
        before = gather_window(total_part, 1, first)
        window = first
        while window < spans - 1:
            count = min(-(-(spans - 1) // window) - 1, LATER_WINDOW)
            before = before + powers(rate_part, float(group * window)) * gather_window(before, window, count)
            window *= count + 1
    else:
        before = jnp.zeros_like(total_part)

    whole = jnp.zeros_like(local)
    for k in range(group):
        part = before if k == 0 else exchange(before, k)
        whole = lax.dynamic_update_slice_in_dim(whole, part, ((member - k) % group) * piece, 1)
    carried = powers(rate_t, member.astype(jnp.float32)) * whole + inside

    return run_out(x, halo, short_filter, rate_t, residue_t, skip.reshape(1, width), ends, ends_fix, carried)


def solution(mesh):
    return jax.shard_map(
        body,
        mesh=mesh,
        in_specs=(P(("ctx", "tp"), None, None), P(), P(), P(), P()),
        out_specs=P(("ctx", "tp"), None),
        check_vma=False,
    )
```

```python
import jax
import jax.numpy as jnp
from jax import lax
from jax.experimental import pallas as pl
from jax.experimental.pallas import tpu as pltpu
from jax.sharding import PartitionSpec as P

LANES = 128
SUB = 8
BLOCK = 1024
FIRST_WINDOW = 3
LATER_WINDOW = 4
UNROLL = 8


def lane_slice(c):
    return pl.ds(pl.multiple_of(c * LANES, LANES), LANES)


def row(ref, index, lanes):
    return jnp.broadcast_to(ref[pl.ds(index, 1), lanes], (SUB, LANES))


def first_prev(xs, halo_ref, c, lanes, seg, taps, sub):
    prev = []
    for back in range(1, taps):
        per_stream = []
        for s in range(xs.shape[0]):
            rows = xs[s, c, pl.ds(seg - back, SUB, stride=seg), :]
            edge = jnp.broadcast_to(halo_ref[s, pl.ds(taps - 1 - back, 1), lanes], (SUB, LANES))
            per_stream.append(jnp.where(sub == 0, edge, pltpu.roll(rows, 1, 0)))
        prev.append(per_stream)
    return prev


def fill_filters(f_ref, fsc, lanes):
    streams_count = f_ref.shape[1]
    for tap in range(f_ref.shape[0]):
        for s in range(streams_count):
            fsc[tap * streams_count + s] = row(f_ref.at[tap], s, lanes)


def step_features(xs, fsc, c, seg, j, prev):
    streams_count = xs.shape[0]
    taps = len(prev) + 1
    now = [xs[s, c, pl.ds(j, SUB, stride=seg), :] for s in range(streams_count)]
    feats = []
    for s in range(streams_count):
        acc = fsc[s] * now[s]
        for tap in range(1, taps):
            acc = acc + fsc[tap * streams_count + s] * prev[tap - 1][s]
        feats.append(acc)
    new_prev = [now] + prev[:-1]
    return feats, new_prev


def gate(feats):
    return (feats[1] * feats[2]).astype(jnp.bfloat16).astype(jnp.float32)


def state_kernel(x_ref, halo_ref, f_ref, a_ref, seg_ref, h_ref, xs, dsc, fsc):
    streams_count, rows, block = x_ref.shape
    taps = f_ref.shape[0]
    modes = a_ref.shape[0]
    seg = rows // SUB
    for c in range(block // LANES):
        xs[:, c] = x_ref[:, :, c * LANES : (c + 1) * LANES].astype(jnp.float32)
    sub = lax.broadcasted_iota(jnp.int32, (SUB, LANES), 0)

    def lane_group(c, carry):
        lanes = lane_slice(c)
        fill_filters(f_ref, fsc, lanes)
        for m in range(modes):
            dsc[m] = jnp.exp(-row(a_ref, m, lanes))

        def step(j, state):
            prev, states = state
            feats, prev = step_features(xs, fsc, c, seg, j, prev)
            u = gate(feats)
            return prev, tuple(dsc[m] * states[m] + u for m in range(modes))

        zero = jnp.zeros((SUB, LANES), jnp.float32)
        init = (first_prev(xs, halo_ref, c, lanes, seg, taps, sub), (zero,) * modes)
        _, states = lax.fori_loop(0, seg, step, init, unroll=UNROLL)
        later = (SUB - 1 - sub).astype(jnp.float32) * float(seg)
        for m in range(modes):
            seg_ref[m, :, lanes] = states[m]
            weight = jnp.exp(-row(a_ref, m, lanes) * later)
            h_ref[pl.ds(m, 1), lanes] = jnp.sum(weight * states[m], axis=0, keepdims=True)
        return carry

    lax.fori_loop(0, block // LANES, lane_group, 0)


def out_kernel(
    x_ref, halo_ref, f_ref, a_ref, r_ref, skip_ref, seg_ref, fix_ref, hin_ref, o_ref, xs, ys, dsc, rsc, fsc
):
    streams_count, rows, block = x_ref.shape
    taps = f_ref.shape[0]
    modes = a_ref.shape[0]
    seg = rows // SUB
    for c in range(block // LANES):
        xs[:, c] = x_ref[:, :, c * LANES : (c + 1) * LANES].astype(jnp.float32)
    sub = lax.broadcasted_iota(jnp.int32, (SUB, LANES), 0)

    def lane_group(c, carry):
        lanes = lane_slice(c)
        fill_filters(f_ref, fsc, lanes)
        starts = []
        for m in range(modes):
            rate = row(a_ref, m, lanes)
            dsc[m] = jnp.exp(-rate)
            rsc[m] = row(r_ref, m, lanes)
            ends = seg_ref[m, :, lanes] + jnp.where(sub == 0, row(fix_ref, m, lanes), 0.0)
            carried = jnp.where(sub >= 1, pltpu.roll(ends, 1, 0), 0.0)
            offset = 1
            while offset < SUB:
                factor = jnp.exp(-rate * float(seg * offset))
                carried = carried + jnp.where(sub >= offset, factor * pltpu.roll(carried, offset, 0), 0.0)
                offset *= 2
            lead = jnp.exp(-rate * (sub.astype(jnp.float32) * float(seg)))
            starts.append(carried + lead * row(hin_ref, m, lanes))
        skip_rows = row(skip_ref, 0, lanes)

        def step(j, state):
            prev, states = state
            feats, prev = step_features(xs, fsc, c, seg, j, prev)
            u = gate(feats)
            new = [dsc[m] * states[m] + u for m in range(modes)]
            terms = [rsc[m] * new[m] for m in range(modes)]
            while len(terms) > 1:
                paired = [terms[i] + terms[i + 1] for i in range(0, len(terms) - 1, 2)]
                terms = paired + terms[len(terms) - len(terms) % 2 :]
            conv = terms[0]
            y = (conv + skip_rows * u).astype(jnp.bfloat16).astype(jnp.float32)
            ys[c, pl.ds(j, SUB, stride=seg), :] = feats[0] * y
            return prev, tuple(new)

        init = (first_prev(xs, halo_ref, c, lanes, seg, taps, sub), tuple(starts))
        lax.fori_loop(0, seg, step, init, unroll=UNROLL)
        return carry

    lax.fori_loop(0, block // LANES, lane_group, 0)
    for c in range(block // LANES):
        o_ref[:, c * LANES : (c + 1) * LANES] = ys[c].astype(o_ref.dtype)


def run_state(x, halo, f, rate_t):
    streams_count, rows, width = x.shape
    taps = f.shape[0]
    modes = rate_t.shape[0]
    return pl.pallas_call(
        state_kernel,
        grid=(width // BLOCK,),
        in_specs=[
            pl.BlockSpec((streams_count, rows, BLOCK), lambda i: (0, 0, i)),
            pl.BlockSpec((streams_count, taps - 1, BLOCK), lambda i: (0, 0, i)),
            pl.BlockSpec((taps, streams_count, BLOCK), lambda i: (0, 0, i)),
            pl.BlockSpec((modes, BLOCK), lambda i: (0, i)),
        ],
        out_specs=[
            pl.BlockSpec((modes, SUB, BLOCK), lambda i: (0, 0, i)),
            pl.BlockSpec((modes, BLOCK), lambda i: (0, i)),
        ],
        out_shape=[
            jax.ShapeDtypeStruct((modes, SUB, width), jnp.float32),
            jax.ShapeDtypeStruct((modes, width), jnp.float32),
        ],
        scratch_shapes=[
            pltpu.VMEM((streams_count, BLOCK // LANES, rows, LANES), jnp.float32),
            pltpu.VMEM((modes, SUB, LANES), jnp.float32),
            pltpu.VMEM((taps * streams_count, SUB, LANES), jnp.float32),
        ],
    )(x, halo, f, rate_t)


def run_out_part(x, halo, f, rate_t, residue_t, skip, ends, fix, hin, first_block, prior=None):
    streams_count, rows, width = x.shape
    taps = f.shape[0]
    modes = rate_t.shape[0]
    block = min(BLOCK, hin.shape[1])

    def at(i, off):
        return off[0] + i

    in_specs = [
        pl.BlockSpec((streams_count, rows, block), lambda i, off: (0, 0, at(i, off))),
        pl.BlockSpec((streams_count, taps - 1, block), lambda i, off: (0, 0, at(i, off))),
        pl.BlockSpec((taps, streams_count, block), lambda i, off: (0, 0, at(i, off))),
        pl.BlockSpec((modes, block), lambda i, off: (0, at(i, off))),
        pl.BlockSpec((modes, block), lambda i, off: (0, at(i, off))),
        pl.BlockSpec((1, block), lambda i, off: (0, at(i, off))),
        pl.BlockSpec((modes, SUB, block), lambda i, off: (0, 0, at(i, off))),
        pl.BlockSpec((modes, block), lambda i, off: (0, at(i, off))),
        pl.BlockSpec((modes, block), lambda i, off: (0, i)),
    ]
    operands = [x, halo, f, rate_t, residue_t, skip, ends, fix, hin]
    count = len(operands)
    aliases = {}
    if prior is not None:
        in_specs.append(pl.BlockSpec(memory_space=pl.ANY))
        operands.append(prior)
        aliases = {len(operands): 0}

    def kernel(off_ref, *refs):
        out_kernel(*refs[:count], *refs[len(operands) :])

    grid_spec = pltpu.PrefetchScalarGridSpec(
        num_scalar_prefetch=1,
        grid=(hin.shape[1] // block,),
        in_specs=in_specs,
        out_specs=pl.BlockSpec((rows, block), lambda i, off: (0, at(i, off))),
        scratch_shapes=[
            pltpu.VMEM((streams_count, block // LANES, rows, LANES), jnp.float32),
            pltpu.VMEM((block // LANES, rows, LANES), jnp.float32),
            pltpu.VMEM((modes, SUB, LANES), jnp.float32),
            pltpu.VMEM((modes, SUB, LANES), jnp.float32),
            pltpu.VMEM((taps * streams_count, SUB, LANES), jnp.float32),
        ],
    )
    offset = jnp.reshape(first_block, (1,)).astype(jnp.int32)
    return pl.pallas_call(
        kernel,
        grid_spec=grid_spec,
        out_shape=jax.ShapeDtypeStruct((rows, width), jnp.bfloat16),
        input_output_aliases=aliases,
    )(offset, *operands)


def body(streams, short_filter, skip, rates, residues):
    axes = ("ctx", "tp")
    devices = lax.axis_size("ctx") * lax.axis_size("tp")
    tok_rows, streams_count, width = streams.shape
    taps = short_filter.shape[0]
    modes = rates.shape[1]

    def shift(value, offset):
        pairs = [(j, j + offset) for j in range(devices - offset)]
        return lax.ppermute(value, axes, pairs)

    halo_rows = shift(streams[tok_rows - (taps - 1) :], 1).astype(jnp.float32)
    halo = jnp.transpose(halo_rows, (1, 0, 2))
    x = jnp.transpose(streams, (1, 0, 2))
    rate_t = rates.T
    residue_t = residues.T
    ends, local = run_state(x, jnp.zeros_like(halo), short_filter, rate_t)

    head = streams[: taps - 1].astype(jnp.float32)

    def head_gate(before):
        rows = jnp.concatenate([before, head], axis=0)
        gated = []
        for t in range(taps - 1):
            feat = short_filter[0] * rows[t + taps - 1]
            for tap in range(1, taps):
                feat = feat + short_filter[tap] * rows[t + taps - 1 - tap]
            gated.append((feat[1] * feat[2]).astype(jnp.bfloat16).astype(jnp.float32))
        return gated

    seg = tok_rows // SUB
    true_head = head_gate(halo_rows)
    zero_head = head_gate(jnp.zeros_like(halo_rows))
    local_fix = None
    ends_fix = None
    for t in range(taps - 1):
        delta = (true_head[t] - zero_head[t])[None, :]
        to_end = jnp.exp(-rate_t * float(tok_rows - 1 - t)) * delta
        to_seg = jnp.exp(-rate_t * float(seg - 1 - t)) * delta
        local_fix = to_end if local_fix is None else local_fix + to_end
        ends_fix = to_seg if ends_fix is None else ends_fix + to_seg
    local = local + local_fix

    group = lax.axis_size("tp")
    spans = lax.axis_size("ctx")
    member = lax.axis_index("tp")
    piece = width // group

    def exchange(value, k):
        return lax.ppermute(value, "tp", [(q, (q + k) % group) for q in range(group)])

    def powers(rates_part, count):
        return jnp.exp(-rates_part * (float(tok_rows) * count))

    inside = None
    total = powers(rate_t, (group - 1 - member).astype(jnp.float32)) * local
    for k in range(1, group):
        other = exchange(local, k)
        source = (member - k) % group
        total = total + powers(rate_t, (group - 1 - source).astype(jnp.float32)) * other
        term = jnp.where(k <= member, powers(rate_t, float(k - 1)) * other, 0.0)
        inside = term if inside is None else inside + term
    if inside is None:
        inside = jnp.zeros_like(local)

    first_channel = member * piece
    rate_part = lax.dynamic_slice_in_dim(rate_t, first_channel, piece, 1)
    total_part = lax.dynamic_slice_in_dim(total, first_channel, piece, 1)

    def span_shift(value, offset):
        return lax.ppermute(value, "ctx", [(j, j + offset) for j in range(spans - offset)])

    def gather_window(value, spacing, count):
        gathered = None
        for k in range(1, count + 1):
            if k * spacing >= spans:
                break
            term = powers(rate_part, float(group * (k - 1) * spacing)) * span_shift(value, k * spacing)
            gathered = term if gathered is None else gathered + term
        return gathered

    if spans > 1:
        first = min(FIRST_WINDOW, spans - 1)
        before = gather_window(total_part, 1, first)
        window = first
        while window < spans - 1:
            count = min(-(-(spans - 1) // window) - 1, LATER_WINDOW)
            before = before + powers(rate_part, float(group * window)) * gather_window(before, window, count)
            window *= count + 1
    else:
        before = jnp.zeros_like(total_part)

    out = None
    for k in range(group):
        part = before if k == 0 else exchange(before, k)
        slot = (member - k) % group
        rate_slot = lax.dynamic_slice_in_dim(rate_t, slot * piece, piece, 1)
        inside_slot = lax.dynamic_slice_in_dim(inside, slot * piece, piece, 1)
        hin = powers(rate_slot, member.astype(jnp.float32)) * part + inside_slot
        out = run_out_part(
            x, halo, short_filter, rate_t, residue_t, skip.reshape(1, width), ends, ends_fix, hin,
            slot * (piece // min(BLOCK, piece)), out,
        )
    return out


def solution(mesh):
    return jax.shard_map(
        body,
        mesh=mesh,
        in_specs=(P(("ctx", "tp"), None, None), P(), P(), P(), P()),
        out_specs=P(("ctx", "tp"), None),
        check_vma=False,
    )
```

```python
import jax
import jax.numpy as jnp
from jax import lax
from jax.experimental import pallas as pl
from jax.experimental.pallas import tpu as pltpu
from jax.sharding import PartitionSpec as P

LANES = 128
SUB = 8
BLOCK = 1024
FIRST_WINDOW = 3
LATER_WINDOW = 4
UNROLL = 8


def lane_slice(c):
    return pl.ds(pl.multiple_of(c * LANES, LANES), LANES)


def row(ref, index, lanes):
    return jnp.broadcast_to(ref[pl.ds(index, 1), lanes], (SUB, LANES))


def first_prev(xs, halo_ref, c, lanes, seg, taps, sub):
    prev = []
    for back in range(1, taps):
        per_stream = []
        for s in range(xs.shape[0]):
            rows = xs[s, c, pl.ds(seg - back, SUB, stride=seg), :]
            edge = jnp.broadcast_to(halo_ref[s, pl.ds(taps - 1 - back, 1), lanes], (SUB, LANES))
            per_stream.append(jnp.where(sub == 0, edge, pltpu.roll(rows, 1, 0)))
        prev.append(per_stream)
    return prev


def fill_filters(f_ref, fsc, lanes):
    streams_count = f_ref.shape[1]
    for tap in range(f_ref.shape[0]):
        for s in range(streams_count):
            fsc[tap * streams_count + s] = row(f_ref.at[tap], s, lanes)


def step_features(xs, fsc, c, seg, j, prev):
    streams_count = xs.shape[0]
    taps = len(prev) + 1
    now = [xs[s, c, pl.ds(j, SUB, stride=seg), :] for s in range(streams_count)]
    feats = []
    for s in range(streams_count):
        acc = fsc[s] * now[s]
        for tap in range(1, taps):
            acc = acc + fsc[tap * streams_count + s] * prev[tap - 1][s]
        feats.append(acc)
    new_prev = [now] + prev[:-1]
    return feats, new_prev


def gate(feats):
    return (feats[1] * feats[2]).astype(jnp.bfloat16).astype(jnp.float32)


def state_kernel(x_ref, halo_ref, f_ref, a_ref, seg_ref, h_ref, xs, dsc, fsc):
    streams_count, rows, block = x_ref.shape
    taps = f_ref.shape[0]
    modes = a_ref.shape[0]
    seg = rows // SUB
    for c in range(block // LANES):
        xs[:, c] = x_ref[:, :, c * LANES : (c + 1) * LANES].astype(jnp.float32)
    sub = lax.broadcasted_iota(jnp.int32, (SUB, LANES), 0)

    def lane_group(c, carry):
        lanes = lane_slice(c)
        fill_filters(f_ref, fsc, lanes)
        for m in range(modes):
            dsc[m] = jnp.exp(-row(a_ref, m, lanes))

        def step(j, state):
            prev, states = state
            feats, prev = step_features(xs, fsc, c, seg, j, prev)
            u = gate(feats)
            return prev, tuple(dsc[m] * states[m] + u for m in range(modes))

        zero = jnp.zeros((SUB, LANES), jnp.float32)
        init = (first_prev(xs, halo_ref, c, lanes, seg, taps, sub), (zero,) * modes)
        _, states = lax.fori_loop(0, seg, step, init, unroll=UNROLL)
        later = (SUB - 1 - sub).astype(jnp.float32) * float(seg)
        for m in range(modes):
            seg_ref[m, :, lanes] = states[m]
            weight = jnp.exp(-row(a_ref, m, lanes) * later)
            h_ref[pl.ds(m, 1), lanes] = jnp.sum(weight * states[m], axis=0, keepdims=True)
        return carry

    lax.fori_loop(0, block // LANES, lane_group, 0)


def out_kernel(
    x_ref, halo_ref, f_ref, a_ref, r_ref, skip_ref, seg_ref, fix_ref, hin_ref, o_ref, xs, ys, dsc, rsc, fsc
):
    streams_count, rows, block = x_ref.shape
    taps = f_ref.shape[0]
    modes = a_ref.shape[0]
    seg = rows // SUB
    for c in range(block // LANES):
        xs[:, c] = x_ref[:, :, c * LANES : (c + 1) * LANES].astype(jnp.float32)
    sub = lax.broadcasted_iota(jnp.int32, (SUB, LANES), 0)

    def lane_group(c, carry):
        lanes = lane_slice(c)
        fill_filters(f_ref, fsc, lanes)
        starts = []
        for m in range(modes):
            rate = row(a_ref, m, lanes)
            dsc[m] = jnp.exp(-rate)
            rsc[m] = row(r_ref, m, lanes)
            ends = seg_ref[m, :, lanes] + jnp.where(sub == 0, row(fix_ref, m, lanes), 0.0)
            carried = jnp.where(sub >= 1, pltpu.roll(ends, 1, 0), 0.0)
            offset = 1
            while offset < SUB:
                factor = jnp.exp(-rate * float(seg * offset))
                carried = carried + jnp.where(sub >= offset, factor * pltpu.roll(carried, offset, 0), 0.0)
                offset *= 2
            lead = jnp.exp(-rate * (sub.astype(jnp.float32) * float(seg)))
            starts.append(carried + lead * row(hin_ref, m, lanes))
        skip_rows = row(skip_ref, 0, lanes)

        def step(j, state):
            prev, states = state
            feats, prev = step_features(xs, fsc, c, seg, j, prev)
            u = gate(feats)
            new = [dsc[m] * states[m] + u for m in range(modes)]
            terms = [rsc[m] * new[m] for m in range(modes)]
            while len(terms) > 1:
                paired = [terms[i] + terms[i + 1] for i in range(0, len(terms) - 1, 2)]
                terms = paired + terms[len(terms) - len(terms) % 2 :]
            conv = terms[0]
            y = (conv + skip_rows * u).astype(jnp.bfloat16).astype(jnp.float32)
            ys[c, pl.ds(j, SUB, stride=seg), :] = feats[0] * y
            return prev, tuple(new)

        init = (first_prev(xs, halo_ref, c, lanes, seg, taps, sub), tuple(starts))
        lax.fori_loop(0, seg, step, init, unroll=UNROLL)
        return carry

    lax.fori_loop(0, block // LANES, lane_group, 0)
    for c in range(block // LANES):
        o_ref[:, c * LANES : (c + 1) * LANES] = ys[c].astype(o_ref.dtype)


def run_state(x, halo, f, rate_t):
    streams_count, rows, width = x.shape
    taps = f.shape[0]
    modes = rate_t.shape[0]
    return pl.pallas_call(
        state_kernel,
        grid=(width // BLOCK,),
        in_specs=[
            pl.BlockSpec((streams_count, rows, BLOCK), lambda i: (0, 0, i)),
            pl.BlockSpec((streams_count, taps - 1, BLOCK), lambda i: (0, 0, i)),
            pl.BlockSpec((taps, streams_count, BLOCK), lambda i: (0, 0, i)),
            pl.BlockSpec((modes, BLOCK), lambda i: (0, i)),
        ],
        out_specs=[
            pl.BlockSpec((modes, SUB, BLOCK), lambda i: (0, 0, i)),
            pl.BlockSpec((modes, BLOCK), lambda i: (0, i)),
        ],
        out_shape=[
            jax.ShapeDtypeStruct((modes, SUB, width), jnp.float32),
            jax.ShapeDtypeStruct((modes, width), jnp.float32),
        ],
        scratch_shapes=[
            pltpu.VMEM((streams_count, BLOCK // LANES, rows, LANES), jnp.float32),
            pltpu.VMEM((modes, SUB, LANES), jnp.float32),
            pltpu.VMEM((taps * streams_count, SUB, LANES), jnp.float32),
        ],
    )(x, halo, f, rate_t)


def run_out(x, halo, f, rate_t, residue_t, skip, ends, fix, hin):
    streams_count, rows, width = x.shape
    taps = f.shape[0]
    modes = rate_t.shape[0]
    return pl.pallas_call(
        out_kernel,
        grid=(width // BLOCK,),
        in_specs=[
            pl.BlockSpec((streams_count, rows, BLOCK), lambda i: (0, 0, i)),
            pl.BlockSpec((streams_count, taps - 1, BLOCK), lambda i: (0, 0, i)),
            pl.BlockSpec((taps, streams_count, BLOCK), lambda i: (0, 0, i)),
            pl.BlockSpec((modes, BLOCK), lambda i: (0, i)),
            pl.BlockSpec((modes, BLOCK), lambda i: (0, i)),
            pl.BlockSpec((1, BLOCK), lambda i: (0, i)),
            pl.BlockSpec((modes, SUB, BLOCK), lambda i: (0, 0, i)),
            pl.BlockSpec((modes, BLOCK), lambda i: (0, i)),
            pl.BlockSpec((modes, BLOCK), lambda i: (0, i)),
        ],
        out_specs=pl.BlockSpec((rows, BLOCK), lambda i: (0, i)),
        out_shape=jax.ShapeDtypeStruct((rows, width), jnp.bfloat16),
        scratch_shapes=[
            pltpu.VMEM((streams_count, BLOCK // LANES, rows, LANES), jnp.float32),
            pltpu.VMEM((BLOCK // LANES, rows, LANES), jnp.float32),
            pltpu.VMEM((modes, SUB, LANES), jnp.float32),
            pltpu.VMEM((modes, SUB, LANES), jnp.float32),
            pltpu.VMEM((taps * streams_count, SUB, LANES), jnp.float32),
        ],
    )(x, halo, f, rate_t, residue_t, skip, ends, fix, hin)


def body(streams, short_filter, skip, rates, residues):
    axes = ("ctx", "tp")
    devices = lax.axis_size("ctx") * lax.axis_size("tp")
    tok_rows, streams_count, width = streams.shape
    taps = short_filter.shape[0]
    modes = rates.shape[1]

    def shift(value, offset):
        pairs = [(j, j + offset) for j in range(devices - offset)]
        return lax.ppermute(value, axes, pairs)

    x = jnp.transpose(streams, (1, 0, 2))
    rate_t = rates.T
    residue_t = residues.T
    zero_halo = jnp.zeros((streams_count, taps - 1, width), jnp.float32)
    ends, local = run_state(x, zero_halo, short_filter, rate_t)
    tail, local = lax.optimization_barrier((streams[tok_rows - (taps - 1) :], local))
    halo_rows = shift(tail, 1).astype(jnp.float32)
    halo = jnp.transpose(halo_rows, (1, 0, 2))

    head = streams[: taps - 1].astype(jnp.float32)

    def head_gate(before):
        rows = jnp.concatenate([before, head], axis=0)
        gated = []
        for t in range(taps - 1):
            feat = short_filter[0] * rows[t + taps - 1]
            for tap in range(1, taps):
                feat = feat + short_filter[tap] * rows[t + taps - 1 - tap]
            gated.append((feat[1] * feat[2]).astype(jnp.bfloat16).astype(jnp.float32))
        return gated

    seg = tok_rows // SUB
    true_head = head_gate(halo_rows)
    zero_head = head_gate(jnp.zeros_like(halo_rows))
    local_fix = None
    ends_fix = None
    for t in range(taps - 1):
        delta = (true_head[t] - zero_head[t])[None, :]
        to_end = jnp.exp(-rate_t * float(tok_rows - 1 - t)) * delta
        to_seg = jnp.exp(-rate_t * float(seg - 1 - t)) * delta
        local_fix = to_end if local_fix is None else local_fix + to_end
        ends_fix = to_seg if ends_fix is None else ends_fix + to_seg
    local = local + local_fix

    group = lax.axis_size("tp")
    spans = lax.axis_size("ctx")
    member = lax.axis_index("tp")
    piece = width // group

    def exchange(value, k):
        return lax.ppermute(value, "tp", [(q, (q + k) % group) for q in range(group)])

    def powers(rates_part, count):
        return jnp.exp(-rates_part * (float(tok_rows) * count))

    inside = None
    total = powers(rate_t, (group - 1 - member).astype(jnp.float32)) * local
    for k in range(1, group):
        other = exchange(local, k)
        source = (member - k) % group
        total = total + powers(rate_t, (group - 1 - source).astype(jnp.float32)) * other
        term = jnp.where(k <= member, powers(rate_t, float(k - 1)) * other, 0.0)
        inside = term if inside is None else inside + term
    if inside is None:
        inside = jnp.zeros_like(local)

    first_channel = member * piece
    rate_part = lax.dynamic_slice_in_dim(rate_t, first_channel, piece, 1)
    total_part = lax.dynamic_slice_in_dim(total, first_channel, piece, 1)

    def span_shift(value, offset):
        return lax.ppermute(value, "ctx", [(j, j + offset) for j in range(spans - offset)])

    def gather_window(value, spacing, count):
        gathered = None
        for k in range(1, count + 1):
            if k * spacing >= spans:
                break
            term = powers(rate_part, float(group * (k - 1) * spacing)) * span_shift(value, k * spacing)
            gathered = term if gathered is None else gathered + term
        return gathered

    if spans > 1:
        first = min(FIRST_WINDOW, spans - 1)
        before = gather_window(total_part, 1, first)
        window = first
        while window < spans - 1:
            count = min(-(-(spans - 1) // window) - 1, LATER_WINDOW)
            before = before + powers(rate_part, float(group * window)) * gather_window(before, window, count)
            window *= count + 1
    else:
        before = jnp.zeros_like(total_part)

    whole = jnp.zeros_like(local)
    for k in range(group):
        part = before if k == 0 else exchange(before, k)
        whole = lax.dynamic_update_slice_in_dim(whole, part, ((member - k) % group) * piece, 1)
    carried = powers(rate_t, member.astype(jnp.float32)) * whole + inside

    return run_out(x, halo, short_filter, rate_t, residue_t, skip.reshape(1, width), ends, ends_fix, carried)


def solution(mesh):
    return jax.shard_map(
        body,
        mesh=mesh,
        in_specs=(P(("ctx", "tp"), None, None), P(), P(), P(), P()),
        out_specs=P(("ctx", "tp"), None),
        check_vma=False,
    )
```

```python
import jax
import jax.numpy as jnp
from jax import lax
from jax.experimental import pallas as pl
from jax.experimental.pallas import tpu as pltpu
from jax.sharding import PartitionSpec as P

LANES = 128
SUB = 8
BLOCK = 1024
FIRST_WINDOW = 4
LATER_WINDOW = 3
UNROLL = 8


def lane_slice(c):
    return pl.ds(pl.multiple_of(c * LANES, LANES), LANES)


def row(ref, index, lanes):
    return jnp.broadcast_to(ref[pl.ds(index, 1), lanes], (SUB, LANES))


def first_prev(xs, halo_ref, c, lanes, seg, taps, sub):
    prev = []
    for back in range(1, taps):
        per_stream = []
        for s in range(xs.shape[0]):
            rows = xs[s, c, pl.ds(seg - back, SUB, stride=seg), :]
            edge = jnp.broadcast_to(halo_ref[s, pl.ds(taps - 1 - back, 1), lanes], (SUB, LANES))
            per_stream.append(jnp.where(sub == 0, edge, pltpu.roll(rows, 1, 0)))
        prev.append(per_stream)
    return prev


def fill_filters(f_ref, fsc, lanes):
    streams_count = f_ref.shape[1]
    for tap in range(f_ref.shape[0]):
        for s in range(streams_count):
            fsc[tap * streams_count + s] = row(f_ref.at[tap], s, lanes)


def step_features(xs, fsc, c, seg, j, prev):
    streams_count = xs.shape[0]
    taps = len(prev) + 1
    now = [xs[s, c, pl.ds(j, SUB, stride=seg), :] for s in range(streams_count)]
    feats = []
    for s in range(streams_count):
        acc = fsc[s] * now[s]
        for tap in range(1, taps):
            acc = acc + fsc[tap * streams_count + s] * prev[tap - 1][s]
        feats.append(acc)
    new_prev = [now] + prev[:-1]
    return feats, new_prev


def gate(feats):
    return (feats[1] * feats[2]).astype(jnp.bfloat16).astype(jnp.float32)


def state_kernel(x_ref, halo_ref, f_ref, a_ref, seg_ref, h_ref, xs, dsc, fsc):
    streams_count, rows, block = x_ref.shape
    taps = f_ref.shape[0]
    modes = a_ref.shape[0]
    seg = rows // SUB
    for c in range(block // LANES):
        xs[:, c] = x_ref[:, :, c * LANES : (c + 1) * LANES].astype(jnp.float32)
    sub = lax.broadcasted_iota(jnp.int32, (SUB, LANES), 0)

    def lane_group(c, carry):
        lanes = lane_slice(c)
        fill_filters(f_ref, fsc, lanes)
        for m in range(modes):
            dsc[m] = jnp.exp(-row(a_ref, m, lanes))

        def step(j, state):
            prev, states = state
            feats, prev = step_features(xs, fsc, c, seg, j, prev)
            u = gate(feats)
            return prev, tuple(dsc[m] * states[m] + u for m in range(modes))

        zero = jnp.zeros((SUB, LANES), jnp.float32)
        init = (first_prev(xs, halo_ref, c, lanes, seg, taps, sub), (zero,) * modes)
        _, states = lax.fori_loop(0, seg, step, init, unroll=UNROLL)
        later = (SUB - 1 - sub).astype(jnp.float32) * float(seg)
        for m in range(modes):
            seg_ref[m, :, lanes] = states[m]
            weight = jnp.exp(-row(a_ref, m, lanes) * later)
            h_ref[pl.ds(m, 1), lanes] = jnp.sum(weight * states[m], axis=0, keepdims=True)
        return carry

    lax.fori_loop(0, block // LANES, lane_group, 0)


def out_kernel(
    x_ref, halo_ref, f_ref, a_ref, r_ref, skip_ref, seg_ref, fix_ref, hin_ref, o_ref, xs, ys, dsc, rsc, fsc
):
    streams_count, rows, block = x_ref.shape
    taps = f_ref.shape[0]
    modes = a_ref.shape[0]
    seg = rows // SUB
    for c in range(block // LANES):
        xs[:, c] = x_ref[:, :, c * LANES : (c + 1) * LANES].astype(jnp.float32)
    sub = lax.broadcasted_iota(jnp.int32, (SUB, LANES), 0)

    def lane_group(c, carry):
        lanes = lane_slice(c)
        fill_filters(f_ref, fsc, lanes)
        starts = []
        for m in range(modes):
            rate = row(a_ref, m, lanes)
            dsc[m] = jnp.exp(-rate)
            rsc[m] = row(r_ref, m, lanes)
            ends = seg_ref[m, :, lanes] + jnp.where(sub == 0, row(fix_ref, m, lanes), 0.0)
            carried = jnp.where(sub >= 1, pltpu.roll(ends, 1, 0), 0.0)
            offset = 1
            while offset < SUB:
                factor = jnp.exp(-rate * float(seg * offset))
                carried = carried + jnp.where(sub >= offset, factor * pltpu.roll(carried, offset, 0), 0.0)
                offset *= 2
            lead = jnp.exp(-rate * (sub.astype(jnp.float32) * float(seg)))
            starts.append(carried + lead * row(hin_ref, m, lanes))
        skip_rows = row(skip_ref, 0, lanes)

        def step(j, state):
            prev, states = state
            feats, prev = step_features(xs, fsc, c, seg, j, prev)
            u = gate(feats)
            new = [dsc[m] * states[m] + u for m in range(modes)]
            terms = [rsc[m] * new[m] for m in range(modes)]
            while len(terms) > 1:
                paired = [terms[i] + terms[i + 1] for i in range(0, len(terms) - 1, 2)]
                terms = paired + terms[len(terms) - len(terms) % 2 :]
            conv = terms[0]
            y = (conv + skip_rows * u).astype(jnp.bfloat16).astype(jnp.float32)
            ys[c, pl.ds(j, SUB, stride=seg), :] = feats[0] * y
            return prev, tuple(new)

        init = (first_prev(xs, halo_ref, c, lanes, seg, taps, sub), tuple(starts))
        lax.fori_loop(0, seg, step, init, unroll=UNROLL)
        return carry

    lax.fori_loop(0, block // LANES, lane_group, 0)
    for c in range(block // LANES):
        o_ref[:, c * LANES : (c + 1) * LANES] = ys[c].astype(o_ref.dtype)


def run_state(x, halo, f, rate_t):
    streams_count, rows, width = x.shape
    taps = f.shape[0]
    modes = rate_t.shape[0]
    return pl.pallas_call(
        state_kernel,
        grid=(width // BLOCK,),
        in_specs=[
            pl.BlockSpec((streams_count, rows, BLOCK), lambda i: (0, 0, i)),
            pl.BlockSpec((streams_count, taps - 1, BLOCK), lambda i: (0, 0, i)),
            pl.BlockSpec((taps, streams_count, BLOCK), lambda i: (0, 0, i)),
            pl.BlockSpec((modes, BLOCK), lambda i: (0, i)),
        ],
        out_specs=[
            pl.BlockSpec((modes, SUB, BLOCK), lambda i: (0, 0, i)),
            pl.BlockSpec((modes, BLOCK), lambda i: (0, i)),
        ],
        out_shape=[
            jax.ShapeDtypeStruct((modes, SUB, width), jnp.float32),
            jax.ShapeDtypeStruct((modes, width), jnp.float32),
        ],
        scratch_shapes=[
            pltpu.VMEM((streams_count, BLOCK // LANES, rows, LANES), jnp.float32),
            pltpu.VMEM((modes, SUB, LANES), jnp.float32),
            pltpu.VMEM((taps * streams_count, SUB, LANES), jnp.float32),
        ],
    )(x, halo, f, rate_t)


def run_out(x, halo, f, rate_t, residue_t, skip, ends, fix, hin):
    streams_count, rows, width = x.shape
    taps = f.shape[0]
    modes = rate_t.shape[0]
    return pl.pallas_call(
        out_kernel,
        grid=(width // BLOCK,),
        in_specs=[
            pl.BlockSpec((streams_count, rows, BLOCK), lambda i: (0, 0, i)),
            pl.BlockSpec((streams_count, taps - 1, BLOCK), lambda i: (0, 0, i)),
            pl.BlockSpec((taps, streams_count, BLOCK), lambda i: (0, 0, i)),
            pl.BlockSpec((modes, BLOCK), lambda i: (0, i)),
            pl.BlockSpec((modes, BLOCK), lambda i: (0, i)),
            pl.BlockSpec((1, BLOCK), lambda i: (0, i)),
            pl.BlockSpec((modes, SUB, BLOCK), lambda i: (0, 0, i)),
            pl.BlockSpec((modes, BLOCK), lambda i: (0, i)),
            pl.BlockSpec((modes, BLOCK), lambda i: (0, i)),
        ],
        out_specs=pl.BlockSpec((rows, BLOCK), lambda i: (0, i)),
        out_shape=jax.ShapeDtypeStruct((rows, width), jnp.bfloat16),
        scratch_shapes=[
            pltpu.VMEM((streams_count, BLOCK // LANES, rows, LANES), jnp.float32),
            pltpu.VMEM((BLOCK // LANES, rows, LANES), jnp.float32),
            pltpu.VMEM((modes, SUB, LANES), jnp.float32),
            pltpu.VMEM((modes, SUB, LANES), jnp.float32),
            pltpu.VMEM((taps * streams_count, SUB, LANES), jnp.float32),
        ],
    )(x, halo, f, rate_t, residue_t, skip, ends, fix, hin)


def body(streams, short_filter, skip, rates, residues):
    axes = ("ctx", "tp")
    devices = lax.axis_size("ctx") * lax.axis_size("tp")
    tok_rows, streams_count, width = streams.shape
    taps = short_filter.shape[0]
    modes = rates.shape[1]

    def shift(value, offset):
        pairs = [(j, j + offset) for j in range(devices - offset)]
        return lax.ppermute(value, axes, pairs)

    halo_rows = shift(streams[tok_rows - (taps - 1) :], 1).astype(jnp.float32)
    halo = jnp.transpose(halo_rows, (1, 0, 2))
    x = jnp.transpose(streams, (1, 0, 2))
    rate_t = rates.T
    residue_t = residues.T
    ends, local = run_state(x, jnp.zeros_like(halo), short_filter, rate_t)

    head = streams[: taps - 1].astype(jnp.float32)

    def head_gate(before):
        rows = jnp.concatenate([before, head], axis=0)
        gated = []
        for t in range(taps - 1):
            feat = short_filter[0] * rows[t + taps - 1]
            for tap in range(1, taps):
                feat = feat + short_filter[tap] * rows[t + taps - 1 - tap]
            gated.append((feat[1] * feat[2]).astype(jnp.bfloat16).astype(jnp.float32))
        return gated

    seg = tok_rows // SUB
    true_head = head_gate(halo_rows)
    zero_head = head_gate(jnp.zeros_like(halo_rows))
    local_fix = None
    ends_fix = None
    for t in range(taps - 1):
        delta = (true_head[t] - zero_head[t])[None, :]
        to_end = jnp.exp(-rate_t * float(tok_rows - 1 - t)) * delta
        to_seg = jnp.exp(-rate_t * float(seg - 1 - t)) * delta
        local_fix = to_end if local_fix is None else local_fix + to_end
        ends_fix = to_seg if ends_fix is None else ends_fix + to_seg
    local = local + local_fix

    group = lax.axis_size("tp")
    spans = lax.axis_size("ctx")
    member = lax.axis_index("tp")
    piece = width // group

    def exchange(value, k):
        return lax.ppermute(value, "tp", [(q, (q + k) % group) for q in range(group)])

    def powers(rates_part, count):
        return jnp.exp(-rates_part * (float(tok_rows) * count))

    inside = None
    total = powers(rate_t, (group - 1 - member).astype(jnp.float32)) * local
    for k in range(1, group):
        other = exchange(local, k)
        source = (member - k) % group
        total = total + powers(rate_t, (group - 1 - source).astype(jnp.float32)) * other
        term = jnp.where(k <= member, powers(rate_t, float(k - 1)) * other, 0.0)
        inside = term if inside is None else inside + term
    if inside is None:
        inside = jnp.zeros_like(local)

    first_channel = member * piece
    rate_part = lax.dynamic_slice_in_dim(rate_t, first_channel, piece, 1)
    total_part = lax.dynamic_slice_in_dim(total, first_channel, piece, 1)

    def span_shift(value, offset):
        return lax.ppermute(value, "ctx", [(j, j + offset) for j in range(spans - offset)])

    def gather_window(value, spacing, count):
        gathered = None
        for k in range(1, count + 1):
            if k * spacing >= spans:
                break
            term = powers(rate_part, float(group * (k - 1) * spacing)) * span_shift(value, k * spacing)
            gathered = term if gathered is None else gathered + term
        return gathered

    if spans > 1:
        first = min(FIRST_WINDOW, spans - 1)
        before = gather_window(total_part, 1, first)
        window = first
        while window < spans - 1:
            count = min(-(-(spans - 1) // window) - 1, LATER_WINDOW)
            before = before + powers(rate_part, float(group * window)) * gather_window(before, window, count)
            window *= count + 1
    else:
        before = jnp.zeros_like(total_part)

    whole = jnp.zeros_like(local)
    for k in range(group):
        part = before if k == 0 else exchange(before, k)
        whole = lax.dynamic_update_slice_in_dim(whole, part, ((member - k) % group) * piece, 1)
    carried = powers(rate_t, member.astype(jnp.float32)) * whole + inside

    return run_out(x, halo, short_filter, rate_t, residue_t, skip.reshape(1, width), ends, ends_fix, carried)


def solution(mesh):
    return jax.shard_map(
        body,
        mesh=mesh,
        in_specs=(P(("ctx", "tp"), None, None), P(), P(), P(), P()),
        out_specs=P(("ctx", "tp"), None),
        check_vma=False,
    )
```

```python
import jax
import jax.numpy as jnp
from jax import lax
from jax.experimental import pallas as pl
from jax.experimental.pallas import tpu as pltpu
from jax.sharding import PartitionSpec as P

LANES = 128
SUB = 8
BLOCK = 1024
FIRST_WINDOW = 3
LATER_WINDOW = 4
UNROLL = 8


def lane_slice(c):
    return pl.ds(pl.multiple_of(c * LANES, LANES), LANES)


def row(ref, index, lanes):
    return jnp.broadcast_to(ref[pl.ds(index, 1), lanes], (SUB, LANES))


def first_prev(xs, halo_ref, c, lanes, seg, taps, sub):
    prev = []
    for back in range(1, taps):
        per_stream = []
        for s in range(xs.shape[0]):
            rows = xs[s, c, pl.ds(seg - back, SUB, stride=seg), :]
            edge = jnp.broadcast_to(halo_ref[s, pl.ds(taps - 1 - back, 1), lanes], (SUB, LANES))
            per_stream.append(jnp.where(sub == 0, edge, pltpu.roll(rows, 1, 0)))
        prev.append(per_stream)
    return prev


def fill_filters(f_ref, fsc, lanes):
    streams_count = f_ref.shape[1]
    for tap in range(f_ref.shape[0]):
        for s in range(streams_count):
            fsc[tap * streams_count + s] = row(f_ref.at[tap], s, lanes)


def step_features(xs, fsc, c, seg, j, prev):
    streams_count = xs.shape[0]
    taps = len(prev) + 1
    now = [xs[s, c, pl.ds(j, SUB, stride=seg), :] for s in range(streams_count)]
    feats = []
    for s in range(streams_count):
        acc = fsc[s] * now[s]
        for tap in range(1, taps):
            acc = acc + fsc[tap * streams_count + s] * prev[tap - 1][s]
        feats.append(acc)
    new_prev = [now] + prev[:-1]
    return feats, new_prev


def gate(feats):
    return (feats[1] * feats[2]).astype(jnp.bfloat16).astype(jnp.float32)


def state_kernel(x_ref, halo_ref, f_ref, a_ref, seg_ref, h_ref, xs, dsc, fsc):
    streams_count, rows, block = x_ref.shape
    taps = f_ref.shape[0]
    modes = a_ref.shape[0]
    seg = rows // SUB
    for c in range(block // LANES):
        xs[:, c] = x_ref[:, :, c * LANES : (c + 1) * LANES].astype(jnp.float32)
    sub = lax.broadcasted_iota(jnp.int32, (SUB, LANES), 0)

    def lane_group(c, carry):
        lanes = lane_slice(c)
        fill_filters(f_ref, fsc, lanes)
        for m in range(modes):
            dsc[m] = jnp.exp(-row(a_ref, m, lanes))

        def step(j, state):
            prev, states = state
            feats, prev = step_features(xs, fsc, c, seg, j, prev)
            u = gate(feats)
            return prev, tuple(dsc[m] * states[m] + u for m in range(modes))

        zero = jnp.zeros((SUB, LANES), jnp.float32)
        init = (first_prev(xs, halo_ref, c, lanes, seg, taps, sub), (zero,) * modes)
        _, states = lax.fori_loop(0, seg, step, init, unroll=UNROLL)
        later = (SUB - 1 - sub).astype(jnp.float32) * float(seg)
        for m in range(modes):
            seg_ref[m, :, lanes] = states[m]
            weight = jnp.exp(-row(a_ref, m, lanes) * later)
            h_ref[pl.ds(m, 1), lanes] = jnp.sum(weight * states[m], axis=0, keepdims=True)
        return carry

    lax.fori_loop(0, block // LANES, lane_group, 0)


def out_kernel(
    x_ref, halo_ref, f_ref, a_ref, r_ref, skip_ref, seg_ref, fix_ref, hin_ref, o_ref, xs, ys, dsc, rsc, fsc
):
    streams_count, rows, block = x_ref.shape
    taps = f_ref.shape[0]
    modes = a_ref.shape[0]
    seg = rows // SUB
    for c in range(block // LANES):
        xs[:, c] = x_ref[:, :, c * LANES : (c + 1) * LANES].astype(jnp.float32)
    sub = lax.broadcasted_iota(jnp.int32, (SUB, LANES), 0)

    def lane_group(c, carry):
        lanes = lane_slice(c)
        fill_filters(f_ref, fsc, lanes)
        starts = []
        for m in range(modes):
            rate = row(a_ref, m, lanes)
            dsc[m] = jnp.exp(-rate)
            rsc[m] = row(r_ref, m, lanes)
            ends = seg_ref[m, :, lanes] + jnp.where(sub == 0, row(fix_ref, m, lanes), 0.0)
            carried = jnp.where(sub >= 1, pltpu.roll(ends, 1, 0), 0.0)
            offset = 1
            while offset < SUB:
                factor = jnp.exp(-rate * float(seg * offset))
                carried = carried + jnp.where(sub >= offset, factor * pltpu.roll(carried, offset, 0), 0.0)
                offset *= 2
            lead = jnp.exp(-rate * (sub.astype(jnp.float32) * float(seg)))
            starts.append(carried + lead * row(hin_ref, m, lanes))
        skip_rows = row(skip_ref, 0, lanes)

        def step(j, state):
            prev, states = state
            feats, prev = step_features(xs, fsc, c, seg, j, prev)
            u = gate(feats)
            new = [dsc[m] * states[m] + u for m in range(modes)]
            terms = [rsc[m] * new[m] for m in range(modes)]
            while len(terms) > 1:
                paired = [terms[i] + terms[i + 1] for i in range(0, len(terms) - 1, 2)]
                terms = paired + terms[len(terms) - len(terms) % 2 :]
            conv = terms[0]
            y = (conv + skip_rows * u).astype(jnp.bfloat16).astype(jnp.float32)
            ys[c, pl.ds(j, SUB, stride=seg), :] = feats[0] * y
            return prev, tuple(new)

        init = (first_prev(xs, halo_ref, c, lanes, seg, taps, sub), tuple(starts))
        lax.fori_loop(0, seg, step, init, unroll=UNROLL)
        return carry

    lax.fori_loop(0, block // LANES, lane_group, 0)
    for c in range(block // LANES):
        o_ref[:, c * LANES : (c + 1) * LANES] = ys[c].astype(o_ref.dtype)


def run_state(x, halo, f, rate_t):
    streams_count, rows, width = x.shape
    taps = f.shape[0]
    modes = rate_t.shape[0]
    return pl.pallas_call(
        state_kernel,
        grid=(width // BLOCK,),
        in_specs=[
            pl.BlockSpec((streams_count, rows, BLOCK), lambda i: (0, 0, i)),
            pl.BlockSpec((streams_count, taps - 1, BLOCK), lambda i: (0, 0, i)),
            pl.BlockSpec((taps, streams_count, BLOCK), lambda i: (0, 0, i)),
            pl.BlockSpec((modes, BLOCK), lambda i: (0, i)),
        ],
        out_specs=[
            pl.BlockSpec((modes, SUB, BLOCK), lambda i: (0, 0, i)),
            pl.BlockSpec((modes, BLOCK), lambda i: (0, i)),
        ],
        out_shape=[
            jax.ShapeDtypeStruct((modes, SUB, width), jnp.float32),
            jax.ShapeDtypeStruct((modes, width), jnp.float32),
        ],
        scratch_shapes=[
            pltpu.VMEM((streams_count, BLOCK // LANES, rows, LANES), jnp.float32),
            pltpu.VMEM((modes, SUB, LANES), jnp.float32),
            pltpu.VMEM((taps * streams_count, SUB, LANES), jnp.float32),
        ],
    )(x, halo, f, rate_t)


def run_out(x, halo, f, rate_t, residue_t, skip, ends, fix, hin):
    streams_count, rows, width = x.shape
    taps = f.shape[0]
    modes = rate_t.shape[0]
    return pl.pallas_call(
        out_kernel,
        grid=(width // BLOCK,),
        in_specs=[
            pl.BlockSpec((streams_count, rows, BLOCK), lambda i: (0, 0, i)),
            pl.BlockSpec((streams_count, taps - 1, BLOCK), lambda i: (0, 0, i)),
            pl.BlockSpec((taps, streams_count, BLOCK), lambda i: (0, 0, i)),
            pl.BlockSpec((modes, BLOCK), lambda i: (0, i)),
            pl.BlockSpec((modes, BLOCK), lambda i: (0, i)),
            pl.BlockSpec((1, BLOCK), lambda i: (0, i)),
            pl.BlockSpec((modes, SUB, BLOCK), lambda i: (0, 0, i)),
            pl.BlockSpec((modes, BLOCK), lambda i: (0, i)),
            pl.BlockSpec((modes, BLOCK), lambda i: (0, i)),
        ],
        out_specs=pl.BlockSpec((rows, BLOCK), lambda i: (0, i)),
        out_shape=jax.ShapeDtypeStruct((rows, width), jnp.bfloat16),
        scratch_shapes=[
            pltpu.VMEM((streams_count, BLOCK // LANES, rows, LANES), jnp.float32),
            pltpu.VMEM((BLOCK // LANES, rows, LANES), jnp.float32),
            pltpu.VMEM((modes, SUB, LANES), jnp.float32),
            pltpu.VMEM((modes, SUB, LANES), jnp.float32),
            pltpu.VMEM((taps * streams_count, SUB, LANES), jnp.float32),
        ],
    )(x, halo, f, rate_t, residue_t, skip, ends, fix, hin)


def body(streams, short_filter, skip, rates, residues):
    axes = ("ctx", "tp")
    devices = lax.axis_size("ctx") * lax.axis_size("tp")
    tok_rows, streams_count, width = streams.shape
    taps = short_filter.shape[0]
    modes = rates.shape[1]

    def shift(value, offset):
        pairs = [(j, j + offset) for j in range(devices - offset)]
        return lax.ppermute(value, axes, pairs)

    halo_rows = shift(streams[tok_rows - (taps - 1) :], 1).astype(jnp.float32)
    halo = jnp.transpose(halo_rows, (1, 0, 2))
    x = jnp.transpose(streams, (1, 0, 2))
    rate_t = rates.T
    residue_t = residues.T
    ends, local = run_state(x, jnp.zeros_like(halo), short_filter, rate_t)

    head = streams[: taps - 1].astype(jnp.float32)

    def head_gate(before):
        rows = jnp.concatenate([before, head], axis=0)
        gated = []
        for t in range(taps - 1):
            feat = short_filter[0] * rows[t + taps - 1]
            for tap in range(1, taps):
                feat = feat + short_filter[tap] * rows[t + taps - 1 - tap]
            gated.append((feat[1] * feat[2]).astype(jnp.bfloat16).astype(jnp.float32))
        return gated

    seg = tok_rows // SUB
    true_head = head_gate(halo_rows)
    zero_head = head_gate(jnp.zeros_like(halo_rows))
    local_fix = None
    ends_fix = None
    for t in range(taps - 1):
        delta = (true_head[t] - zero_head[t])[None, :]
        to_end = jnp.exp(-rate_t * float(tok_rows - 1 - t)) * delta
        to_seg = jnp.exp(-rate_t * float(seg - 1 - t)) * delta
        local_fix = to_end if local_fix is None else local_fix + to_end
        ends_fix = to_seg if ends_fix is None else ends_fix + to_seg
    local = local + local_fix

    group = lax.axis_size("tp")
    spans = lax.axis_size("ctx")
    member = lax.axis_index("tp")
    piece = width // group

    def exchange(value, k):
        return lax.ppermute(value, "tp", [(q, (q + k) % group) for q in range(group)])

    def powers(rates_part, count):
        return jnp.exp(-rates_part * (float(tok_rows) * count))

    def cut(value, slot):
        return lax.dynamic_slice_in_dim(value, slot * piece, piece, 1)

    first_channel = member * piece
    rate_part = lax.dynamic_slice_in_dim(rate_t, first_channel, piece, 1)
    pieces = {0: cut(local, member)}
    for k in range(1, group):
        pieces[k] = exchange(cut(local, (member + k) % group), k)
    sources = {k: (member - k) % group for k in range(group)}

    def level(count):
        return count.astype(jnp.float32) if hasattr(count, "astype") else float(count)

    total_part = None
    for k in range(group):
        term = powers(rate_part, level(group - 1 - sources[k])) * pieces[k]
        total_part = term if total_part is None else total_part + term

    def span_shift(value, offset):
        return lax.ppermute(value, "ctx", [(j, j + offset) for j in range(spans - offset)])

    def gather_window(value, spacing, count):
        gathered = None
        for k in range(1, count + 1):
            if k * spacing >= spans:
                break
            term = powers(rate_part, float(group * (k - 1) * spacing)) * span_shift(value, k * spacing)
            gathered = term if gathered is None else gathered + term
        return gathered

    if spans > 1:
        first = min(FIRST_WINDOW, spans - 1)
        before = gather_window(total_part, 1, first)
        window = first
        while window < spans - 1:
            count = min(-(-(spans - 1) // window) - 1, LATER_WINDOW)
            before = before + powers(rate_part, float(group * window)) * gather_window(before, window, count)
            window *= count + 1
    else:
        before = jnp.zeros_like(total_part)

    whole = None
    for k in range(group):
        target = (member + k) % group
        start = powers(rate_part, level(target)) * before
        for j in range(group):
            ahead = target - 1 - sources[j]
            term = powers(rate_part, level(jnp.maximum(ahead, 0))) * pieces[j]
            start = start + jnp.where(sources[j] < target, term, 0.0)
        got = start if k == 0 else exchange(start, k)
        slot = (member - k) % group
        if whole is None:
            whole = jnp.zeros_like(local)
        whole = lax.dynamic_update_slice_in_dim(whole, got, slot * piece, 1)
    carried = whole

    return run_out(x, halo, short_filter, rate_t, residue_t, skip.reshape(1, width), ends, ends_fix, carried)


def solution(mesh):
    return jax.shard_map(
        body,
        mesh=mesh,
        in_specs=(P(("ctx", "tp"), None, None), P(), P(), P(), P()),
        out_specs=P(("ctx", "tp"), None),
        check_vma=False,
    )
```

```python
import jax
import jax.numpy as jnp
from jax import lax
from jax.experimental import pallas as pl
from jax.experimental.pallas import tpu as pltpu
from jax.sharding import PartitionSpec as P

LANES = 128
SUB = 8
BLOCK = 1024
FIRST_WINDOW = 3
LATER_WINDOW = 4
UNROLL = 16


def lane_slice(c):
    return pl.ds(pl.multiple_of(c * LANES, LANES), LANES)


def row(ref, index, lanes):
    return jnp.broadcast_to(ref[pl.ds(index, 1), lanes], (SUB, LANES))


def first_prev(xs, halo_ref, c, lanes, seg, taps, sub):
    prev = []
    for back in range(1, taps):
        per_stream = []
        for s in range(xs.shape[0]):
            rows = xs[s, c, pl.ds(seg - back, SUB, stride=seg), :]
            edge = jnp.broadcast_to(halo_ref[s, pl.ds(taps - 1 - back, 1), lanes], (SUB, LANES))
            per_stream.append(jnp.where(sub == 0, edge, pltpu.roll(rows, 1, 0)))
        prev.append(per_stream)
    return prev


def fill_filters(f_ref, fsc, lanes):
    streams_count = f_ref.shape[1]
    for tap in range(f_ref.shape[0]):
        for s in range(streams_count):
            fsc[tap * streams_count + s] = row(f_ref.at[tap], s, lanes)


def step_features(xs, fsc, c, seg, j, prev):
    streams_count = xs.shape[0]
    taps = len(prev) + 1
    now = [xs[s, c, pl.ds(j, SUB, stride=seg), :] for s in range(streams_count)]
    feats = []
    for s in range(streams_count):
        acc = fsc[s] * now[s]
        for tap in range(1, taps):
            acc = acc + fsc[tap * streams_count + s] * prev[tap - 1][s]
        feats.append(acc)
    new_prev = [now] + prev[:-1]
    return feats, new_prev


def gate(feats):
    return (feats[1] * feats[2]).astype(jnp.bfloat16).astype(jnp.float32)


def state_kernel(x_ref, halo_ref, f_ref, a_ref, seg_ref, h_ref, xs, dsc, fsc):
    streams_count, rows, block = x_ref.shape
    taps = f_ref.shape[0]
    modes = a_ref.shape[0]
    seg = rows // SUB
    for c in range(block // LANES):
        xs[:, c] = x_ref[:, :, c * LANES : (c + 1) * LANES].astype(jnp.float32)
    sub = lax.broadcasted_iota(jnp.int32, (SUB, LANES), 0)

    def lane_group(c, carry):
        lanes = lane_slice(c)
        fill_filters(f_ref, fsc, lanes)
        for m in range(modes):
            dsc[m] = jnp.exp(-row(a_ref, m, lanes))

        def step(j, state):
            prev, states = state
            feats, prev = step_features(xs, fsc, c, seg, j, prev)
            u = gate(feats)
            return prev, tuple(dsc[m] * states[m] + u for m in range(modes))

        zero = jnp.zeros((SUB, LANES), jnp.float32)
        init = (first_prev(xs, halo_ref, c, lanes, seg, taps, sub), (zero,) * modes)
        _, states = lax.fori_loop(0, seg, step, init, unroll=UNROLL)
        later = (SUB - 1 - sub).astype(jnp.float32) * float(seg)
        for m in range(modes):
            seg_ref[m, :, lanes] = states[m]
            weight = jnp.exp(-row(a_ref, m, lanes) * later)
            h_ref[pl.ds(m, 1), lanes] = jnp.sum(weight * states[m], axis=0, keepdims=True)
        return carry

    lax.fori_loop(0, block // LANES, lane_group, 0)


def out_kernel(
    x_ref, halo_ref, f_ref, a_ref, r_ref, skip_ref, seg_ref, fix_ref, hin_ref, o_ref, xs, ys, dsc, rsc, fsc
):
    streams_count, rows, block = x_ref.shape
    taps = f_ref.shape[0]
    modes = a_ref.shape[0]
    seg = rows // SUB
    for c in range(block // LANES):
        xs[:, c] = x_ref[:, :, c * LANES : (c + 1) * LANES].astype(jnp.float32)
    sub = lax.broadcasted_iota(jnp.int32, (SUB, LANES), 0)

    def lane_group(c, carry):
        lanes = lane_slice(c)
        fill_filters(f_ref, fsc, lanes)
        starts = []
        for m in range(modes):
            rate = row(a_ref, m, lanes)
            dsc[m] = jnp.exp(-rate)
            rsc[m] = row(r_ref, m, lanes)
            ends = seg_ref[m, :, lanes] + jnp.where(sub == 0, row(fix_ref, m, lanes), 0.0)
            carried = jnp.where(sub >= 1, pltpu.roll(ends, 1, 0), 0.0)
            offset = 1
            while offset < SUB:
                factor = jnp.exp(-rate * float(seg * offset))
                carried = carried + jnp.where(sub >= offset, factor * pltpu.roll(carried, offset, 0), 0.0)
                offset *= 2
            lead = jnp.exp(-rate * (sub.astype(jnp.float32) * float(seg)))
            starts.append(carried + lead * row(hin_ref, m, lanes))
        skip_rows = row(skip_ref, 0, lanes)

        def step(j, state):
            prev, states = state
            feats, prev = step_features(xs, fsc, c, seg, j, prev)
            u = gate(feats)
            new = [dsc[m] * states[m] + u for m in range(modes)]
            terms = [rsc[m] * new[m] for m in range(modes)]
            while len(terms) > 1:
                paired = [terms[i] + terms[i + 1] for i in range(0, len(terms) - 1, 2)]
                terms = paired + terms[len(terms) - len(terms) % 2 :]
            conv = terms[0]
            y = (conv + skip_rows * u).astype(jnp.bfloat16).astype(jnp.float32)
            ys[c, pl.ds(j, SUB, stride=seg), :] = feats[0] * y
            return prev, tuple(new)

        init = (first_prev(xs, halo_ref, c, lanes, seg, taps, sub), tuple(starts))
        lax.fori_loop(0, seg, step, init, unroll=UNROLL)
        return carry

    lax.fori_loop(0, block // LANES, lane_group, 0)
    for c in range(block // LANES):
        o_ref[:, c * LANES : (c + 1) * LANES] = ys[c].astype(o_ref.dtype)


def run_state(x, halo, f, rate_t):
    streams_count, rows, width = x.shape
    taps = f.shape[0]
    modes = rate_t.shape[0]
    return pl.pallas_call(
        state_kernel,
        grid=(width // BLOCK,),
        in_specs=[
            pl.BlockSpec((streams_count, rows, BLOCK), lambda i: (0, 0, i)),
            pl.BlockSpec((streams_count, taps - 1, BLOCK), lambda i: (0, 0, i)),
            pl.BlockSpec((taps, streams_count, BLOCK), lambda i: (0, 0, i)),
            pl.BlockSpec((modes, BLOCK), lambda i: (0, i)),
        ],
        out_specs=[
            pl.BlockSpec((modes, SUB, BLOCK), lambda i: (0, 0, i)),
            pl.BlockSpec((modes, BLOCK), lambda i: (0, i)),
        ],
        out_shape=[
            jax.ShapeDtypeStruct((modes, SUB, width), jnp.float32),
            jax.ShapeDtypeStruct((modes, width), jnp.float32),
        ],
        scratch_shapes=[
            pltpu.VMEM((streams_count, BLOCK // LANES, rows, LANES), jnp.float32),
            pltpu.VMEM((modes, SUB, LANES), jnp.float32),
            pltpu.VMEM((taps * streams_count, SUB, LANES), jnp.float32),
        ],
    )(x, halo, f, rate_t)


def run_out(x, halo, f, rate_t, residue_t, skip, ends, fix, hin):
    streams_count, rows, width = x.shape
    taps = f.shape[0]
    modes = rate_t.shape[0]
    return pl.pallas_call(
        out_kernel,
        grid=(width // BLOCK,),
        in_specs=[
            pl.BlockSpec((streams_count, rows, BLOCK), lambda i: (0, 0, i)),
            pl.BlockSpec((streams_count, taps - 1, BLOCK), lambda i: (0, 0, i)),
            pl.BlockSpec((taps, streams_count, BLOCK), lambda i: (0, 0, i)),
            pl.BlockSpec((modes, BLOCK), lambda i: (0, i)),
            pl.BlockSpec((modes, BLOCK), lambda i: (0, i)),
            pl.BlockSpec((1, BLOCK), lambda i: (0, i)),
            pl.BlockSpec((modes, SUB, BLOCK), lambda i: (0, 0, i)),
            pl.BlockSpec((modes, BLOCK), lambda i: (0, i)),
            pl.BlockSpec((modes, BLOCK), lambda i: (0, i)),
        ],
        out_specs=pl.BlockSpec((rows, BLOCK), lambda i: (0, i)),
        out_shape=jax.ShapeDtypeStruct((rows, width), jnp.bfloat16),
        scratch_shapes=[
            pltpu.VMEM((streams_count, BLOCK // LANES, rows, LANES), jnp.float32),
            pltpu.VMEM((BLOCK // LANES, rows, LANES), jnp.float32),
            pltpu.VMEM((modes, SUB, LANES), jnp.float32),
            pltpu.VMEM((modes, SUB, LANES), jnp.float32),
            pltpu.VMEM((taps * streams_count, SUB, LANES), jnp.float32),
        ],
    )(x, halo, f, rate_t, residue_t, skip, ends, fix, hin)


def body(streams, short_filter, skip, rates, residues):
    axes = ("ctx", "tp")
    devices = lax.axis_size("ctx") * lax.axis_size("tp")
    tok_rows, streams_count, width = streams.shape
    taps = short_filter.shape[0]
    modes = rates.shape[1]

    def shift(value, offset):
        pairs = [(j, j + offset) for j in range(devices - offset)]
        return lax.ppermute(value, axes, pairs)

    halo_rows = shift(streams[tok_rows - (taps - 1) :], 1).astype(jnp.float32)
    halo = jnp.transpose(halo_rows, (1, 0, 2))
    x = jnp.transpose(streams, (1, 0, 2))
    rate_t = rates.T
    residue_t = residues.T
    ends, local = run_state(x, jnp.zeros_like(halo), short_filter, rate_t)

    head = streams[: taps - 1].astype(jnp.float32)

    def head_gate(before):
        rows = jnp.concatenate([before, head], axis=0)
        gated = []
        for t in range(taps - 1):
            feat = short_filter[0] * rows[t + taps - 1]
            for tap in range(1, taps):
                feat = feat + short_filter[tap] * rows[t + taps - 1 - tap]
            gated.append((feat[1] * feat[2]).astype(jnp.bfloat16).astype(jnp.float32))
        return gated

    seg = tok_rows // SUB
    true_head = head_gate(halo_rows)
    zero_head = head_gate(jnp.zeros_like(halo_rows))
    local_fix = None
    ends_fix = None
    for t in range(taps - 1):
        delta = (true_head[t] - zero_head[t])[None, :]
        to_end = jnp.exp(-rate_t * float(tok_rows - 1 - t)) * delta
        to_seg = jnp.exp(-rate_t * float(seg - 1 - t)) * delta
        local_fix = to_end if local_fix is None else local_fix + to_end
        ends_fix = to_seg if ends_fix is None else ends_fix + to_seg
    local = local + local_fix

    group = lax.axis_size("tp")
    spans = lax.axis_size("ctx")
    member = lax.axis_index("tp")
    piece = width // group

    def exchange(value, k):
        return lax.ppermute(value, "tp", [(q, (q + k) % group) for q in range(group)])

    def powers(rates_part, count):
        return jnp.exp(-rates_part * (float(tok_rows) * count))

    inside = None
    total = powers(rate_t, (group - 1 - member).astype(jnp.float32)) * local
    for k in range(1, group):
        other = exchange(local, k)
        source = (member - k) % group
        total = total + powers(rate_t, (group - 1 - source).astype(jnp.float32)) * other
        term = jnp.where(k <= member, powers(rate_t, float(k - 1)) * other, 0.0)
        inside = term if inside is None else inside + term
    if inside is None:
        inside = jnp.zeros_like(local)

    first_channel = member * piece
    rate_part = lax.dynamic_slice_in_dim(rate_t, first_channel, piece, 1)
    total_part = lax.dynamic_slice_in_dim(total, first_channel, piece, 1)

    def span_shift(value, offset):
        return lax.ppermute(value, "ctx", [(j, j + offset) for j in range(spans - offset)])

    def gather_window(value, spacing, count):
        gathered = None
        for k in range(1, count + 1):
            if k * spacing >= spans:
                break
            term = powers(rate_part, float(group * (k - 1) * spacing)) * span_shift(value, k * spacing)
            gathered = term if gathered is None else gathered + term
        return gathered

    if spans > 1:
        first = min(FIRST_WINDOW, spans - 1)
        before = gather_window(total_part, 1, first)
        window = first
        while window < spans - 1:
            count = min(-(-(spans - 1) // window) - 1, LATER_WINDOW)
            before = before + powers(rate_part, float(group * window)) * gather_window(before, window, count)
            window *= count + 1
    else:
        before = jnp.zeros_like(total_part)

    whole = jnp.zeros_like(local)
    for k in range(group):
        part = before if k == 0 else exchange(before, k)
        whole = lax.dynamic_update_slice_in_dim(whole, part, ((member - k) % group) * piece, 1)
    carried = powers(rate_t, member.astype(jnp.float32)) * whole + inside

    return run_out(x, halo, short_filter, rate_t, residue_t, skip.reshape(1, width), ends, ends_fix, carried)


def solution(mesh):
    return jax.shard_map(
        body,
        mesh=mesh,
        in_specs=(P(("ctx", "tp"), None, None), P(), P(), P(), P()),
        out_specs=P(("ctx", "tp"), None),
        check_vma=False,
    )
```

```python
import jax
import jax.numpy as jnp
from jax import lax
from jax.experimental import pallas as pl
from jax.experimental.pallas import tpu as pltpu
from jax.sharding import PartitionSpec as P

LANES = 128
SUB = 8
BLOCK = 1024
FIRST_WINDOW = 3
LATER_WINDOW = 4
UNROLL = 16


def lane_slice(c):
    return pl.ds(pl.multiple_of(c * LANES, LANES), LANES)


def row(ref, index, lanes):
    return jnp.broadcast_to(ref[pl.ds(index, 1), lanes], (SUB, LANES))


def first_prev(xs, halo_ref, c, lanes, seg, taps, sub):
    prev = []
    for back in range(1, taps):
        per_stream = []
        for s in range(xs.shape[0]):
            rows = xs[s, c, pl.ds(seg - back, SUB, stride=seg), :]
            edge = jnp.broadcast_to(halo_ref[s, pl.ds(taps - 1 - back, 1), lanes], (SUB, LANES))
            per_stream.append(jnp.where(sub == 0, edge, pltpu.roll(rows, 1, 0)))
        prev.append(per_stream)
    return prev


def fill_filters(f_ref, fsc, lanes):
    streams_count = f_ref.shape[1]
    for tap in range(f_ref.shape[0]):
        for s in range(streams_count):
            fsc[tap * streams_count + s] = row(f_ref.at[tap], s, lanes)


def step_features(xs, fsc, c, seg, j, prev):
    streams_count = xs.shape[0]
    taps = len(prev) + 1
    now = [xs[s, c, pl.ds(j, SUB, stride=seg), :] for s in range(streams_count)]
    feats = []
    for s in range(streams_count):
        acc = fsc[s] * now[s]
        for tap in range(1, taps):
            acc = acc + fsc[tap * streams_count + s] * prev[tap - 1][s]
        feats.append(acc)
    new_prev = [now] + prev[:-1]
    return feats, new_prev


def gate(feats):
    return (feats[1] * feats[2]).astype(jnp.bfloat16).astype(jnp.float32)


def state_kernel(x_ref, halo_ref, f_ref, a_ref, seg_ref, h_ref, xs, dsc, fsc):
    streams_count, rows, block = x_ref.shape
    taps = f_ref.shape[0]
    modes = a_ref.shape[0]
    seg = rows // SUB
    for c in range(block // LANES):
        xs[:, c] = x_ref[:, :, c * LANES : (c + 1) * LANES].astype(jnp.float32)
    sub = lax.broadcasted_iota(jnp.int32, (SUB, LANES), 0)

    def lane_group(c, carry):
        lanes = lane_slice(c)
        fill_filters(f_ref, fsc, lanes)
        for m in range(modes):
            dsc[m] = jnp.exp(-row(a_ref, m, lanes))

        def step(j, state):
            prev, states = state
            feats, prev = step_features(xs, fsc, c, seg, j, prev)
            u = gate(feats)
            return prev, tuple(dsc[m] * states[m] + u for m in range(modes))

        zero = jnp.zeros((SUB, LANES), jnp.float32)
        init = (first_prev(xs, halo_ref, c, lanes, seg, taps, sub), (zero,) * modes)
        _, states = lax.fori_loop(0, seg, step, init, unroll=UNROLL)
        later = (SUB - 1 - sub).astype(jnp.float32) * float(seg)
        for m in range(modes):
            seg_ref[m, :, lanes] = states[m]
            weight = jnp.exp(-row(a_ref, m, lanes) * later)
            h_ref[pl.ds(m, 1), lanes] = jnp.sum(weight * states[m], axis=0, keepdims=True)
        return carry

    lax.fori_loop(0, block // LANES, lane_group, 0, unroll=2)


def out_kernel(
    x_ref, halo_ref, f_ref, a_ref, r_ref, skip_ref, seg_ref, fix_ref, hin_ref, o_ref, xs, ys, dsc, rsc, fsc
):
    streams_count, rows, block = x_ref.shape
    taps = f_ref.shape[0]
    modes = a_ref.shape[0]
    seg = rows // SUB
    for c in range(block // LANES):
        xs[:, c] = x_ref[:, :, c * LANES : (c + 1) * LANES].astype(jnp.float32)
    sub = lax.broadcasted_iota(jnp.int32, (SUB, LANES), 0)

    def lane_group(c, carry):
        lanes = lane_slice(c)
        fill_filters(f_ref, fsc, lanes)
        starts = []
        for m in range(modes):
            rate = row(a_ref, m, lanes)
            dsc[m] = jnp.exp(-rate)
            rsc[m] = row(r_ref, m, lanes)
            ends = seg_ref[m, :, lanes] + jnp.where(sub == 0, row(fix_ref, m, lanes), 0.0)
            carried = jnp.where(sub >= 1, pltpu.roll(ends, 1, 0), 0.0)
            offset = 1
            while offset < SUB:
                factor = jnp.exp(-rate * float(seg * offset))
                carried = carried + jnp.where(sub >= offset, factor * pltpu.roll(carried, offset, 0), 0.0)
                offset *= 2
            lead = jnp.exp(-rate * (sub.astype(jnp.float32) * float(seg)))
            starts.append(carried + lead * row(hin_ref, m, lanes))
        skip_rows = row(skip_ref, 0, lanes)

        def step(j, state):
            prev, states = state
            feats, prev = step_features(xs, fsc, c, seg, j, prev)
            u = gate(feats)
            new = [dsc[m] * states[m] + u for m in range(modes)]
            terms = [rsc[m] * new[m] for m in range(modes)]
            while len(terms) > 1:
                paired = [terms[i] + terms[i + 1] for i in range(0, len(terms) - 1, 2)]
                terms = paired + terms[len(terms) - len(terms) % 2 :]
            conv = terms[0]
            y = (conv + skip_rows * u).astype(jnp.bfloat16).astype(jnp.float32)
            ys[c, pl.ds(j, SUB, stride=seg), :] = feats[0] * y
            return prev, tuple(new)

        init = (first_prev(xs, halo_ref, c, lanes, seg, taps, sub), tuple(starts))
        lax.fori_loop(0, seg, step, init, unroll=UNROLL)
        return carry

    lax.fori_loop(0, block // LANES, lane_group, 0, unroll=2)
    for c in range(block // LANES):
        o_ref[:, c * LANES : (c + 1) * LANES] = ys[c].astype(o_ref.dtype)


def run_state(x, halo, f, rate_t):
    streams_count, rows, width = x.shape
    taps = f.shape[0]
    modes = rate_t.shape[0]
    return pl.pallas_call(
        state_kernel,
        grid=(width // BLOCK,),
        in_specs=[
            pl.BlockSpec((streams_count, rows, BLOCK), lambda i: (0, 0, i)),
            pl.BlockSpec((streams_count, taps - 1, BLOCK), lambda i: (0, 0, i)),
            pl.BlockSpec((taps, streams_count, BLOCK), lambda i: (0, 0, i)),
            pl.BlockSpec((modes, BLOCK), lambda i: (0, i)),
        ],
        out_specs=[
            pl.BlockSpec((modes, SUB, BLOCK), lambda i: (0, 0, i)),
            pl.BlockSpec((modes, BLOCK), lambda i: (0, i)),
        ],
        out_shape=[
            jax.ShapeDtypeStruct((modes, SUB, width), jnp.float32),
            jax.ShapeDtypeStruct((modes, width), jnp.float32),
        ],
        scratch_shapes=[
            pltpu.VMEM((streams_count, BLOCK // LANES, rows, LANES), jnp.float32),
            pltpu.VMEM((modes, SUB, LANES), jnp.float32),
            pltpu.VMEM((taps * streams_count, SUB, LANES), jnp.float32),
        ],
    )(x, halo, f, rate_t)


def run_out(x, halo, f, rate_t, residue_t, skip, ends, fix, hin):
    streams_count, rows, width = x.shape
    taps = f.shape[0]
    modes = rate_t.shape[0]
    return pl.pallas_call(
        out_kernel,
        grid=(width // BLOCK,),
        in_specs=[
            pl.BlockSpec((streams_count, rows, BLOCK), lambda i: (0, 0, i)),
            pl.BlockSpec((streams_count, taps - 1, BLOCK), lambda i: (0, 0, i)),
            pl.BlockSpec((taps, streams_count, BLOCK), lambda i: (0, 0, i)),
            pl.BlockSpec((modes, BLOCK), lambda i: (0, i)),
            pl.BlockSpec((modes, BLOCK), lambda i: (0, i)),
            pl.BlockSpec((1, BLOCK), lambda i: (0, i)),
            pl.BlockSpec((modes, SUB, BLOCK), lambda i: (0, 0, i)),
            pl.BlockSpec((modes, BLOCK), lambda i: (0, i)),
            pl.BlockSpec((modes, BLOCK), lambda i: (0, i)),
        ],
        out_specs=pl.BlockSpec((rows, BLOCK), lambda i: (0, i)),
        out_shape=jax.ShapeDtypeStruct((rows, width), jnp.bfloat16),
        scratch_shapes=[
            pltpu.VMEM((streams_count, BLOCK // LANES, rows, LANES), jnp.float32),
            pltpu.VMEM((BLOCK // LANES, rows, LANES), jnp.float32),
            pltpu.VMEM((modes, SUB, LANES), jnp.float32),
            pltpu.VMEM((modes, SUB, LANES), jnp.float32),
            pltpu.VMEM((taps * streams_count, SUB, LANES), jnp.float32),
        ],
    )(x, halo, f, rate_t, residue_t, skip, ends, fix, hin)


def body(streams, short_filter, skip, rates, residues):
    axes = ("ctx", "tp")
    devices = lax.axis_size("ctx") * lax.axis_size("tp")
    tok_rows, streams_count, width = streams.shape
    taps = short_filter.shape[0]
    modes = rates.shape[1]

    def shift(value, offset):
        pairs = [(j, j + offset) for j in range(devices - offset)]
        return lax.ppermute(value, axes, pairs)

    halo_rows = shift(streams[tok_rows - (taps - 1) :], 1).astype(jnp.float32)
    halo = jnp.transpose(halo_rows, (1, 0, 2))
    x = jnp.transpose(streams, (1, 0, 2))
    rate_t = rates.T
    residue_t = residues.T
    ends, local = run_state(x, jnp.zeros_like(halo), short_filter, rate_t)

    head = streams[: taps - 1].astype(jnp.float32)

    def head_gate(before):
        rows = jnp.concatenate([before, head], axis=0)
        gated = []
        for t in range(taps - 1):
            feat = short_filter[0] * rows[t + taps - 1]
            for tap in range(1, taps):
                feat = feat + short_filter[tap] * rows[t + taps - 1 - tap]
            gated.append((feat[1] * feat[2]).astype(jnp.bfloat16).astype(jnp.float32))
        return gated

    seg = tok_rows // SUB
    true_head = head_gate(halo_rows)
    zero_head = head_gate(jnp.zeros_like(halo_rows))
    local_fix = None
    ends_fix = None
    for t in range(taps - 1):
        delta = (true_head[t] - zero_head[t])[None, :]
        to_end = jnp.exp(-rate_t * float(tok_rows - 1 - t)) * delta
        to_seg = jnp.exp(-rate_t * float(seg - 1 - t)) * delta
        local_fix = to_end if local_fix is None else local_fix + to_end
        ends_fix = to_seg if ends_fix is None else ends_fix + to_seg
    local = local + local_fix

    group = lax.axis_size("tp")
    spans = lax.axis_size("ctx")
    member = lax.axis_index("tp")
    piece = width // group

    def exchange(value, k):
        return lax.ppermute(value, "tp", [(q, (q + k) % group) for q in range(group)])

    def powers(rates_part, count):
        return jnp.exp(-rates_part * (float(tok_rows) * count))

    inside = None
    total = powers(rate_t, (group - 1 - member).astype(jnp.float32)) * local
    for k in range(1, group):
        other = exchange(local, k)
        source = (member - k) % group
        total = total + powers(rate_t, (group - 1 - source).astype(jnp.float32)) * other
        term = jnp.where(k <= member, powers(rate_t, float(k - 1)) * other, 0.0)
        inside = term if inside is None else inside + term
    if inside is None:
        inside = jnp.zeros_like(local)

    first_channel = member * piece
    rate_part = lax.dynamic_slice_in_dim(rate_t, first_channel, piece, 1)
    total_part = lax.dynamic_slice_in_dim(total, first_channel, piece, 1)

    def span_shift(value, offset):
        return lax.ppermute(value, "ctx", [(j, j + offset) for j in range(spans - offset)])

    def gather_window(value, spacing, count):
        gathered = None
        for k in range(1, count + 1):
            if k * spacing >= spans:
                break
            term = powers(rate_part, float(group * (k - 1) * spacing)) * span_shift(value, k * spacing)
            gathered = term if gathered is None else gathered + term
        return gathered

    if spans > 1:
        first = min(FIRST_WINDOW, spans - 1)
        before = gather_window(total_part, 1, first)
        window = first
        while window < spans - 1:
            count = min(-(-(spans - 1) // window) - 1, LATER_WINDOW)
            before = before + powers(rate_part, float(group * window)) * gather_window(before, window, count)
            window *= count + 1
    else:
        before = jnp.zeros_like(total_part)

    whole = jnp.zeros_like(local)
    for k in range(group):
        part = before if k == 0 else exchange(before, k)
        whole = lax.dynamic_update_slice_in_dim(whole, part, ((member - k) % group) * piece, 1)
    carried = powers(rate_t, member.astype(jnp.float32)) * whole + inside

    return run_out(x, halo, short_filter, rate_t, residue_t, skip.reshape(1, width), ends, ends_fix, carried)


def solution(mesh):
    return jax.shard_map(
        body,
        mesh=mesh,
        in_specs=(P(("ctx", "tp"), None, None), P(), P(), P(), P()),
        out_specs=P(("ctx", "tp"), None),
        check_vma=False,
    )
```

```python
import jax
import jax.numpy as jnp
from jax import lax
from jax.experimental import pallas as pl
from jax.experimental.pallas import tpu as pltpu
from jax.sharding import PartitionSpec as P

LANES = 128
SUB = 8
BLOCK = 1024
FIRST_WINDOW = 3
LATER_WINDOW = 4
UNROLL = 16


def lane_slice(c):
    return pl.ds(pl.multiple_of(c * LANES, LANES), LANES)


def row(ref, index, lanes):
    return jnp.broadcast_to(ref[pl.ds(index, 1), lanes], (SUB, LANES))


def first_prev(xs, halo_ref, c, lanes, seg, taps, sub):
    prev = []
    for back in range(1, taps):
        per_stream = []
        for s in range(xs.shape[0]):
            rows = xs[s, c, pl.ds(seg - back, SUB, stride=seg), :]
            edge = jnp.broadcast_to(halo_ref[s, pl.ds(taps - 1 - back, 1), lanes], (SUB, LANES))
            per_stream.append(jnp.where(sub == 0, edge, pltpu.roll(rows, 1, 0)))
        prev.append(per_stream)
    return prev


def fill_filters(f_ref, fsc, lanes):
    streams_count = f_ref.shape[1]
    for tap in range(f_ref.shape[0]):
        for s in range(streams_count):
            fsc[tap * streams_count + s] = row(f_ref.at[tap], s, lanes)


def step_features(xs, fsc, c, seg, j, prev):
    streams_count = xs.shape[0]
    taps = len(prev) + 1
    now = [xs[s, c, pl.ds(j, SUB, stride=seg), :] for s in range(streams_count)]
    feats = []
    for s in range(streams_count):
        acc = fsc[s] * now[s]
        for tap in range(1, taps):
            acc = acc + fsc[tap * streams_count + s] * prev[tap - 1][s]
        feats.append(acc)
    new_prev = [now] + prev[:-1]
    return feats, new_prev


def gate(feats):
    return (feats[1] * feats[2]).astype(jnp.bfloat16).astype(jnp.float32)


def state_kernel(x_ref, halo_ref, f_ref, a_ref, seg_ref, h_ref, xs, dsc, fsc):
    streams_count, rows, block = x_ref.shape
    taps = f_ref.shape[0]
    modes = a_ref.shape[0]
    seg = rows // SUB
    for c in range(block // LANES):
        xs[:, c] = x_ref[:, :, c * LANES : (c + 1) * LANES].astype(jnp.float32)
    sub = lax.broadcasted_iota(jnp.int32, (SUB, LANES), 0)

    def lane_group(c, carry):
        lanes = lane_slice(c)
        fill_filters(f_ref, fsc, lanes)
        for m in range(modes):
            dsc[m] = jnp.exp(-row(a_ref, m, lanes))

        def step(j, state):
            prev, states = state
            feats, prev = step_features(xs, fsc, c, seg, j, prev)
            u = gate(feats)
            return prev, tuple(dsc[m] * states[m] + u for m in range(modes))

        zero = jnp.zeros((SUB, LANES), jnp.float32)
        init = (first_prev(xs, halo_ref, c, lanes, seg, taps, sub), (zero,) * modes)
        _, states = lax.fori_loop(0, seg, step, init, unroll=UNROLL)
        later = (SUB - 1 - sub).astype(jnp.float32) * float(seg)
        for m in range(modes):
            seg_ref[m, :, lanes] = states[m]
            weight = jnp.exp(-row(a_ref, m, lanes) * later)
            h_ref[pl.ds(m, 1), lanes] = jnp.sum(weight * states[m], axis=0, keepdims=True)
        return carry

    lax.fori_loop(0, block // LANES, lane_group, 0)


def out_kernel(
    x_ref, halo_ref, f_ref, a_ref, r_ref, skip_ref, seg_ref, fix_ref, hin_ref, o_ref, xs, ys, dsc, rsc, fsc
):
    streams_count, rows, block = x_ref.shape
    taps = f_ref.shape[0]
    modes = a_ref.shape[0]
    seg = rows // SUB
    for c in range(block // LANES):
        xs[:, c] = x_ref[:, :, c * LANES : (c + 1) * LANES].astype(jnp.float32)
    sub = lax.broadcasted_iota(jnp.int32, (SUB, LANES), 0)

    def lane_group(c, carry):
        lanes = lane_slice(c)
        fill_filters(f_ref, fsc, lanes)
        starts = []
        for m in range(modes):
            rate = row(a_ref, m, lanes)
            dsc[m] = jnp.exp(-rate)
            rsc[m] = row(r_ref, m, lanes)
            ends = seg_ref[m, :, lanes] + jnp.where(sub == 0, row(fix_ref, m, lanes), 0.0)
            carried = jnp.where(sub >= 1, pltpu.roll(ends, 1, 0), 0.0)
            factor = jnp.exp(-rate * float(seg))
            lead = jnp.ones_like(factor)
            offset = 1
            while offset < SUB:
                carried = carried + jnp.where(sub >= offset, factor * pltpu.roll(carried, offset, 0), 0.0)
                lead = jnp.where((sub & offset) != 0, lead * factor, lead)
                factor = factor * factor
                offset *= 2
            starts.append(carried + lead * row(hin_ref, m, lanes))
        skip_rows = row(skip_ref, 0, lanes)

        def step(j, state):
            prev, states = state
            feats, prev = step_features(xs, fsc, c, seg, j, prev)
            u = gate(feats)
            new = [dsc[m] * states[m] + u for m in range(modes)]
            terms = [rsc[m] * new[m] for m in range(modes)]
            while len(terms) > 1:
                paired = [terms[i] + terms[i + 1] for i in range(0, len(terms) - 1, 2)]
                terms = paired + terms[len(terms) - len(terms) % 2 :]
            conv = terms[0]
            y = (conv + skip_rows * u).astype(jnp.bfloat16).astype(jnp.float32)
            ys[c, pl.ds(j, SUB, stride=seg), :] = feats[0] * y
            return prev, tuple(new)

        init = (first_prev(xs, halo_ref, c, lanes, seg, taps, sub), tuple(starts))
        lax.fori_loop(0, seg, step, init, unroll=UNROLL)
        return carry

    lax.fori_loop(0, block // LANES, lane_group, 0)
    for c in range(block // LANES):
        o_ref[:, c * LANES : (c + 1) * LANES] = ys[c].astype(o_ref.dtype)


def run_state(x, halo, f, rate_t):
    streams_count, rows, width = x.shape
    taps = f.shape[0]
    modes = rate_t.shape[0]
    return pl.pallas_call(
        state_kernel,
        grid=(width // BLOCK,),
        in_specs=[
            pl.BlockSpec((streams_count, rows, BLOCK), lambda i: (0, 0, i)),
            pl.BlockSpec((streams_count, taps - 1, BLOCK), lambda i: (0, 0, i)),
            pl.BlockSpec((taps, streams_count, BLOCK), lambda i: (0, 0, i)),
            pl.BlockSpec((modes, BLOCK), lambda i: (0, i)),
        ],
        out_specs=[
            pl.BlockSpec((modes, SUB, BLOCK), lambda i: (0, 0, i)),
            pl.BlockSpec((modes, BLOCK), lambda i: (0, i)),
        ],
        out_shape=[
            jax.ShapeDtypeStruct((modes, SUB, width), jnp.float32),
            jax.ShapeDtypeStruct((modes, width), jnp.float32),
        ],
        scratch_shapes=[
            pltpu.VMEM((streams_count, BLOCK // LANES, rows, LANES), jnp.float32),
            pltpu.VMEM((modes, SUB, LANES), jnp.float32),
            pltpu.VMEM((taps * streams_count, SUB, LANES), jnp.float32),
        ],
    )(x, halo, f, rate_t)


def run_out(x, halo, f, rate_t, residue_t, skip, ends, fix, hin):
    streams_count, rows, width = x.shape
    taps = f.shape[0]
    modes = rate_t.shape[0]
    return pl.pallas_call(
        out_kernel,
        grid=(width // BLOCK,),
        in_specs=[
            pl.BlockSpec((streams_count, rows, BLOCK), lambda i: (0, 0, i)),
            pl.BlockSpec((streams_count, taps - 1, BLOCK), lambda i: (0, 0, i)),
            pl.BlockSpec((taps, streams_count, BLOCK), lambda i: (0, 0, i)),
            pl.BlockSpec((modes, BLOCK), lambda i: (0, i)),
            pl.BlockSpec((modes, BLOCK), lambda i: (0, i)),
            pl.BlockSpec((1, BLOCK), lambda i: (0, i)),
            pl.BlockSpec((modes, SUB, BLOCK), lambda i: (0, 0, i)),
            pl.BlockSpec((modes, BLOCK), lambda i: (0, i)),
            pl.BlockSpec((modes, BLOCK), lambda i: (0, i)),
        ],
        out_specs=pl.BlockSpec((rows, BLOCK), lambda i: (0, i)),
        out_shape=jax.ShapeDtypeStruct((rows, width), jnp.bfloat16),
        scratch_shapes=[
            pltpu.VMEM((streams_count, BLOCK // LANES, rows, LANES), jnp.float32),
            pltpu.VMEM((BLOCK // LANES, rows, LANES), jnp.float32),
            pltpu.VMEM((modes, SUB, LANES), jnp.float32),
            pltpu.VMEM((modes, SUB, LANES), jnp.float32),
            pltpu.VMEM((taps * streams_count, SUB, LANES), jnp.float32),
        ],
    )(x, halo, f, rate_t, residue_t, skip, ends, fix, hin)


def body(streams, short_filter, skip, rates, residues):
    axes = ("ctx", "tp")
    devices = lax.axis_size("ctx") * lax.axis_size("tp")
    tok_rows, streams_count, width = streams.shape
    taps = short_filter.shape[0]
    modes = rates.shape[1]

    def shift(value, offset):
        pairs = [(j, j + offset) for j in range(devices - offset)]
        return lax.ppermute(value, axes, pairs)

    halo_rows = shift(streams[tok_rows - (taps - 1) :], 1).astype(jnp.float32)
    halo = jnp.transpose(halo_rows, (1, 0, 2))
    x = jnp.transpose(streams, (1, 0, 2))
    rate_t = rates.T
    residue_t = residues.T
    ends, local = run_state(x, jnp.zeros_like(halo), short_filter, rate_t)

    head = streams[: taps - 1].astype(jnp.float32)

    def head_gate(before):
        rows = jnp.concatenate([before, head], axis=0)
        gated = []
        for t in range(taps - 1):
            feat = short_filter[0] * rows[t + taps - 1]
            for tap in range(1, taps):
                feat = feat + short_filter[tap] * rows[t + taps - 1 - tap]
            gated.append((feat[1] * feat[2]).astype(jnp.bfloat16).astype(jnp.float32))
        return gated

    seg = tok_rows // SUB
    true_head = head_gate(halo_rows)
    zero_head = head_gate(jnp.zeros_like(halo_rows))
    local_fix = None
    ends_fix = None
    for t in range(taps - 1):
        delta = (true_head[t] - zero_head[t])[None, :]
        to_end = jnp.exp(-rate_t * float(tok_rows - 1 - t)) * delta
        to_seg = jnp.exp(-rate_t * float(seg - 1 - t)) * delta
        local_fix = to_end if local_fix is None else local_fix + to_end
        ends_fix = to_seg if ends_fix is None else ends_fix + to_seg
    local = local + local_fix

    group = lax.axis_size("tp")
    spans = lax.axis_size("ctx")
    member = lax.axis_index("tp")
    piece = width // group

    def exchange(value, k):
        return lax.ppermute(value, "tp", [(q, (q + k) % group) for q in range(group)])

    def powers(rates_part, count):
        return jnp.exp(-rates_part * (float(tok_rows) * count))

    inside = None
    total = powers(rate_t, (group - 1 - member).astype(jnp.float32)) * local
    for k in range(1, group):
        other = exchange(local, k)
        source = (member - k) % group
        total = total + powers(rate_t, (group - 1 - source).astype(jnp.float32)) * other
        term = jnp.where(k <= member, powers(rate_t, float(k - 1)) * other, 0.0)
        inside = term if inside is None else inside + term
    if inside is None:
        inside = jnp.zeros_like(local)

    first_channel = member * piece
    rate_part = lax.dynamic_slice_in_dim(rate_t, first_channel, piece, 1)
    total_part = lax.dynamic_slice_in_dim(total, first_channel, piece, 1)

    def span_shift(value, offset):
        return lax.ppermute(value, "ctx", [(j, j + offset) for j in range(spans - offset)])

    def gather_window(value, spacing, count):
        gathered = None
        for k in range(1, count + 1):
            if k * spacing >= spans:
                break
            term = powers(rate_part, float(group * (k - 1) * spacing)) * span_shift(value, k * spacing)
            gathered = term if gathered is None else gathered + term
        return gathered

    if spans > 1:
        first = min(FIRST_WINDOW, spans - 1)
        before = gather_window(total_part, 1, first)
        window = first
        while window < spans - 1:
            count = min(-(-(spans - 1) // window) - 1, LATER_WINDOW)
            before = before + powers(rate_part, float(group * window)) * gather_window(before, window, count)
            window *= count + 1
    else:
        before = jnp.zeros_like(total_part)

    whole = jnp.zeros_like(local)
    for k in range(group):
        part = before if k == 0 else exchange(before, k)
        whole = lax.dynamic_update_slice_in_dim(whole, part, ((member - k) % group) * piece, 1)
    carried = powers(rate_t, member.astype(jnp.float32)) * whole + inside

    return run_out(x, halo, short_filter, rate_t, residue_t, skip.reshape(1, width), ends, ends_fix, carried)


def solution(mesh):
    return jax.shard_map(
        body,
        mesh=mesh,
        in_specs=(P(("ctx", "tp"), None, None), P(), P(), P(), P()),
        out_specs=P(("ctx", "tp"), None),
        check_vma=False,
    )
```

```python
import jax
import jax.numpy as jnp
from jax import lax
from jax.experimental import pallas as pl
from jax.experimental.pallas import tpu as pltpu
from jax.sharding import PartitionSpec as P

LANES = 128
SUB = 8
BLOCK = 1024
FIRST_WINDOW = 3
LATER_WINDOW = 4
UNROLL = 16


def lane_slice(c):
    return pl.ds(pl.multiple_of(c * LANES, LANES), LANES)


def row(ref, index, lanes):
    return jnp.broadcast_to(ref[pl.ds(index, 1), lanes], (SUB, LANES))


def first_prev(xs, halo_ref, c, lanes, seg, taps, sub):
    prev = []
    for back in range(1, taps):
        per_stream = []
        for s in range(xs.shape[0]):
            rows = xs[s, c, pl.ds(seg - back, SUB, stride=seg), :]
            edge = jnp.broadcast_to(halo_ref[s, pl.ds(taps - 1 - back, 1), lanes], (SUB, LANES))
            per_stream.append(jnp.where(sub == 0, edge, pltpu.roll(rows, 1, 0)))
        prev.append(per_stream)
    return prev


def fill_filters(f_ref, fsc, lanes):
    streams_count = f_ref.shape[1]
    for tap in range(f_ref.shape[0]):
        for s in range(streams_count):
            fsc[tap * streams_count + s] = row(f_ref.at[tap], s, lanes)


def step_features(xs, fsc, c, seg, j, prev):
    streams_count = xs.shape[0]
    taps = len(prev) + 1
    now = [xs[s, c, pl.ds(j, SUB, stride=seg), :] for s in range(streams_count)]
    feats = []
    for s in range(streams_count):
        acc = fsc[s] * now[s]
        for tap in range(1, taps):
            acc = acc + fsc[tap * streams_count + s] * prev[tap - 1][s]
        feats.append(acc)
    new_prev = [now] + prev[:-1]
    return feats, new_prev


def gate(feats):
    return (feats[1] * feats[2]).astype(jnp.bfloat16).astype(jnp.float32)


def state_kernel(x_ref, halo_ref, f_ref, a_ref, seg_ref, h_ref, xs, dsc, fsc):
    streams_count, rows, block = x_ref.shape
    taps = f_ref.shape[0]
    modes = a_ref.shape[0]
    seg = rows // SUB
    for c in range(block // LANES):
        xs[:, c] = x_ref[:, :, c * LANES : (c + 1) * LANES].astype(jnp.float32)
    sub = lax.broadcasted_iota(jnp.int32, (SUB, LANES), 0)

    def lane_group(c, carry):
        lanes = lane_slice(c)
        fill_filters(f_ref, fsc, lanes)
        for m in range(modes):
            dsc[m] = jnp.exp(-row(a_ref, m, lanes))

        def step(j, state):
            prev, states = state
            feats, prev = step_features(xs, fsc, c, seg, j, prev)
            u = gate(feats)
            return prev, tuple(dsc[m] * states[m] + u for m in range(modes))

        zero = jnp.zeros((SUB, LANES), jnp.float32)
        init = (first_prev(xs, halo_ref, c, lanes, seg, taps, sub), (zero,) * modes)
        _, states = lax.fori_loop(0, seg, step, init, unroll=UNROLL)
        later = SUB - 1 - sub
        for m in range(modes):
            seg_ref[m, :, lanes] = states[m]
            factor = jnp.exp(-row(a_ref, m, lanes) * float(seg))
            weight = jnp.ones_like(factor)
            bit = 1
            while bit < SUB:
                weight = jnp.where((later & bit) != 0, weight * factor, weight)
                factor = factor * factor
                bit *= 2
            h_ref[pl.ds(m, 1), lanes] = jnp.sum(weight * states[m], axis=0, keepdims=True)
        return carry

    lax.fori_loop(0, block // LANES, lane_group, 0, unroll=2)


def out_kernel(
    x_ref, halo_ref, f_ref, a_ref, r_ref, skip_ref, seg_ref, fix_ref, hin_ref, o_ref, xs, ys, dsc, rsc, fsc
):
    streams_count, rows, block = x_ref.shape
    taps = f_ref.shape[0]
    modes = a_ref.shape[0]
    seg = rows // SUB
    for c in range(block // LANES):
        xs[:, c] = x_ref[:, :, c * LANES : (c + 1) * LANES].astype(jnp.float32)
    sub = lax.broadcasted_iota(jnp.int32, (SUB, LANES), 0)

    def lane_group(c, carry):
        lanes = lane_slice(c)
        fill_filters(f_ref, fsc, lanes)
        starts = []
        for m in range(modes):
            rate = row(a_ref, m, lanes)
            dsc[m] = jnp.exp(-rate)
            rsc[m] = row(r_ref, m, lanes)
            ends = seg_ref[m, :, lanes] + jnp.where(sub == 0, row(fix_ref, m, lanes), 0.0)
            carried = jnp.where(sub >= 1, pltpu.roll(ends, 1, 0), 0.0)
            factor = jnp.exp(-rate * float(seg))
            lead = jnp.ones_like(factor)
            offset = 1
            while offset < SUB:
                carried = carried + jnp.where(sub >= offset, factor * pltpu.roll(carried, offset, 0), 0.0)
                lead = jnp.where((sub & offset) != 0, lead * factor, lead)
                factor = factor * factor
                offset *= 2
            starts.append(carried + lead * row(hin_ref, m, lanes))
        skip_rows = row(skip_ref, 0, lanes)

        def step(j, state):
            prev, states = state
            feats, prev = step_features(xs, fsc, c, seg, j, prev)
            u = gate(feats)
            new = [dsc[m] * states[m] + u for m in range(modes)]
            terms = [rsc[m] * new[m] for m in range(modes)]
            while len(terms) > 1:
                paired = [terms[i] + terms[i + 1] for i in range(0, len(terms) - 1, 2)]
                terms = paired + terms[len(terms) - len(terms) % 2 :]
            conv = terms[0]
            y = (conv + skip_rows * u).astype(jnp.bfloat16).astype(jnp.float32)
            ys[c, pl.ds(j, SUB, stride=seg), :] = feats[0] * y
            return prev, tuple(new)

        init = (first_prev(xs, halo_ref, c, lanes, seg, taps, sub), tuple(starts))
        lax.fori_loop(0, seg, step, init, unroll=UNROLL)
        return carry

    lax.fori_loop(0, block // LANES, lane_group, 0, unroll=2)
    for c in range(block // LANES):
        o_ref[:, c * LANES : (c + 1) * LANES] = ys[c].astype(o_ref.dtype)


def run_state(x, halo, f, rate_t):
    streams_count, rows, width = x.shape
    taps = f.shape[0]
    modes = rate_t.shape[0]
    return pl.pallas_call(
        state_kernel,
        grid=(width // BLOCK,),
        in_specs=[
            pl.BlockSpec((streams_count, rows, BLOCK), lambda i: (0, 0, i)),
            pl.BlockSpec((streams_count, taps - 1, BLOCK), lambda i: (0, 0, i)),
            pl.BlockSpec((taps, streams_count, BLOCK), lambda i: (0, 0, i)),
            pl.BlockSpec((modes, BLOCK), lambda i: (0, i)),
        ],
        out_specs=[
            pl.BlockSpec((modes, SUB, BLOCK), lambda i: (0, 0, i)),
            pl.BlockSpec((modes, BLOCK), lambda i: (0, i)),
        ],
        out_shape=[
            jax.ShapeDtypeStruct((modes, SUB, width), jnp.float32),
            jax.ShapeDtypeStruct((modes, width), jnp.float32),
        ],
        scratch_shapes=[
            pltpu.VMEM((streams_count, BLOCK // LANES, rows, LANES), jnp.float32),
            pltpu.VMEM((modes, SUB, LANES), jnp.float32),
            pltpu.VMEM((taps * streams_count, SUB, LANES), jnp.float32),
        ],
    )(x, halo, f, rate_t)


def run_out(x, halo, f, rate_t, residue_t, skip, ends, fix, hin):
    streams_count, rows, width = x.shape
    taps = f.shape[0]
    modes = rate_t.shape[0]
    return pl.pallas_call(
        out_kernel,
        grid=(width // BLOCK,),
        in_specs=[
            pl.BlockSpec((streams_count, rows, BLOCK), lambda i: (0, 0, i)),
            pl.BlockSpec((streams_count, taps - 1, BLOCK), lambda i: (0, 0, i)),
            pl.BlockSpec((taps, streams_count, BLOCK), lambda i: (0, 0, i)),
            pl.BlockSpec((modes, BLOCK), lambda i: (0, i)),
            pl.BlockSpec((modes, BLOCK), lambda i: (0, i)),
            pl.BlockSpec((1, BLOCK), lambda i: (0, i)),
            pl.BlockSpec((modes, SUB, BLOCK), lambda i: (0, 0, i)),
            pl.BlockSpec((modes, BLOCK), lambda i: (0, i)),
            pl.BlockSpec((modes, BLOCK), lambda i: (0, i)),
        ],
        out_specs=pl.BlockSpec((rows, BLOCK), lambda i: (0, i)),
        out_shape=jax.ShapeDtypeStruct((rows, width), jnp.bfloat16),
        scratch_shapes=[
            pltpu.VMEM((streams_count, BLOCK // LANES, rows, LANES), jnp.float32),
            pltpu.VMEM((BLOCK // LANES, rows, LANES), jnp.float32),
            pltpu.VMEM((modes, SUB, LANES), jnp.float32),
            pltpu.VMEM((modes, SUB, LANES), jnp.float32),
            pltpu.VMEM((taps * streams_count, SUB, LANES), jnp.float32),
        ],
    )(x, halo, f, rate_t, residue_t, skip, ends, fix, hin)


def body(streams, short_filter, skip, rates, residues):
    axes = ("ctx", "tp")
    devices = lax.axis_size("ctx") * lax.axis_size("tp")
    tok_rows, streams_count, width = streams.shape
    taps = short_filter.shape[0]
    modes = rates.shape[1]

    def shift(value, offset):
        pairs = [(j, j + offset) for j in range(devices - offset)]
        return lax.ppermute(value, axes, pairs)

    halo_rows = shift(streams[tok_rows - (taps - 1) :], 1).astype(jnp.float32)
    halo = jnp.transpose(halo_rows, (1, 0, 2))
    x = jnp.transpose(streams, (1, 0, 2))
    rate_t = rates.T
    residue_t = residues.T
    ends, local = run_state(x, jnp.zeros_like(halo), short_filter, rate_t)

    head = streams[: taps - 1].astype(jnp.float32)

    def head_gate(before):
        rows = jnp.concatenate([before, head], axis=0)
        gated = []
        for t in range(taps - 1):
            feat = short_filter[0] * rows[t + taps - 1]
            for tap in range(1, taps):
                feat = feat + short_filter[tap] * rows[t + taps - 1 - tap]
            gated.append((feat[1] * feat[2]).astype(jnp.bfloat16).astype(jnp.float32))
        return gated

    seg = tok_rows // SUB
    true_head = head_gate(halo_rows)
    zero_head = head_gate(jnp.zeros_like(halo_rows))
    local_fix = None
    ends_fix = None
    for t in range(taps - 1):
        delta = (true_head[t] - zero_head[t])[None, :]
        to_end = jnp.exp(-rate_t * float(tok_rows - 1 - t)) * delta
        to_seg = jnp.exp(-rate_t * float(seg - 1 - t)) * delta
        local_fix = to_end if local_fix is None else local_fix + to_end
        ends_fix = to_seg if ends_fix is None else ends_fix + to_seg
    local = local + local_fix

    group = lax.axis_size("tp")
    spans = lax.axis_size("ctx")
    member = lax.axis_index("tp")
    piece = width // group

    def exchange(value, k):
        return lax.ppermute(value, "tp", [(q, (q + k) % group) for q in range(group)])

    def powers(rates_part, count):
        return jnp.exp(-rates_part * (float(tok_rows) * count))

    inside = None
    total = powers(rate_t, (group - 1 - member).astype(jnp.float32)) * local
    for k in range(1, group):
        other = exchange(local, k)
        source = (member - k) % group
        total = total + powers(rate_t, (group - 1 - source).astype(jnp.float32)) * other
        term = jnp.where(k <= member, powers(rate_t, float(k - 1)) * other, 0.0)
        inside = term if inside is None else inside + term
    if inside is None:
        inside = jnp.zeros_like(local)

    first_channel = member * piece
    rate_part = lax.dynamic_slice_in_dim(rate_t, first_channel, piece, 1)
    total_part = lax.dynamic_slice_in_dim(total, first_channel, piece, 1)

    def span_shift(value, offset):
        return lax.ppermute(value, "ctx", [(j, j + offset) for j in range(spans - offset)])

    def gather_window(value, spacing, count):
        gathered = None
        for k in range(1, count + 1):
            if k * spacing >= spans:
                break
            term = powers(rate_part, float(group * (k - 1) * spacing)) * span_shift(value, k * spacing)
            gathered = term if gathered is None else gathered + term
        return gathered

    if spans > 1:
        first = min(FIRST_WINDOW, spans - 1)
        before = gather_window(total_part, 1, first)
        window = first
        while window < spans - 1:
            count = min(-(-(spans - 1) // window) - 1, LATER_WINDOW)
            before = before + powers(rate_part, float(group * window)) * gather_window(before, window, count)
            window *= count + 1
    else:
        before = jnp.zeros_like(total_part)

    whole = jnp.zeros_like(local)
    for k in range(group):
        part = before if k == 0 else exchange(before, k)
        whole = lax.dynamic_update_slice_in_dim(whole, part, ((member - k) % group) * piece, 1)
    carried = powers(rate_t, member.astype(jnp.float32)) * whole + inside

    return run_out(x, halo, short_filter, rate_t, residue_t, skip.reshape(1, width), ends, ends_fix, carried)


def solution(mesh):
    return jax.shard_map(
        body,
        mesh=mesh,
        in_specs=(P(("ctx", "tp"), None, None), P(), P(), P(), P()),
        out_specs=P(("ctx", "tp"), None),
        check_vma=False,
    )
```

```python
import jax
import jax.numpy as jnp
from jax import lax
from jax.experimental import pallas as pl
from jax.experimental.pallas import tpu as pltpu
from jax.sharding import PartitionSpec as P

LANES = 128
SUB = 8
BLOCK = 512
FIRST_WINDOW = 3
LATER_WINDOW = 4
UNROLL = 16


def lane_slice(c):
    return pl.ds(pl.multiple_of(c * LANES, LANES), LANES)


def row(ref, index, lanes):
    return jnp.broadcast_to(ref[pl.ds(index, 1), lanes], (SUB, LANES))


def first_prev(xs, halo_ref, c, lanes, seg, taps, sub):
    prev = []
    for back in range(1, taps):
        per_stream = []
        for s in range(xs.shape[0]):
            rows = xs[s, c, pl.ds(seg - back, SUB, stride=seg), :]
            edge = jnp.broadcast_to(halo_ref[s, pl.ds(taps - 1 - back, 1), lanes], (SUB, LANES))
            per_stream.append(jnp.where(sub == 0, edge, pltpu.roll(rows, 1, 0)))
        prev.append(per_stream)
    return prev


def fill_filters(f_ref, fsc, lanes):
    streams_count = f_ref.shape[1]
    for tap in range(f_ref.shape[0]):
        for s in range(streams_count):
            fsc[tap * streams_count + s] = row(f_ref.at[tap], s, lanes)


def step_features(xs, fsc, c, seg, j, prev):
    streams_count = xs.shape[0]
    taps = len(prev) + 1
    now = [xs[s, c, pl.ds(j, SUB, stride=seg), :] for s in range(streams_count)]
    feats = []
    for s in range(streams_count):
        acc = fsc[s] * now[s]
        for tap in range(1, taps):
            acc = acc + fsc[tap * streams_count + s] * prev[tap - 1][s]
        feats.append(acc)
    new_prev = [now] + prev[:-1]
    return feats, new_prev


def gate(feats):
    return (feats[1] * feats[2]).astype(jnp.bfloat16).astype(jnp.float32)


def state_kernel(x_ref, halo_ref, f_ref, a_ref, seg_ref, h_ref, xs, dsc, fsc):
    streams_count, rows, block = x_ref.shape
    taps = f_ref.shape[0]
    modes = a_ref.shape[0]
    seg = rows // SUB
    for c in range(block // LANES):
        xs[:, c] = x_ref[:, :, c * LANES : (c + 1) * LANES].astype(jnp.float32)
    sub = lax.broadcasted_iota(jnp.int32, (SUB, LANES), 0)

    def lane_group(c, carry):
        lanes = lane_slice(c)
        fill_filters(f_ref, fsc, lanes)
        for m in range(modes):
            dsc[m] = jnp.exp(-row(a_ref, m, lanes))

        def step(j, state):
            prev, states = state
            feats, prev = step_features(xs, fsc, c, seg, j, prev)
            u = gate(feats)
            return prev, tuple(dsc[m] * states[m] + u for m in range(modes))

        zero = jnp.zeros((SUB, LANES), jnp.float32)
        init = (first_prev(xs, halo_ref, c, lanes, seg, taps, sub), (zero,) * modes)
        _, states = lax.fori_loop(0, seg, step, init, unroll=UNROLL)
        later = (SUB - 1 - sub).astype(jnp.float32) * float(seg)
        for m in range(modes):
            seg_ref[m, :, lanes] = states[m]
            weight = jnp.exp(-row(a_ref, m, lanes) * later)
            h_ref[pl.ds(m, 1), lanes] = jnp.sum(weight * states[m], axis=0, keepdims=True)
        return carry

    lax.fori_loop(0, block // LANES, lane_group, 0, unroll=2)


def out_kernel(
    x_ref, halo_ref, f_ref, a_ref, r_ref, skip_ref, seg_ref, fix_ref, hin_ref, o_ref, xs, ys, dsc, rsc, fsc
):
    streams_count, rows, block = x_ref.shape
    taps = f_ref.shape[0]
    modes = a_ref.shape[0]
    seg = rows // SUB
    for c in range(block // LANES):
        xs[:, c] = x_ref[:, :, c * LANES : (c + 1) * LANES].astype(jnp.float32)
    sub = lax.broadcasted_iota(jnp.int32, (SUB, LANES), 0)

    def lane_group(c, carry):
        lanes = lane_slice(c)
        fill_filters(f_ref, fsc, lanes)
        starts = []
        for m in range(modes):
            rate = row(a_ref, m, lanes)
            dsc[m] = jnp.exp(-rate)
            rsc[m] = row(r_ref, m, lanes)
            ends = seg_ref[m, :, lanes] + jnp.where(sub == 0, row(fix_ref, m, lanes), 0.0)
            carried = jnp.where(sub >= 1, pltpu.roll(ends, 1, 0), 0.0)
            offset = 1
            while offset < SUB:
                factor = jnp.exp(-rate * float(seg * offset))
                carried = carried + jnp.where(sub >= offset, factor * pltpu.roll(carried, offset, 0), 0.0)
                offset *= 2
            lead = jnp.exp(-rate * (sub.astype(jnp.float32) * float(seg)))
            starts.append(carried + lead * row(hin_ref, m, lanes))
        skip_rows = row(skip_ref, 0, lanes)

        def step(j, state):
            prev, states = state
            feats, prev = step_features(xs, fsc, c, seg, j, prev)
            u = gate(feats)
            new = [dsc[m] * states[m] + u for m in range(modes)]
            terms = [rsc[m] * new[m] for m in range(modes)]
            while len(terms) > 1:
                paired = [terms[i] + terms[i + 1] for i in range(0, len(terms) - 1, 2)]
                terms = paired + terms[len(terms) - len(terms) % 2 :]
            conv = terms[0]
            y = (conv + skip_rows * u).astype(jnp.bfloat16).astype(jnp.float32)
            ys[c, pl.ds(j, SUB, stride=seg), :] = feats[0] * y
            return prev, tuple(new)

        init = (first_prev(xs, halo_ref, c, lanes, seg, taps, sub), tuple(starts))
        lax.fori_loop(0, seg, step, init, unroll=UNROLL)
        return carry

    lax.fori_loop(0, block // LANES, lane_group, 0, unroll=2)
    for c in range(block // LANES):
        o_ref[:, c * LANES : (c + 1) * LANES] = ys[c].astype(o_ref.dtype)


def run_state(x, halo, f, rate_t):
    streams_count, rows, width = x.shape
    taps = f.shape[0]
    modes = rate_t.shape[0]
    return pl.pallas_call(
        state_kernel,
        grid=(width // BLOCK,),
        in_specs=[
            pl.BlockSpec((streams_count, rows, BLOCK), lambda i: (0, 0, i)),
            pl.BlockSpec((streams_count, taps - 1, BLOCK), lambda i: (0, 0, i)),
            pl.BlockSpec((taps, streams_count, BLOCK), lambda i: (0, 0, i)),
            pl.BlockSpec((modes, BLOCK), lambda i: (0, i)),
        ],
        out_specs=[
            pl.BlockSpec((modes, SUB, BLOCK), lambda i: (0, 0, i)),
            pl.BlockSpec((modes, BLOCK), lambda i: (0, i)),
        ],
        out_shape=[
            jax.ShapeDtypeStruct((modes, SUB, width), jnp.float32),
            jax.ShapeDtypeStruct((modes, width), jnp.float32),
        ],
        scratch_shapes=[
            pltpu.VMEM((streams_count, BLOCK // LANES, rows, LANES), jnp.float32),
            pltpu.VMEM((modes, SUB, LANES), jnp.float32),
            pltpu.VMEM((taps * streams_count, SUB, LANES), jnp.float32),
        ],
    )(x, halo, f, rate_t)


def run_out(x, halo, f, rate_t, residue_t, skip, ends, fix, hin):
    streams_count, rows, width = x.shape
    taps = f.shape[0]
    modes = rate_t.shape[0]
    return pl.pallas_call(
        out_kernel,
        grid=(width // BLOCK,),
        in_specs=[
            pl.BlockSpec((streams_count, rows, BLOCK), lambda i: (0, 0, i)),
            pl.BlockSpec((streams_count, taps - 1, BLOCK), lambda i: (0, 0, i)),
            pl.BlockSpec((taps, streams_count, BLOCK), lambda i: (0, 0, i)),
            pl.BlockSpec((modes, BLOCK), lambda i: (0, i)),
            pl.BlockSpec((modes, BLOCK), lambda i: (0, i)),
            pl.BlockSpec((1, BLOCK), lambda i: (0, i)),
            pl.BlockSpec((modes, SUB, BLOCK), lambda i: (0, 0, i)),
            pl.BlockSpec((modes, BLOCK), lambda i: (0, i)),
            pl.BlockSpec((modes, BLOCK), lambda i: (0, i)),
        ],
        out_specs=pl.BlockSpec((rows, BLOCK), lambda i: (0, i)),
        out_shape=jax.ShapeDtypeStruct((rows, width), jnp.bfloat16),
        scratch_shapes=[
            pltpu.VMEM((streams_count, BLOCK // LANES, rows, LANES), jnp.float32),
            pltpu.VMEM((BLOCK // LANES, rows, LANES), jnp.float32),
            pltpu.VMEM((modes, SUB, LANES), jnp.float32),
            pltpu.VMEM((modes, SUB, LANES), jnp.float32),
            pltpu.VMEM((taps * streams_count, SUB, LANES), jnp.float32),
        ],
    )(x, halo, f, rate_t, residue_t, skip, ends, fix, hin)


def body(streams, short_filter, skip, rates, residues):
    axes = ("ctx", "tp")
    devices = lax.axis_size("ctx") * lax.axis_size("tp")
    tok_rows, streams_count, width = streams.shape
    taps = short_filter.shape[0]
    modes = rates.shape[1]

    def shift(value, offset):
        pairs = [(j, j + offset) for j in range(devices - offset)]
        return lax.ppermute(value, axes, pairs)

    halo_rows = shift(streams[tok_rows - (taps - 1) :], 1).astype(jnp.float32)
    halo = jnp.transpose(halo_rows, (1, 0, 2))
    x = jnp.transpose(streams, (1, 0, 2))
    rate_t = rates.T
    residue_t = residues.T
    ends, local = run_state(x, jnp.zeros_like(halo), short_filter, rate_t)

    head = streams[: taps - 1].astype(jnp.float32)

    def head_gate(before):
        rows = jnp.concatenate([before, head], axis=0)
        gated = []
        for t in range(taps - 1):
            feat = short_filter[0] * rows[t + taps - 1]
            for tap in range(1, taps):
                feat = feat + short_filter[tap] * rows[t + taps - 1 - tap]
            gated.append((feat[1] * feat[2]).astype(jnp.bfloat16).astype(jnp.float32))
        return gated

    seg = tok_rows // SUB
    true_head = head_gate(halo_rows)
    zero_head = head_gate(jnp.zeros_like(halo_rows))
    local_fix = None
    ends_fix = None
    for t in range(taps - 1):
        delta = (true_head[t] - zero_head[t])[None, :]
        to_end = jnp.exp(-rate_t * float(tok_rows - 1 - t)) * delta
        to_seg = jnp.exp(-rate_t * float(seg - 1 - t)) * delta
        local_fix = to_end if local_fix is None else local_fix + to_end
        ends_fix = to_seg if ends_fix is None else ends_fix + to_seg
    local = local + local_fix

    group = lax.axis_size("tp")
    spans = lax.axis_size("ctx")
    member = lax.axis_index("tp")
    piece = width // group

    def exchange(value, k):
        return lax.ppermute(value, "tp", [(q, (q + k) % group) for q in range(group)])

    def powers(rates_part, count):
        return jnp.exp(-rates_part * (float(tok_rows) * count))

    inside = None
    total = powers(rate_t, (group - 1 - member).astype(jnp.float32)) * local
    for k in range(1, group):
        other = exchange(local, k)
        source = (member - k) % group
        total = total + powers(rate_t, (group - 1 - source).astype(jnp.float32)) * other
        term = jnp.where(k <= member, powers(rate_t, float(k - 1)) * other, 0.0)
        inside = term if inside is None else inside + term
    if inside is None:
        inside = jnp.zeros_like(local)

    first_channel = member * piece
    rate_part = lax.dynamic_slice_in_dim(rate_t, first_channel, piece, 1)
    total_part = lax.dynamic_slice_in_dim(total, first_channel, piece, 1)

    def span_shift(value, offset):
        return lax.ppermute(value, "ctx", [(j, j + offset) for j in range(spans - offset)])

    def gather_window(value, spacing, count):
        gathered = None
        for k in range(1, count + 1):
            if k * spacing >= spans:
                break
            term = powers(rate_part, float(group * (k - 1) * spacing)) * span_shift(value, k * spacing)
            gathered = term if gathered is None else gathered + term
        return gathered

    if spans > 1:
        first = min(FIRST_WINDOW, spans - 1)
        before = gather_window(total_part, 1, first)
        window = first
        while window < spans - 1:
            count = min(-(-(spans - 1) // window) - 1, LATER_WINDOW)
            before = before + powers(rate_part, float(group * window)) * gather_window(before, window, count)
            window *= count + 1
    else:
        before = jnp.zeros_like(total_part)

    whole = jnp.zeros_like(local)
    for k in range(group):
        part = before if k == 0 else exchange(before, k)
        whole = lax.dynamic_update_slice_in_dim(whole, part, ((member - k) % group) * piece, 1)
    carried = powers(rate_t, member.astype(jnp.float32)) * whole + inside

    return run_out(x, halo, short_filter, rate_t, residue_t, skip.reshape(1, width), ends, ends_fix, carried)


def solution(mesh):
    return jax.shard_map(
        body,
        mesh=mesh,
        in_specs=(P(("ctx", "tp"), None, None), P(), P(), P(), P()),
        out_specs=P(("ctx", "tp"), None),
        check_vma=False,
    )
```

```python
import jax
import jax.numpy as jnp
from jax import lax
from jax.experimental import pallas as pl
from jax.experimental.pallas import tpu as pltpu
from jax.sharding import PartitionSpec as P

LANES = 128
SUB = 8
BLOCK = 1024
FIRST_WINDOW = 5
LATER_WINDOW = 2
UNROLL = 16


def lane_slice(c):
    return pl.ds(pl.multiple_of(c * LANES, LANES), LANES)


def row(ref, index, lanes):
    return jnp.broadcast_to(ref[pl.ds(index, 1), lanes], (SUB, LANES))


def first_prev(xs, halo_ref, c, lanes, seg, taps, sub):
    prev = []
    for back in range(1, taps):
        per_stream = []
        for s in range(xs.shape[0]):
            rows = xs[s, c, pl.ds(seg - back, SUB, stride=seg), :]
            edge = jnp.broadcast_to(halo_ref[s, pl.ds(taps - 1 - back, 1), lanes], (SUB, LANES))
            per_stream.append(jnp.where(sub == 0, edge, pltpu.roll(rows, 1, 0)))
        prev.append(per_stream)
    return prev


def fill_filters(f_ref, fsc, lanes):
    streams_count = f_ref.shape[1]
    for tap in range(f_ref.shape[0]):
        for s in range(streams_count):
            fsc[tap * streams_count + s] = row(f_ref.at[tap], s, lanes)


def step_features(xs, fsc, c, seg, j, prev):
    streams_count = xs.shape[0]
    taps = len(prev) + 1
    now = [xs[s, c, pl.ds(j, SUB, stride=seg), :] for s in range(streams_count)]
    feats = []
    for s in range(streams_count):
        acc = fsc[s] * now[s]
        for tap in range(1, taps):
            acc = acc + fsc[tap * streams_count + s] * prev[tap - 1][s]
        feats.append(acc)
    new_prev = [now] + prev[:-1]
    return feats, new_prev


def gate(feats):
    return (feats[1] * feats[2]).astype(jnp.bfloat16).astype(jnp.float32)


def state_kernel(x_ref, halo_ref, f_ref, a_ref, seg_ref, h_ref, xs, dsc, fsc):
    streams_count, rows, block = x_ref.shape
    taps = f_ref.shape[0]
    modes = a_ref.shape[0]
    seg = rows // SUB
    for c in range(block // LANES):
        xs[:, c] = x_ref[:, :, c * LANES : (c + 1) * LANES].astype(jnp.float32)
    sub = lax.broadcasted_iota(jnp.int32, (SUB, LANES), 0)

    def lane_group(c, carry):
        lanes = lane_slice(c)
        fill_filters(f_ref, fsc, lanes)
        for m in range(modes):
            dsc[m] = jnp.exp(-row(a_ref, m, lanes))

        def step(j, state):
            prev, states = state
            feats, prev = step_features(xs, fsc, c, seg, j, prev)
            u = gate(feats)
            return prev, tuple(dsc[m] * states[m] + u for m in range(modes))

        zero = jnp.zeros((SUB, LANES), jnp.float32)
        init = (first_prev(xs, halo_ref, c, lanes, seg, taps, sub), (zero,) * modes)
        _, states = lax.fori_loop(0, seg, step, init, unroll=UNROLL)
        later = (SUB - 1 - sub).astype(jnp.float32) * float(seg)
        for m in range(modes):
            seg_ref[m, :, lanes] = states[m]
            weight = jnp.exp(-row(a_ref, m, lanes) * later)
            h_ref[pl.ds(m, 1), lanes] = jnp.sum(weight * states[m], axis=0, keepdims=True)
        return carry

    lax.fori_loop(0, block // LANES, lane_group, 0, unroll=2)


def out_kernel(
    x_ref, halo_ref, f_ref, a_ref, r_ref, skip_ref, seg_ref, fix_ref, hin_ref, o_ref, xs, ys, dsc, rsc, fsc
):
    streams_count, rows, block = x_ref.shape
    taps = f_ref.shape[0]
    modes = a_ref.shape[0]
    seg = rows // SUB
    for c in range(block // LANES):
        xs[:, c] = x_ref[:, :, c * LANES : (c + 1) * LANES].astype(jnp.float32)
    sub = lax.broadcasted_iota(jnp.int32, (SUB, LANES), 0)

    def lane_group(c, carry):
        lanes = lane_slice(c)
        fill_filters(f_ref, fsc, lanes)
        starts = []
        for m in range(modes):
            rate = row(a_ref, m, lanes)
            dsc[m] = jnp.exp(-rate)
            rsc[m] = row(r_ref, m, lanes)
            ends = seg_ref[m, :, lanes] + jnp.where(sub == 0, row(fix_ref, m, lanes), 0.0)
            carried = jnp.where(sub >= 1, pltpu.roll(ends, 1, 0), 0.0)
            offset = 1
            while offset < SUB:
                factor = jnp.exp(-rate * float(seg * offset))
                carried = carried + jnp.where(sub >= offset, factor * pltpu.roll(carried, offset, 0), 0.0)
                offset *= 2
            lead = jnp.exp(-rate * (sub.astype(jnp.float32) * float(seg)))
            starts.append(carried + lead * row(hin_ref, m, lanes))
        skip_rows = row(skip_ref, 0, lanes)

        def step(j, state):
            prev, states = state
            feats, prev = step_features(xs, fsc, c, seg, j, prev)
            u = gate(feats)
            new = [dsc[m] * states[m] + u for m in range(modes)]
            terms = [rsc[m] * new[m] for m in range(modes)]
            while len(terms) > 1:
                paired = [terms[i] + terms[i + 1] for i in range(0, len(terms) - 1, 2)]
                terms = paired + terms[len(terms) - len(terms) % 2 :]
            conv = terms[0]
            y = (conv + skip_rows * u).astype(jnp.bfloat16).astype(jnp.float32)
            ys[c, pl.ds(j, SUB, stride=seg), :] = feats[0] * y
            return prev, tuple(new)

        init = (first_prev(xs, halo_ref, c, lanes, seg, taps, sub), tuple(starts))
        lax.fori_loop(0, seg, step, init, unroll=UNROLL)
        return carry

    lax.fori_loop(0, block // LANES, lane_group, 0, unroll=2)
    for c in range(block // LANES):
        o_ref[:, c * LANES : (c + 1) * LANES] = ys[c].astype(o_ref.dtype)


def run_state(x, halo, f, rate_t):
    streams_count, rows, width = x.shape
    taps = f.shape[0]
    modes = rate_t.shape[0]
    return pl.pallas_call(
        state_kernel,
        grid=(width // BLOCK,),
        in_specs=[
            pl.BlockSpec((streams_count, rows, BLOCK), lambda i: (0, 0, i)),
            pl.BlockSpec((streams_count, taps - 1, BLOCK), lambda i: (0, 0, i)),
            pl.BlockSpec((taps, streams_count, BLOCK), lambda i: (0, 0, i)),
            pl.BlockSpec((modes, BLOCK), lambda i: (0, i)),
        ],
        out_specs=[
            pl.BlockSpec((modes, SUB, BLOCK), lambda i: (0, 0, i)),
            pl.BlockSpec((modes, BLOCK), lambda i: (0, i)),
        ],
        out_shape=[
            jax.ShapeDtypeStruct((modes, SUB, width), jnp.float32),
            jax.ShapeDtypeStruct((modes, width), jnp.float32),
        ],
        scratch_shapes=[
            pltpu.VMEM((streams_count, BLOCK // LANES, rows, LANES), jnp.float32),
            pltpu.VMEM((modes, SUB, LANES), jnp.float32),
            pltpu.VMEM((taps * streams_count, SUB, LANES), jnp.float32),
        ],
    )(x, halo, f, rate_t)


def run_out(x, halo, f, rate_t, residue_t, skip, ends, fix, hin):
    streams_count, rows, width = x.shape
    taps = f.shape[0]
    modes = rate_t.shape[0]
    return pl.pallas_call(
        out_kernel,
        grid=(width // BLOCK,),
        in_specs=[
            pl.BlockSpec((streams_count, rows, BLOCK), lambda i: (0, 0, i)),
            pl.BlockSpec((streams_count, taps - 1, BLOCK), lambda i: (0, 0, i)),
            pl.BlockSpec((taps, streams_count, BLOCK), lambda i: (0, 0, i)),
            pl.BlockSpec((modes, BLOCK), lambda i: (0, i)),
            pl.BlockSpec((modes, BLOCK), lambda i: (0, i)),
            pl.BlockSpec((1, BLOCK), lambda i: (0, i)),
            pl.BlockSpec((modes, SUB, BLOCK), lambda i: (0, 0, i)),
            pl.BlockSpec((modes, BLOCK), lambda i: (0, i)),
            pl.BlockSpec((modes, BLOCK), lambda i: (0, i)),
        ],
        out_specs=pl.BlockSpec((rows, BLOCK), lambda i: (0, i)),
        out_shape=jax.ShapeDtypeStruct((rows, width), jnp.bfloat16),
        scratch_shapes=[
            pltpu.VMEM((streams_count, BLOCK // LANES, rows, LANES), jnp.float32),
            pltpu.VMEM((BLOCK // LANES, rows, LANES), jnp.float32),
            pltpu.VMEM((modes, SUB, LANES), jnp.float32),
            pltpu.VMEM((modes, SUB, LANES), jnp.float32),
            pltpu.VMEM((taps * streams_count, SUB, LANES), jnp.float32),
        ],
    )(x, halo, f, rate_t, residue_t, skip, ends, fix, hin)


def body(streams, short_filter, skip, rates, residues):
    axes = ("ctx", "tp")
    devices = lax.axis_size("ctx") * lax.axis_size("tp")
    tok_rows, streams_count, width = streams.shape
    taps = short_filter.shape[0]
    modes = rates.shape[1]

    def shift(value, offset):
        pairs = [(j, j + offset) for j in range(devices - offset)]
        return lax.ppermute(value, axes, pairs)

    halo_rows = shift(streams[tok_rows - (taps - 1) :], 1).astype(jnp.float32)
    halo = jnp.transpose(halo_rows, (1, 0, 2))
    x = jnp.transpose(streams, (1, 0, 2))
    rate_t = rates.T
    residue_t = residues.T
    ends, local = run_state(x, jnp.zeros_like(halo), short_filter, rate_t)

    head = streams[: taps - 1].astype(jnp.float32)

    def head_gate(before):
        rows = jnp.concatenate([before, head], axis=0)
        gated = []
        for t in range(taps - 1):
            feat = short_filter[0] * rows[t + taps - 1]
            for tap in range(1, taps):
                feat = feat + short_filter[tap] * rows[t + taps - 1 - tap]
            gated.append((feat[1] * feat[2]).astype(jnp.bfloat16).astype(jnp.float32))
        return gated

    seg = tok_rows // SUB
    true_head = head_gate(halo_rows)
    zero_head = head_gate(jnp.zeros_like(halo_rows))
    local_fix = None
    ends_fix = None
    for t in range(taps - 1):
        delta = (true_head[t] - zero_head[t])[None, :]
        to_end = jnp.exp(-rate_t * float(tok_rows - 1 - t)) * delta
        to_seg = jnp.exp(-rate_t * float(seg - 1 - t)) * delta
        local_fix = to_end if local_fix is None else local_fix + to_end
        ends_fix = to_seg if ends_fix is None else ends_fix + to_seg
    local = local + local_fix

    group = lax.axis_size("tp")
    spans = lax.axis_size("ctx")
    member = lax.axis_index("tp")
    piece = width // group

    def exchange(value, k):
        return lax.ppermute(value, "tp", [(q, (q + k) % group) for q in range(group)])

    def powers(rates_part, count):
        return jnp.exp(-rates_part * (float(tok_rows) * count))

    inside = None
    total = powers(rate_t, (group - 1 - member).astype(jnp.float32)) * local
    for k in range(1, group):
        other = exchange(local, k)
        source = (member - k) % group
        total = total + powers(rate_t, (group - 1 - source).astype(jnp.float32)) * other
        term = jnp.where(k <= member, powers(rate_t, float(k - 1)) * other, 0.0)
        inside = term if inside is None else inside + term
    if inside is None:
        inside = jnp.zeros_like(local)

    first_channel = member * piece
    rate_part = lax.dynamic_slice_in_dim(rate_t, first_channel, piece, 1)
    total_part = lax.dynamic_slice_in_dim(total, first_channel, piece, 1)

    def span_shift(value, offset):
        return lax.ppermute(value, "ctx", [(j, j + offset) for j in range(spans - offset)])

    def gather_window(value, spacing, count):
        gathered = None
        for k in range(1, count + 1):
            if k * spacing >= spans:
                break
            term = powers(rate_part, float(group * (k - 1) * spacing)) * span_shift(value, k * spacing)
            gathered = term if gathered is None else gathered + term
        return gathered

    if spans > 1:
        first = min(FIRST_WINDOW, spans - 1)
        before = gather_window(total_part, 1, first)
        window = first
        while window < spans - 1:
            count = min(-(-(spans - 1) // window) - 1, LATER_WINDOW)
            before = before + powers(rate_part, float(group * window)) * gather_window(before, window, count)
            window *= count + 1
    else:
        before = jnp.zeros_like(total_part)

    whole = jnp.zeros_like(local)
    for k in range(group):
        part = before if k == 0 else exchange(before, k)
        whole = lax.dynamic_update_slice_in_dim(whole, part, ((member - k) % group) * piece, 1)
    carried = powers(rate_t, member.astype(jnp.float32)) * whole + inside

    return run_out(x, halo, short_filter, rate_t, residue_t, skip.reshape(1, width), ends, ends_fix, carried)


def solution(mesh):
    return jax.shard_map(
        body,
        mesh=mesh,
        in_specs=(P(("ctx", "tp"), None, None), P(), P(), P(), P()),
        out_specs=P(("ctx", "tp"), None),
        check_vma=False,
    )
```

```python
import jax
import jax.numpy as jnp
from jax import lax
from jax.experimental import pallas as pl
from jax.experimental.pallas import tpu as pltpu
from jax.sharding import PartitionSpec as P

LANES = 128
SUB = 8
BLOCK = 1024
FIRST_WINDOW = 3
LATER_WINDOW = 4
UNROLL = 16


def lane_slice(c):
    return pl.ds(pl.multiple_of(c * LANES, LANES), LANES)


def row(ref, index, lanes):
    return jnp.broadcast_to(ref[pl.ds(index, 1), lanes], (SUB, LANES))


def first_prev(xs, halo_ref, c, lanes, seg, taps, sub):
    prev = []
    for back in range(1, taps):
        per_stream = []
        for s in range(xs.shape[0]):
            rows = xs[s, c, pl.ds(seg - back, SUB, stride=seg), :]
            edge = jnp.broadcast_to(halo_ref[s, pl.ds(taps - 1 - back, 1), lanes], (SUB, LANES))
            per_stream.append(jnp.where(sub == 0, edge, pltpu.roll(rows, 1, 0)))
        prev.append(per_stream)
    return prev


def fill_filters(f_ref, fsc, lanes):
    streams_count = f_ref.shape[1]
    for tap in range(f_ref.shape[0]):
        for s in range(streams_count):
            fsc[tap * streams_count + s] = row(f_ref.at[tap], s, lanes)


def step_features(xs, fsc, c, seg, j, prev):
    streams_count = xs.shape[0]
    taps = len(prev) + 1
    now = [xs[s, c, pl.ds(j, SUB, stride=seg), :] for s in range(streams_count)]
    feats = []
    for s in range(streams_count):
        acc = fsc[s] * now[s]
        for tap in range(1, taps):
            acc = acc + fsc[tap * streams_count + s] * prev[tap - 1][s]
        feats.append(acc)
    new_prev = [now] + prev[:-1]
    return feats, new_prev


def gate(feats):
    return (feats[1] * feats[2]).astype(jnp.bfloat16).astype(jnp.float32)


def state_kernel(x_ref, halo_ref, f_ref, a_ref, seg_ref, h_ref, xs, dsc, fsc):
    streams_count, rows, block = x_ref.shape
    taps = f_ref.shape[0]
    modes = a_ref.shape[0]
    seg = rows // SUB
    for c in range(block // LANES):
        xs[:, c] = x_ref[:, :, c * LANES : (c + 1) * LANES].astype(jnp.float32)
    sub = lax.broadcasted_iota(jnp.int32, (SUB, LANES), 0)

    def lane_group(c, carry):
        lanes = lane_slice(c)
        fill_filters(f_ref, fsc, lanes)
        for m in range(modes):
            dsc[m] = jnp.exp(-row(a_ref, m, lanes))

        def step(j, state):
            prev, states = state
            feats, prev = step_features(xs, fsc, c, seg, j, prev)
            u = gate(feats)
            return prev, tuple(dsc[m] * states[m] + u for m in range(modes))

        zero = jnp.zeros((SUB, LANES), jnp.float32)
        init = (first_prev(xs, halo_ref, c, lanes, seg, taps, sub), (zero,) * modes)
        _, states = lax.fori_loop(0, seg, step, init, unroll=UNROLL)
        later = (SUB - 1 - sub).astype(jnp.float32) * float(seg)
        for m in range(modes):
            seg_ref[m, :, lanes] = states[m]
            weight = jnp.exp(-row(a_ref, m, lanes) * later)
            h_ref[pl.ds(m, 1), lanes] = jnp.sum(weight * states[m], axis=0, keepdims=True)
        return carry

    lax.fori_loop(0, block // LANES, lane_group, 0, unroll=4)


def out_kernel(
    x_ref, halo_ref, f_ref, a_ref, r_ref, skip_ref, seg_ref, fix_ref, hin_ref, o_ref, xs, ys, dsc, rsc, fsc
):
    streams_count, rows, block = x_ref.shape
    taps = f_ref.shape[0]
    modes = a_ref.shape[0]
    seg = rows // SUB
    for c in range(block // LANES):
        xs[:, c] = x_ref[:, :, c * LANES : (c + 1) * LANES].astype(jnp.float32)
    sub = lax.broadcasted_iota(jnp.int32, (SUB, LANES), 0)

    def lane_group(c, carry):
        lanes = lane_slice(c)
        fill_filters(f_ref, fsc, lanes)
        starts = []
        for m in range(modes):
            rate = row(a_ref, m, lanes)
            dsc[m] = jnp.exp(-rate)
            rsc[m] = row(r_ref, m, lanes)
            ends = seg_ref[m, :, lanes] + jnp.where(sub == 0, row(fix_ref, m, lanes), 0.0)
            carried = jnp.where(sub >= 1, pltpu.roll(ends, 1, 0), 0.0)
            offset = 1
            while offset < SUB:
                factor = jnp.exp(-rate * float(seg * offset))
                carried = carried + jnp.where(sub >= offset, factor * pltpu.roll(carried, offset, 0), 0.0)
                offset *= 2
            lead = jnp.exp(-rate * (sub.astype(jnp.float32) * float(seg)))
            starts.append(carried + lead * row(hin_ref, m, lanes))
        skip_rows = row(skip_ref, 0, lanes)

        def step(j, state):
            prev, states = state
            feats, prev = step_features(xs, fsc, c, seg, j, prev)
            u = gate(feats)
            new = [dsc[m] * states[m] + u for m in range(modes)]
            terms = [rsc[m] * new[m] for m in range(modes)]
            while len(terms) > 1:
                paired = [terms[i] + terms[i + 1] for i in range(0, len(terms) - 1, 2)]
                terms = paired + terms[len(terms) - len(terms) % 2 :]
            conv = terms[0]
            y = (conv + skip_rows * u).astype(jnp.bfloat16).astype(jnp.float32)
            ys[c, pl.ds(j, SUB, stride=seg), :] = feats[0] * y
            return prev, tuple(new)

        init = (first_prev(xs, halo_ref, c, lanes, seg, taps, sub), tuple(starts))
        lax.fori_loop(0, seg, step, init, unroll=UNROLL)
        return carry

    lax.fori_loop(0, block // LANES, lane_group, 0, unroll=4)
    for c in range(block // LANES):
        o_ref[:, c * LANES : (c + 1) * LANES] = ys[c].astype(o_ref.dtype)


def run_state(x, halo, f, rate_t):
    streams_count, rows, width = x.shape
    taps = f.shape[0]
    modes = rate_t.shape[0]
    return pl.pallas_call(
        state_kernel,
        grid=(width // BLOCK,),
        in_specs=[
            pl.BlockSpec((streams_count, rows, BLOCK), lambda i: (0, 0, i)),
            pl.BlockSpec((streams_count, taps - 1, BLOCK), lambda i: (0, 0, i)),
            pl.BlockSpec((taps, streams_count, BLOCK), lambda i: (0, 0, i)),
            pl.BlockSpec((modes, BLOCK), lambda i: (0, i)),
        ],
        out_specs=[
            pl.BlockSpec((modes, SUB, BLOCK), lambda i: (0, 0, i)),
            pl.BlockSpec((modes, BLOCK), lambda i: (0, i)),
        ],
        out_shape=[
            jax.ShapeDtypeStruct((modes, SUB, width), jnp.float32),
            jax.ShapeDtypeStruct((modes, width), jnp.float32),
        ],
        scratch_shapes=[
            pltpu.VMEM((streams_count, BLOCK // LANES, rows, LANES), jnp.float32),
            pltpu.VMEM((modes, SUB, LANES), jnp.float32),
            pltpu.VMEM((taps * streams_count, SUB, LANES), jnp.float32),
        ],
    )(x, halo, f, rate_t)


def run_out(x, halo, f, rate_t, residue_t, skip, ends, fix, hin):
    streams_count, rows, width = x.shape
    taps = f.shape[0]
    modes = rate_t.shape[0]
    return pl.pallas_call(
        out_kernel,
        grid=(width // BLOCK,),
        in_specs=[
            pl.BlockSpec((streams_count, rows, BLOCK), lambda i: (0, 0, i)),
            pl.BlockSpec((streams_count, taps - 1, BLOCK), lambda i: (0, 0, i)),
            pl.BlockSpec((taps, streams_count, BLOCK), lambda i: (0, 0, i)),
            pl.BlockSpec((modes, BLOCK), lambda i: (0, i)),
            pl.BlockSpec((modes, BLOCK), lambda i: (0, i)),
            pl.BlockSpec((1, BLOCK), lambda i: (0, i)),
            pl.BlockSpec((modes, SUB, BLOCK), lambda i: (0, 0, i)),
            pl.BlockSpec((modes, BLOCK), lambda i: (0, i)),
            pl.BlockSpec((modes, BLOCK), lambda i: (0, i)),
        ],
        out_specs=pl.BlockSpec((rows, BLOCK), lambda i: (0, i)),
        out_shape=jax.ShapeDtypeStruct((rows, width), jnp.bfloat16),
        scratch_shapes=[
            pltpu.VMEM((streams_count, BLOCK // LANES, rows, LANES), jnp.float32),
            pltpu.VMEM((BLOCK // LANES, rows, LANES), jnp.float32),
            pltpu.VMEM((modes, SUB, LANES), jnp.float32),
            pltpu.VMEM((modes, SUB, LANES), jnp.float32),
            pltpu.VMEM((taps * streams_count, SUB, LANES), jnp.float32),
        ],
    )(x, halo, f, rate_t, residue_t, skip, ends, fix, hin)


def body(streams, short_filter, skip, rates, residues):
    axes = ("ctx", "tp")
    devices = lax.axis_size("ctx") * lax.axis_size("tp")
    tok_rows, streams_count, width = streams.shape
    taps = short_filter.shape[0]
    modes = rates.shape[1]

    def shift(value, offset):
        pairs = [(j, j + offset) for j in range(devices - offset)]
        return lax.ppermute(value, axes, pairs)

    halo_rows = shift(streams[tok_rows - (taps - 1) :], 1).astype(jnp.float32)
    halo = jnp.transpose(halo_rows, (1, 0, 2))
    x = jnp.transpose(streams, (1, 0, 2))
    rate_t = rates.T
    residue_t = residues.T
    ends, local = run_state(x, jnp.zeros_like(halo), short_filter, rate_t)

    head = streams[: taps - 1].astype(jnp.float32)

    def head_gate(before):
        rows = jnp.concatenate([before, head], axis=0)
        gated = []
        for t in range(taps - 1):
            feat = short_filter[0] * rows[t + taps - 1]
            for tap in range(1, taps):
                feat = feat + short_filter[tap] * rows[t + taps - 1 - tap]
            gated.append((feat[1] * feat[2]).astype(jnp.bfloat16).astype(jnp.float32))
        return gated

    seg = tok_rows // SUB
    true_head = head_gate(halo_rows)
    zero_head = head_gate(jnp.zeros_like(halo_rows))
    local_fix = None
    ends_fix = None
    for t in range(taps - 1):
        delta = (true_head[t] - zero_head[t])[None, :]
        to_end = jnp.exp(-rate_t * float(tok_rows - 1 - t)) * delta
        to_seg = jnp.exp(-rate_t * float(seg - 1 - t)) * delta
        local_fix = to_end if local_fix is None else local_fix + to_end
        ends_fix = to_seg if ends_fix is None else ends_fix + to_seg
    local = local + local_fix

    group = lax.axis_size("tp")
    spans = lax.axis_size("ctx")
    member = lax.axis_index("tp")
    piece = width // group

    def exchange(value, k):
        return lax.ppermute(value, "tp", [(q, (q + k) % group) for q in range(group)])

    def powers(rates_part, count):
        return jnp.exp(-rates_part * (float(tok_rows) * count))

    inside = None
    total = powers(rate_t, (group - 1 - member).astype(jnp.float32)) * local
    for k in range(1, group):
        other = exchange(local, k)
        source = (member - k) % group
        total = total + powers(rate_t, (group - 1 - source).astype(jnp.float32)) * other
        term = jnp.where(k <= member, powers(rate_t, float(k - 1)) * other, 0.0)
        inside = term if inside is None else inside + term
    if inside is None:
        inside = jnp.zeros_like(local)

    first_channel = member * piece
    rate_part = lax.dynamic_slice_in_dim(rate_t, first_channel, piece, 1)
    total_part = lax.dynamic_slice_in_dim(total, first_channel, piece, 1)

    def span_shift(value, offset):
        return lax.ppermute(value, "ctx", [(j, j + offset) for j in range(spans - offset)])

    def gather_window(value, spacing, count):
        gathered = None
        for k in range(1, count + 1):
            if k * spacing >= spans:
                break
            term = powers(rate_part, float(group * (k - 1) * spacing)) * span_shift(value, k * spacing)
            gathered = term if gathered is None else gathered + term
        return gathered

    if spans > 1:
        first = min(FIRST_WINDOW, spans - 1)
        before = gather_window(total_part, 1, first)
        window = first
        while window < spans - 1:
            count = min(-(-(spans - 1) // window) - 1, LATER_WINDOW)
            before = before + powers(rate_part, float(group * window)) * gather_window(before, window, count)
            window *= count + 1
    else:
        before = jnp.zeros_like(total_part)

    whole = jnp.zeros_like(local)
    for k in range(group):
        part = before if k == 0 else exchange(before, k)
        whole = lax.dynamic_update_slice_in_dim(whole, part, ((member - k) % group) * piece, 1)
    carried = powers(rate_t, member.astype(jnp.float32)) * whole + inside

    return run_out(x, halo, short_filter, rate_t, residue_t, skip.reshape(1, width), ends, ends_fix, carried)


def solution(mesh):
    return jax.shard_map(
        body,
        mesh=mesh,
        in_specs=(P(("ctx", "tp"), None, None), P(), P(), P(), P()),
        out_specs=P(("ctx", "tp"), None),
        check_vma=False,
    )
```
